128 devices in a mesh: seq: 64 (over z, x, y_lo, core), chan: 2 (over y_hi).
Axes of the slice: x: 4, y: 4 (y_hi: 2, y_lo: 2; y = y_hi * 2 + y_lo), z: 4, core: 2. Of those that a mesh axis runs over, the one named last changes fastest.
Arguments:
- signal: bfloat16 [2, 32768, 128], P('chan', 'seq'), may hold values from -6 to 6
- cotangent: bfloat16 [2, 32768, 128], P('chan', 'seq'), may hold values from -6 to 6
- band_freq: int32 [16], replicated, may hold values from 1 to 8191
- w_embed: float32 [32, 64], replicated, may hold values from -2 to 2
- b_embed: float32 [64], replicated, may hold values from -3.140625 to 3.140625
- w_out: float32 [64, 128], P(None, 'chan'), may hold values from -0.75 to 0.75
- decay: float32 [128], P('chan'), may hold values from 0.25 to 16, as said below
Outputs:
- conv_out: bfloat16 [2, 32768, 128], P('chan', 'seq')
- d_signal: bfloat16 [2, 32768, 128], P('chan', 'seq')
- grad_embed: float32 [32, 64], replicated
- grad_bias: float32 [64], replicated
- grad_out: float32 [64, 128], P(None, 'chan')
The draws below stay inside these ranges and needn't reach their ends.
Inputs may be any that keep to these rules, and one draw needn't show every extreme that they name: decay rates are positive.
All inputs are finite; a program needn't handle non-finite values.
Results may differ from the reference program's by a relative error of at most 0.007.
Values may be sent and summed in bfloat16 or wider, within the bound.
No kernel may reach another device: no remote copies, remote signals or barrier semaphores. Data moves between devices by JAX's collectives and lax.ppermute only.
A program may use at most 192 MiB of HBM per device.

```python
import math
import jax
import jax.numpy as jnp
from jax import lax

CG = 64
E = 32
F = 64
L = 65536
CHANNELS = 128
N_CHAN = 2


def draw_decay(key, part):
    rate_key = jax.random.fold_in(key, 0)
    low_log = math.log(0.5)
    high_log = math.log(12.0)
    rates = jnp.exp(jax.random.uniform(rate_key, (CHANNELS,), jnp.float32, low_log, high_log))
    rates = jnp.clip(rates, 0.25, 16.0)
    return rates.astype(jnp.float32)


def with_ends(values, own_key, low, largest):
    index_at = [jax.random.randint(jax.random.fold_in(own_key, axis), (), 0, length) for axis, length in enumerate(values.shape)]
    widest = values.shape.index(max(values.shape))
    neighbour = index_at[:widest] + [(index_at[widest] + 1) % values.shape[widest]] + index_at[widest + 1:]
    return values.at[tuple(index_at)].set(low).at[tuple(neighbour)].set(largest)


def shard_levels(own_key, shape, shards, smallest, top_value):
    factor_of, own = 1.0, jax.random.fold_in(own_key, 6)
    for dim, shards_of in shards:
        draws = jnp.exp(jax.random.uniform(jax.random.fold_in(own, dim), (shards_of,), jnp.float32, smallest / len(shards), top_value / len(shards)))
        factor_of = factor_of * jnp.repeat(draws, shape[dim] // shards_of).reshape([-1 if axis == dim else 1 for axis in range(len(shape))])
    return factor_of


def gaussian(own_key, shape, width, bound, cuts=(), kind=jnp.bfloat16):
    entries = width * jax.random.normal(own_key, shape, jnp.float32)
    if cuts:
        entries = entries * shard_levels(own_key, shape, cuts, -0.22, 0.18)
    return jnp.clip(entries, -bound, bound).astype(kind)


def setup_inputs(seed: int = 0) -> dict:
    arg_keys = jax.random.split(jax.random.key(seed), 8)
    signal = gaussian(arg_keys[0], (N_CHAN, L // 2, 2 * CG), 1.0, 6.0, ((0, 2), (1, 64)))
    cotangent = gaussian(arg_keys[1], (N_CHAN, L // 2, 2 * CG), 1.0, 6.0, ((0, 2), (1, 64)))
    band_freq = with_ends(jax.random.randint(arg_keys[2], (E // 2,), 1, L // 8), jax.random.fold_in(arg_keys[2], 1), 1, (L // 8) - 1).astype(jnp.int32)
    w_embed = gaussian(arg_keys[3], (E, F), (E // 4) ** -0.5, 2.0, (), jnp.float32)
    b_embed = jnp.clip(jax.random.uniform(arg_keys[4], (F,), jnp.float32, -3.140625, 3.140625), -3.140625, 3.140625)
    w_out = gaussian(arg_keys[5], (F, CHANNELS), F ** -0.5, 0.75, ((1, 2),), jnp.float32)
    decay = draw_decay(jax.random.fold_in(arg_keys[7], 71), 0)
    return {"signal": signal, "cotangent": cotangent, "band_freq": band_freq, "w_embed": w_embed, "b_embed": b_embed, "w_out": w_out, "decay": decay}


exact_mode = lax.Precision.HIGHEST

def mat_dot(lhs_mat, rhs_mat):
    return jnp.dot(lhs_mat, rhs_mat, preferred_element_type=jnp.float32, precision=exact_mode)

def band_phase(band_freq, places, seq_total):
    upper_part = places // 1024
    lower_part = places % 1024
    partial_turn = upper_part[:, None] * band_freq[None, :] % seq_total
    wrapped = (partial_turn * 1024 + lower_part[:, None] * band_freq[None, :]) % seq_total
    return wrapped.astype(jnp.float32) * (2.0 * math.pi / seq_total)

def filter_parts(places, band_freq, w_embed, b_embed, w_out, decay, seq_total):
    phases = band_phase(band_freq, places, seq_total)
    features = jnp.concatenate([jnp.cos(phases), jnp.sin(phases)], axis=1)
    preact = mat_dot(features, w_embed) + b_embed[None, :]
    hidden = jnp.sin(preact)
    fraction = places.astype(jnp.float32) / seq_total
    envelope = jnp.exp(-decay[None, :] * fraction[:, None]) * jnp.sqrt((1.0 + decay) / seq_total)[None, :]
    taps = mat_dot(hidden, w_out) * envelope
    return (features, preact, hidden, taps, envelope)

def to_rows(blocks):
    return blocks.reshape(N_CHAN, L, CG).transpose(1, 0, 2).reshape(L, N_CHAN * CG)

def to_blocks(rows_data):
    return rows_data.reshape(L, N_CHAN, CG).transpose(1, 0, 2).reshape(N_CHAN, L // 2, 2 * CG)

def reference(signal, cotangent, band_freq, w_embed, b_embed, w_out, decay):
    fft_size = 2 * L
    places = jnp.arange(L, dtype=jnp.int32)
    features, preact, hidden, taps, envelope = filter_parts(places, band_freq, w_embed, b_embed, w_out, decay, L)
    source = to_rows(signal).astype(jnp.float32)
    upstream = to_rows(cotangent).astype(jnp.float32)
    spec_src = jnp.fft.rfft(source, n=fft_size, axis=0)
    spec_up = jnp.fft.rfft(upstream, n=fft_size, axis=0)
    spec_taps = jnp.fft.rfft(taps, n=fft_size, axis=0)
    conv_rows = jnp.fft.irfft(spec_src * spec_taps, n=fft_size, axis=0)[:L].astype(jnp.bfloat16)
    dsig_rows = jnp.fft.irfft(spec_up * jnp.conj(spec_taps), n=fft_size, axis=0)[:L].astype(jnp.bfloat16)
    d_taps = jnp.fft.irfft(spec_up * jnp.conj(spec_src), n=fft_size, axis=0)[:L]
    d_raw = d_taps * envelope
    d_preact = mat_dot(d_raw, w_out.T) * jnp.cos(preact)
    norm_scale = 1.0 / math.sqrt(L)
    grad_out = mat_dot(hidden.T, d_raw) * norm_scale
    grad_embed = mat_dot(features.T, d_preact) * norm_scale
    grad_bias = lax.optimization_barrier(jnp.sum(d_preact, axis=0)) * norm_scale
    return (to_blocks(conv_rows), to_blocks(dsig_rows), grad_embed, grad_bias, grad_out)
```

```python
import math

import jax
import jax.numpy as jnp
from jax import lax
from jax.sharding import PartitionSpec as P

exact_mode = lax.Precision.HIGHEST


def mat_dot(lhs_mat, rhs_mat):
    return jnp.dot(lhs_mat, rhs_mat, preferred_element_type=jnp.float32, precision=exact_mode)


def band_phase(band_freq, places, seq_total):
    upper_part = places // 1024
    lower_part = places % 1024
    partial_turn = upper_part[:, None] * band_freq[None, :] % seq_total
    wrapped = (partial_turn * 1024 + lower_part[:, None] * band_freq[None, :]) % seq_total
    return wrapped.astype(jnp.float32) * (2.0 * math.pi / seq_total)


def filter_parts(places, band_freq, w_embed, b_embed, w_out, decay, seq_total):
    phases = band_phase(band_freq, places, seq_total)
    features = jnp.concatenate([jnp.cos(phases), jnp.sin(phases)], axis=1)
    preact = mat_dot(features, w_embed) + b_embed[None, :]
    hidden = jnp.sin(preact)
    fraction = places.astype(jnp.float32) / seq_total
    envelope = (
        jnp.exp(-decay[None, :] * fraction[:, None]) * jnp.sqrt((1.0 + decay) / seq_total)[None, :]
    )
    taps = mat_dot(hidden, w_out) * envelope
    return (features, preact, hidden, taps, envelope)


def angle_table(rows_idx, cols_idx, modulus):
    wrapped = rows_idx[:, None] * cols_idx[None, :] % modulus
    angles = wrapped.astype(jnp.float32) * (2.0 * math.pi / modulus)
    return (jnp.cos(angles), jnp.sin(angles))


def local(signal, cotangent, band_freq, w_embed, b_embed, w_out, decay):
    devices = lax.axis_size("seq")
    rank_seq = lax.axis_index("seq")
    seg_len = signal.shape[1] * 2
    channels = signal.shape[2] // 2
    block_w = seg_len // devices
    width = block_w * channels
    rows_all = 2 * devices
    pair = rows_all // devices
    seq_total = seg_len * devices
    fft_size = 2 * seq_total
    inv_scale = 1.0 / fft_size
    n_arr = 3

    dev_ids = jnp.arange(devices, dtype=jnp.int32)
    row_ids = jnp.arange(rows_all, dtype=jnp.int32)
    blk_ids = jnp.arange(block_w, dtype=jnp.int32)
    lane_blk = jnp.arange(width, dtype=jnp.int32) // channels
    b_lane = rank_seq * block_w + lane_blk

    src = jnp.stack(
        [signal.reshape(devices, width), cotangent.reshape(devices, width)], axis=1
    )
    cols = lax.all_to_all(src, "seq", split_axis=0, concat_axis=0, tiled=True)

    places = (
        dev_ids[:, None] * seg_len + rank_seq * block_w + blk_ids[None, :]
    ).reshape(-1)
    features, preact, hidden, taps, envelope = filter_parts(
        places, band_freq, w_embed, b_embed, w_out, decay, seq_total
    )
    stacked = jnp.concatenate(
        [cols.astype(jnp.float32), taps.reshape(devices, 1, width)], axis=1
    ).reshape(devices, n_arr * width)

    col_cos, col_sin = angle_table(row_ids, dev_ids, rows_all)
    y_re = mat_dot(col_cos, stacked).reshape(rows_all, n_arr, width)
    y_im = -mat_dot(col_sin, stacked).reshape(rows_all, n_arr, width)
    tw_cos, tw_sin = angle_table(row_ids, b_lane, fft_size)
    tw_cos = tw_cos[:, None, :]
    tw_sin = tw_sin[:, None, :]
    t_re = y_re * tw_cos + y_im * tw_sin
    t_im = y_im * tw_cos - y_re * tw_sin
    spec = jnp.stack([t_re, t_im], axis=1)
    spec = lax.all_to_all(spec, "seq", split_axis=0, concat_axis=0, tiled=True)

    q_cos, q_sin = angle_table(dev_ids, dev_ids, devices)
    stage_a = mat_dot(jnp.concatenate([q_cos, q_sin], axis=0), spec.reshape(devices, -1))
    stage_a = stage_a.reshape(2, devices, pair, 2, n_arr, width)
    a_re = stage_a[0, :, :, 0] + stage_a[1, :, :, 1]
    a_im = stage_a[0, :, :, 1] - stage_a[1, :, :, 0]
    mid_cos, mid_sin = angle_table(dev_ids, lane_blk, seg_len)
    mid_cos = mid_cos[:, None, None, :]
    mid_sin = mid_sin[:, None, None, :]
    b_re = (a_re * mid_cos + a_im * mid_sin).reshape(devices, pair, n_arr, block_w, channels)
    b_im = (a_im * mid_cos - a_re * mid_sin).reshape(devices, pair, n_arr, block_w, channels)
    m_cos, m_sin = angle_table(blk_ids, blk_ids, block_w)

    def blk_mix(table, vals):
        return jnp.einsum(
            "mb,qkzbc->qkzmc", table, vals, preferred_element_type=jnp.float32,
            precision=exact_mode,
        )

    s_re = blk_mix(m_cos, b_re) + blk_mix(m_sin, b_im)
    s_im = blk_mix(m_cos, b_im) - blk_mix(m_sin, b_re)

    sig_r, cot_r, tap_r = s_re[:, :, 0], s_re[:, :, 1], s_re[:, :, 2]
    sig_i, cot_i, tap_i = s_im[:, :, 0], s_im[:, :, 1], s_im[:, :, 2]
    prod_r = jnp.stack(
        [sig_r * tap_r - sig_i * tap_i, cot_r * tap_r + cot_i * tap_i, cot_r * sig_r + cot_i * sig_i],
        axis=2,
    )
    prod_i = jnp.stack(
        [sig_r * tap_i + sig_i * tap_r, cot_i * tap_r - cot_r * tap_i, cot_i * sig_r - cot_r * sig_i],
        axis=2,
    )

    u_re = blk_mix(m_cos, prod_r) - blk_mix(m_sin, prod_i)
    u_im = blk_mix(m_cos, prod_i) + blk_mix(m_sin, prod_r)
    u_re = u_re.reshape(devices, pair, n_arr, width)
    u_im = u_im.reshape(devices, pair, n_arr, width)
    v_re = u_re * mid_cos - u_im * mid_sin
    v_im = u_im * mid_cos + u_re * mid_sin
    v_all = jnp.stack([v_re, v_im]).reshape(2 * devices, -1)
    inv_mat = jnp.concatenate(
        [
            jnp.concatenate([q_cos, -q_sin], axis=1),
            jnp.concatenate([q_sin, q_cos], axis=1),
        ],
        axis=0,
    )
    w_all = mat_dot(inv_mat, v_all).reshape(2, devices, pair, n_arr, width)
    b_rows = dev_ids[:, None] * block_w + lane_blk[None, :]
    k1_own = rank_seq * pair + jnp.arange(pair, dtype=jnp.int32)
    ex_ang = (b_rows[:, None, :] * k1_own[None, :, None]) % fft_size
    ex_ang = ex_ang.astype(jnp.float32) * (2.0 * math.pi / fft_size)
    ex_cos = jnp.cos(ex_ang)[:, :, None, :]
    ex_sin = jnp.sin(ex_ang)[:, :, None, :]
    x_re = w_all[0] * ex_cos - w_all[1] * ex_sin
    x_im = w_all[0] * ex_sin + w_all[1] * ex_cos
    back = jnp.stack([x_re, x_im], axis=1)
    back = lax.all_to_all(back, "seq", split_axis=0, concat_axis=0, tiled=True)

    back = back.reshape(devices, 2, pair, n_arr * width)
    back = jnp.transpose(back, (1, 0, 2, 3)).reshape(2 * rows_all, n_arr * width)
    out_mat = jnp.concatenate([col_cos.T, -col_sin.T], axis=1)
    res = (mat_dot(out_mat, back) * inv_scale).reshape(devices, n_arr, width)

    rows_out = lax.all_to_all(
        res[:, 0:2].astype(jnp.bfloat16), "seq", split_axis=0, concat_axis=0, tiled=True
    )
    conv_out = rows_out[:, 0].reshape(1, seg_len // 2, 2 * channels)
    d_signal = rows_out[:, 1].reshape(1, seg_len // 2, 2 * channels)

    d_taps = res[:, 2].reshape(devices * block_w, channels)
    d_raw = d_taps * envelope
    d_preact = mat_dot(d_raw, w_out.T) * jnp.cos(preact)
    out_part = mat_dot(hidden.T, d_raw)
    embed_part = mat_dot(features.T, d_preact)
    bias_part = jnp.sum(d_preact, axis=0)
    out_sum = lax.psum(out_part, "seq")
    embed_all, bias_all = lax.psum((embed_part, bias_part), ("seq", "chan"))
    norm_scale = 1.0 / math.sqrt(seq_total)
    return (conv_out, d_signal, embed_all * norm_scale, bias_all * norm_scale, out_sum * norm_scale)


def solution(mesh):
    return jax.shard_map(
        local,
        mesh=mesh,
        in_specs=(
            P("chan", "seq", None),
            P("chan", "seq", None),
            P(),
            P(),
            P(),
            P(None, "chan"),
            P("chan"),
        ),
        out_specs=(P("chan", "seq", None), P("chan", "seq", None), P(), P(), P(None, "chan")),
        check_vma=False,
    )
```

```python
import math

import jax
import jax.numpy as jnp
from jax import lax
from jax.sharding import PartitionSpec as P

exact_mode = lax.Precision.HIGHEST


def mat_dot(lhs_mat, rhs_mat):
    return jnp.dot(lhs_mat, rhs_mat, preferred_element_type=jnp.float32, precision=exact_mode)


def band_phase(band_freq, places, seq_total):
    upper_part = places // 1024
    lower_part = places % 1024
    partial_turn = upper_part[:, None] * band_freq[None, :] % seq_total
    wrapped = (partial_turn * 1024 + lower_part[:, None] * band_freq[None, :]) % seq_total
    return wrapped.astype(jnp.float32) * (2.0 * math.pi / seq_total)


def filter_parts(places, band_freq, w_embed, b_embed, w_out, decay, seq_total):
    phases = band_phase(band_freq, places, seq_total)
    features = jnp.concatenate([jnp.cos(phases), jnp.sin(phases)], axis=1)
    preact = mat_dot(features, w_embed) + b_embed[None, :]
    hidden = jnp.sin(preact)
    fraction = places.astype(jnp.float32) / seq_total
    envelope = (
        jnp.exp(-decay[None, :] * fraction[:, None]) * jnp.sqrt((1.0 + decay) / seq_total)[None, :]
    )
    taps = mat_dot(hidden, w_out) * envelope
    return (features, preact, hidden, taps, envelope)


def angle_table(rows_idx, cols_idx, modulus):
    wrapped = rows_idx[:, None] * cols_idx[None, :] % modulus
    angles = wrapped.astype(jnp.float32) * (2.0 * math.pi / modulus)
    return (jnp.cos(angles), jnp.sin(angles))


def local(signal, cotangent, band_freq, w_embed, b_embed, w_out, decay):
    devices = lax.axis_size("seq")
    rank_seq = lax.axis_index("seq")
    seg_len = signal.shape[1] * 2
    channels = signal.shape[2] // 2
    block_w = seg_len // devices
    width = block_w * channels
    rows_all = 2 * devices
    pair = rows_all // devices
    seq_total = seg_len * devices
    fft_size = 2 * seq_total
    inv_scale = 1.0 / fft_size
    n_arr = 3

    dev_ids = jnp.arange(devices, dtype=jnp.int32)
    row_ids = jnp.arange(rows_all, dtype=jnp.int32)
    blk_ids = jnp.arange(block_w, dtype=jnp.int32)
    lane_blk = jnp.arange(width, dtype=jnp.int32) // channels
    b_lane = rank_seq * block_w + lane_blk

    src = jnp.stack(
        [signal.reshape(devices, width), cotangent.reshape(devices, width)], axis=1
    )
    cols = lax.all_to_all(src, "seq", split_axis=0, concat_axis=0, tiled=True)

    places = (
        dev_ids[:, None] * seg_len + rank_seq * block_w + blk_ids[None, :]
    ).reshape(-1)
    features, preact, hidden, taps, envelope = filter_parts(
        places, band_freq, w_embed, b_embed, w_out, decay, seq_total
    )
    stacked = jnp.concatenate(
        [cols.astype(jnp.float32), taps.reshape(devices, 1, width)], axis=1
    ).reshape(devices, n_arr * width)

    col_cos, col_sin = angle_table(row_ids, dev_ids, rows_all)
    y_re = mat_dot(col_cos, stacked).reshape(rows_all, n_arr, width)
    y_im = -mat_dot(col_sin, stacked).reshape(rows_all, n_arr, width)
    tw_cos, tw_sin = angle_table(row_ids, b_lane, fft_size)
    tw_cos = tw_cos[:, None, :]
    tw_sin = tw_sin[:, None, :]
    t_re = y_re * tw_cos + y_im * tw_sin
    t_im = y_im * tw_cos - y_re * tw_sin
    spec = jnp.stack([t_re, t_im], axis=1)
    spec = lax.all_to_all(spec, "seq", split_axis=0, concat_axis=0, tiled=True)

    q_cos, q_sin = angle_table(dev_ids, dev_ids, devices)
    stage_a = mat_dot(jnp.concatenate([q_cos, q_sin], axis=0), spec.reshape(devices, -1))
    stage_a = stage_a.reshape(2, devices, pair, 2, n_arr, width)
    a_re = stage_a[0, :, :, 0] + stage_a[1, :, :, 1]
    a_im = stage_a[0, :, :, 1] - stage_a[1, :, :, 0]
    mid_cos, mid_sin = angle_table(dev_ids, lane_blk, seg_len)
    mid_cos = mid_cos[:, None, None, :]
    mid_sin = mid_sin[:, None, None, :]
    b_re = (a_re * mid_cos + a_im * mid_sin).reshape(devices, pair, n_arr, block_w, channels)
    b_im = (a_im * mid_cos - a_re * mid_sin).reshape(devices, pair, n_arr, block_w, channels)
    m_cos, m_sin = angle_table(blk_ids, blk_ids, block_w)

    def blk_mix(table, vals):
        return jnp.einsum(
            "mb,qkzbc->qkzmc", table, vals, preferred_element_type=jnp.float32,
            precision=exact_mode,
        )

    s_re = blk_mix(m_cos, b_re) + blk_mix(m_sin, b_im)
    s_im = blk_mix(m_cos, b_im) - blk_mix(m_sin, b_re)

    sig_r, cot_r, tap_r = s_re[:, :, 0], s_re[:, :, 1], s_re[:, :, 2]
    sig_i, cot_i, tap_i = s_im[:, :, 0], s_im[:, :, 1], s_im[:, :, 2]
    prod_r = jnp.stack(
        [sig_r * tap_r - sig_i * tap_i, cot_r * tap_r + cot_i * tap_i, cot_r * sig_r + cot_i * sig_i],
        axis=2,
    )
    prod_i = jnp.stack(
        [sig_r * tap_i + sig_i * tap_r, cot_i * tap_r - cot_r * tap_i, cot_i * sig_r - cot_r * sig_i],
        axis=2,
    )

    u_re = blk_mix(m_cos, prod_r) - blk_mix(m_sin, prod_i)
    u_im = blk_mix(m_cos, prod_i) + blk_mix(m_sin, prod_r)
    u_re = u_re.reshape(devices, pair, n_arr, width)
    u_im = u_im.reshape(devices, pair, n_arr, width)
    v_re = u_re * mid_cos - u_im * mid_sin
    v_im = u_im * mid_cos + u_re * mid_sin
    v_all = jnp.stack([v_re, v_im]).reshape(2 * devices, -1)
    inv_mat = jnp.concatenate(
        [
            jnp.concatenate([q_cos, -q_sin], axis=1),
            jnp.concatenate([q_sin, q_cos], axis=1),
        ],
        axis=0,
    )
    w_all = mat_dot(inv_mat, v_all).reshape(2, devices, pair, n_arr, width)
    b_rows = dev_ids[:, None] * block_w + lane_blk[None, :]
    k1_own = rank_seq * pair + jnp.arange(pair, dtype=jnp.int32)
    ex_ang = (b_rows[:, None, :] * k1_own[None, :, None]) % fft_size
    ex_ang = ex_ang.astype(jnp.float32) * (2.0 * math.pi / fft_size)
    ex_cos = jnp.cos(ex_ang)[:, :, None, :]
    ex_sin = jnp.sin(ex_ang)[:, :, None, :]
    x_re = w_all[0] * ex_cos - w_all[1] * ex_sin
    x_im = w_all[0] * ex_sin + w_all[1] * ex_cos
    back = jnp.stack([x_re, x_im], axis=1)
    back = lax.all_to_all(back, "seq", split_axis=0, concat_axis=0, tiled=True)

    back = back.reshape(devices, 2, pair, n_arr * width)
    back = jnp.transpose(back, (1, 0, 2, 3)).reshape(2 * rows_all, n_arr * width)
    out_mat = jnp.concatenate([col_cos.T, -col_sin.T], axis=1)
    res = (mat_dot(out_mat, back) * inv_scale).reshape(devices, n_arr, width)

    rows_out = lax.all_to_all(
        res[:, 0:2].astype(jnp.bfloat16), "seq", split_axis=0, concat_axis=0, tiled=True
    )
    conv_out = rows_out[:, 0].reshape(1, seg_len // 2, 2 * channels)
    d_signal = rows_out[:, 1].reshape(1, seg_len // 2, 2 * channels)

    d_taps = res[:, 2].reshape(devices * block_w, channels)
    d_raw = d_taps * envelope
    d_preact = mat_dot(d_raw, w_out.T) * jnp.cos(preact)
    out_part = mat_dot(hidden.T, d_raw)
    embed_part = mat_dot(features.T, d_preact)
    bias_part = jnp.sum(d_preact, axis=0)
    rank_chan = lax.axis_index("chan")
    n_chan = lax.axis_size("chan")
    out_wide = jnp.zeros((out_part.shape[0], n_chan * channels), jnp.float32)
    out_wide = lax.dynamic_update_slice_in_dim(out_wide, out_part, rank_chan * channels, axis=1)
    wide_sum, embed_all, bias_all = lax.psum((out_wide, embed_part, bias_part), ("seq", "chan"))
    out_sum = lax.dynamic_slice_in_dim(wide_sum, rank_chan * channels, channels, axis=1)
    norm_scale = 1.0 / math.sqrt(seq_total)
    return (conv_out, d_signal, embed_all * norm_scale, bias_all * norm_scale, out_sum * norm_scale)


def solution(mesh):
    return jax.shard_map(
        local,
        mesh=mesh,
        in_specs=(
            P("chan", "seq", None),
            P("chan", "seq", None),
            P(),
            P(),
            P(),
            P(None, "chan"),
            P("chan"),
        ),
        out_specs=(P("chan", "seq", None), P("chan", "seq", None), P(), P(), P(None, "chan")),
        check_vma=False,
    )
```

```python
import math

import jax
import jax.numpy as jnp
from jax import lax
from jax.sharding import PartitionSpec as P

exact_mode = lax.Precision.HIGHEST


def mat_dot(lhs_mat, rhs_mat):
    return jnp.dot(lhs_mat, rhs_mat, preferred_element_type=jnp.float32, precision=exact_mode)


def band_phase(band_freq, places, seq_total):
    upper_part = places // 1024
    lower_part = places % 1024
    partial_turn = upper_part[:, None] * band_freq[None, :] % seq_total
    wrapped = (partial_turn * 1024 + lower_part[:, None] * band_freq[None, :]) % seq_total
    return wrapped.astype(jnp.float32) * (2.0 * math.pi / seq_total)


def filter_parts(places, band_freq, w_embed, b_embed, w_out, decay, seq_total):
    phases = band_phase(band_freq, places, seq_total)
    features = jnp.concatenate([jnp.cos(phases), jnp.sin(phases)], axis=1)
    preact = mat_dot(features, w_embed) + b_embed[None, :]
    hidden = jnp.sin(preact)
    fraction = places.astype(jnp.float32) / seq_total
    envelope = (
        jnp.exp(-decay[None, :] * fraction[:, None]) * jnp.sqrt((1.0 + decay) / seq_total)[None, :]
    )
    taps = mat_dot(hidden, w_out) * envelope
    return (features, preact, hidden, taps, envelope)


def angle_table(rows_idx, cols_idx, modulus):
    wrapped = rows_idx[:, None] * cols_idx[None, :] % modulus
    angles = wrapped.astype(jnp.float32) * (2.0 * math.pi / modulus)
    return (jnp.cos(angles), jnp.sin(angles))


def local(signal, cotangent, band_freq, w_embed, b_embed, w_out, decay):
    devices = lax.axis_size("seq")
    rank_seq = lax.axis_index("seq")
    seg_len = signal.shape[1] * 2
    channels = signal.shape[2] // 2
    block_w = seg_len // devices
    width = block_w * channels
    rows_all = 2 * devices
    pair = rows_all // devices
    seq_total = seg_len * devices
    fft_size = 2 * seq_total
    inv_scale = 1.0 / fft_size
    n_arr = 3

    dev_ids = jnp.arange(devices, dtype=jnp.int32)
    row_ids = jnp.arange(rows_all, dtype=jnp.int32)
    blk_ids = jnp.arange(block_w, dtype=jnp.int32)

    src = jnp.stack(
        [signal.reshape(devices, width), cotangent.reshape(devices, width)], axis=1
    )
    cols = lax.all_to_all(src, "seq", split_axis=0, concat_axis=0, tiled=True)

    places = (
        dev_ids[:, None] * seg_len + rank_seq * block_w + blk_ids[None, :]
    ).reshape(-1)
    features, preact, hidden, taps, envelope = filter_parts(
        places, band_freq, w_embed, b_embed, w_out, decay, seq_total
    )
    stacked = jnp.concatenate(
        [cols.astype(jnp.float32), taps.reshape(devices, 1, width)], axis=1
    ).reshape(devices, n_arr * width)

    col_cos, col_sin = angle_table(row_ids, dev_ids, rows_all)
    y_re = mat_dot(col_cos, stacked).reshape(rows_all, n_arr, block_w, channels)
    y_im = -mat_dot(col_sin, stacked).reshape(rows_all, n_arr, block_w, channels)
    tw_cos, tw_sin = angle_table(row_ids, rank_seq * block_w + blk_ids, fft_size)
    tw_cos = tw_cos[:, None, :, None]
    tw_sin = tw_sin[:, None, :, None]
    t_re = y_re * tw_cos + y_im * tw_sin
    t_im = y_im * tw_cos - y_re * tw_sin
    spec = jnp.transpose(jnp.stack([t_re, t_im]), (3, 1, 0, 2, 4))
    spec = lax.all_to_all(spec, "seq", split_axis=1, concat_axis=0, tiled=True)

    seg_ids = jnp.arange(seg_len, dtype=jnp.int32)
    seg_cos, seg_sin = angle_table(seg_ids, seg_ids, seg_len)
    seg_tab = jnp.concatenate([seg_cos, seg_sin], axis=0)
    fwd = mat_dot(seg_tab, spec.reshape(seg_len, -1)).reshape(2, seg_len, pair, 2, n_arr, channels)
    s_re = fwd[0, :, :, 0] + fwd[1, :, :, 1]
    s_im = fwd[0, :, :, 1] - fwd[1, :, :, 0]

    sig_r, cot_r, tap_r = s_re[:, :, 0], s_re[:, :, 1], s_re[:, :, 2]
    sig_i, cot_i, tap_i = s_im[:, :, 0], s_im[:, :, 1], s_im[:, :, 2]
    prod_r = jnp.stack(
        [sig_r * tap_r - sig_i * tap_i, cot_r * tap_r + cot_i * tap_i, cot_r * sig_r + cot_i * sig_i],
        axis=2,
    )
    prod_i = jnp.stack(
        [sig_r * tap_i + sig_i * tap_r, cot_i * tap_r - cot_r * tap_i, cot_i * sig_r - cot_r * sig_i],
        axis=2,
    )
    prods = jnp.stack([prod_r, prod_i], axis=2).reshape(seg_len, -1)

    inv = mat_dot(seg_tab, prods).reshape(2, seg_len, pair, 2, n_arr, channels)
    r_re = inv[0, :, :, 0] - inv[1, :, :, 1]
    r_im = inv[0, :, :, 1] + inv[1, :, :, 0]
    k1_own = rank_seq * pair + jnp.arange(pair, dtype=jnp.int32)
    ex_cos, ex_sin = angle_table(seg_ids, k1_own, fft_size)
    ex_cos = ex_cos[:, :, None, None]
    ex_sin = ex_sin[:, :, None, None]
    x_re = r_re * ex_cos - r_im * ex_sin
    x_im = r_re * ex_sin + r_im * ex_cos
    back = jnp.transpose(jnp.stack([x_re, x_im]), (0, 2, 1, 3, 4))
    back = lax.all_to_all(back, "seq", split_axis=2, concat_axis=1, tiled=True)

    out_mat = jnp.concatenate([col_cos.T, -col_sin.T], axis=1)
    res = mat_dot(out_mat, back.reshape(2 * rows_all, -1)) * inv_scale
    res = res.reshape(devices, block_w, n_arr, channels)

    rows_out = lax.all_to_all(
        res[:, :, 0:2].astype(jnp.bfloat16), "seq", split_axis=0, concat_axis=0, tiled=True
    )
    conv_out = rows_out[:, :, 0].reshape(1, seg_len // 2, 2 * channels)
    d_signal = rows_out[:, :, 1].reshape(1, seg_len // 2, 2 * channels)

    d_taps = res[:, :, 2].reshape(devices * block_w, channels)
    d_raw = d_taps * envelope
    d_preact = mat_dot(d_raw, w_out.T) * jnp.cos(preact)
    out_part = mat_dot(hidden.T, d_raw)
    embed_part = mat_dot(features.T, d_preact)
    bias_part = jnp.sum(d_preact, axis=0)
    rank_chan = lax.axis_index("chan")
    n_chan = lax.axis_size("chan")
    out_wide = jnp.zeros((out_part.shape[0], n_chan * channels), jnp.float32)
    out_wide = lax.dynamic_update_slice_in_dim(out_wide, out_part, rank_chan * channels, axis=1)
    wide_sum, embed_all, bias_all = lax.psum((out_wide, embed_part, bias_part), ("seq", "chan"))
    out_sum = lax.dynamic_slice_in_dim(wide_sum, rank_chan * channels, channels, axis=1)
    norm_scale = 1.0 / math.sqrt(seq_total)
    return (conv_out, d_signal, embed_all * norm_scale, bias_all * norm_scale, out_sum * norm_scale)


def solution(mesh):
    return jax.shard_map(
        local,
        mesh=mesh,
        in_specs=(
            P("chan", "seq", None),
            P("chan", "seq", None),
            P(),
            P(),
            P(),
            P(None, "chan"),
            P("chan"),
        ),
        out_specs=(P("chan", "seq", None), P("chan", "seq", None), P(), P(), P(None, "chan")),
        check_vma=False,
    )
```

```python
import math

import jax
import jax.numpy as jnp
from jax import lax
from jax.sharding import PartitionSpec as P

exact_mode = lax.Precision.HIGHEST


def mat_dot(lhs_mat, rhs_mat):
    return jnp.dot(lhs_mat, rhs_mat, preferred_element_type=jnp.float32, precision=exact_mode)


def band_phase(band_freq, places, seq_total):
    upper_part = places // 1024
    lower_part = places % 1024
    partial_turn = upper_part[:, None] * band_freq[None, :] % seq_total
    wrapped = (partial_turn * 1024 + lower_part[:, None] * band_freq[None, :]) % seq_total
    return wrapped.astype(jnp.float32) * (2.0 * math.pi / seq_total)


def filter_parts(places, band_freq, w_embed, b_embed, w_out, decay, seq_total):
    phases = band_phase(band_freq, places, seq_total)
    features = jnp.concatenate([jnp.cos(phases), jnp.sin(phases)], axis=1)
    preact = mat_dot(features, w_embed) + b_embed[None, :]
    hidden = jnp.sin(preact)
    fraction = places.astype(jnp.float32) / seq_total
    envelope = (
        jnp.exp(-decay[None, :] * fraction[:, None]) * jnp.sqrt((1.0 + decay) / seq_total)[None, :]
    )
    taps = mat_dot(hidden, w_out) * envelope
    return (features, preact, hidden, taps, envelope)


def angle_table(rows_idx, cols_idx, modulus):
    wrapped = rows_idx[:, None] * cols_idx[None, :] % modulus
    angles = wrapped.astype(jnp.float32) * (2.0 * math.pi / modulus)
    return (jnp.cos(angles), jnp.sin(angles))


def local(signal, cotangent, band_freq, w_embed, b_embed, w_out, decay):
    devices = lax.axis_size("seq")
    rank_seq = lax.axis_index("seq")
    seg_len = signal.shape[1] * 2
    channels = signal.shape[2] // 2
    block_w = seg_len // devices
    width = block_w * channels
    rows_all = 2 * devices
    pair = rows_all // devices
    seq_total = seg_len * devices
    fft_size = 2 * seq_total
    inv_scale = 1.0 / fft_size
    n_arr = 3

    dev_ids = jnp.arange(devices, dtype=jnp.int32)
    row_ids = jnp.arange(rows_all, dtype=jnp.int32)
    blk_ids = jnp.arange(block_w, dtype=jnp.int32)
    lane_blk = jnp.arange(width, dtype=jnp.int32) // channels
    b_lane = rank_seq * block_w + lane_blk

    src = jnp.stack(
        [signal.reshape(devices, width), cotangent.reshape(devices, width)], axis=1
    )
    cols = lax.all_to_all(src, "seq", split_axis=0, concat_axis=0, tiled=True)

    places = (
        dev_ids[:, None] * seg_len + rank_seq * block_w + blk_ids[None, :]
    ).reshape(-1)
    features, preact, hidden, taps, envelope = filter_parts(
        places, band_freq, w_embed, b_embed, w_out, decay, seq_total
    )
    stacked = jnp.concatenate(
        [cols.astype(jnp.float32), taps.reshape(devices, 1, width)], axis=1
    ).reshape(devices, n_arr * width)

    col_cos, col_sin = angle_table(row_ids, dev_ids, rows_all)
    y_re = mat_dot(col_cos, stacked).reshape(rows_all, n_arr, width)
    y_im = -mat_dot(col_sin, stacked).reshape(rows_all, n_arr, width)
    tw_cos, tw_sin = angle_table(row_ids, b_lane, fft_size)
    tw_cos = tw_cos[:, None, :]
    tw_sin = tw_sin[:, None, :]
    t_re = y_re * tw_cos + y_im * tw_sin
    t_im = y_im * tw_cos - y_re * tw_sin
    spec = jnp.stack([t_re, t_im], axis=1)
    spec = lax.all_to_all(spec, "seq", split_axis=0, concat_axis=0, tiled=True)

    q_cos, q_sin = angle_table(dev_ids, dev_ids, devices)
    stage_a = mat_dot(jnp.concatenate([q_cos, q_sin], axis=0), spec.reshape(devices, -1))
    stage_a = stage_a.reshape(2, devices, pair, 2, n_arr, width)
    a_re = stage_a[0, :, :, 0] + stage_a[1, :, :, 1]
    a_im = stage_a[0, :, :, 1] - stage_a[1, :, :, 0]
    mid_cos, mid_sin = angle_table(dev_ids, lane_blk, seg_len)
    mid_cos = mid_cos[:, None, None, :]
    mid_sin = mid_sin[:, None, None, :]
    b_re = (a_re * mid_cos + a_im * mid_sin).reshape(devices, pair, n_arr, block_w, channels)
    b_im = (a_im * mid_cos - a_re * mid_sin).reshape(devices, pair, n_arr, block_w, channels)
    m_cos, m_sin = angle_table(blk_ids, blk_ids, block_w)

    def blk_mix(table, vals):
        return jnp.einsum(
            "mb,qkzbc->qkzmc", table, vals, preferred_element_type=jnp.float32,
            precision=exact_mode,
        )

    s_re = blk_mix(m_cos, b_re) + blk_mix(m_sin, b_im)
    s_im = blk_mix(m_cos, b_im) - blk_mix(m_sin, b_re)

    sig_r, cot_r, tap_r = s_re[:, :, 0], s_re[:, :, 1], s_re[:, :, 2]
    sig_i, cot_i, tap_i = s_im[:, :, 0], s_im[:, :, 1], s_im[:, :, 2]
    prod_r = jnp.stack(
        [sig_r * tap_r - sig_i * tap_i, cot_r * tap_r + cot_i * tap_i, cot_r * sig_r + cot_i * sig_i],
        axis=2,
    )
    prod_i = jnp.stack(
        [sig_r * tap_i + sig_i * tap_r, cot_i * tap_r - cot_r * tap_i, cot_i * sig_r - cot_r * sig_i],
        axis=2,
    )

    u_re = blk_mix(m_cos, prod_r) - blk_mix(m_sin, prod_i)
    u_im = blk_mix(m_cos, prod_i) + blk_mix(m_sin, prod_r)
    u_re = u_re.reshape(devices, pair, n_arr, width)
    u_im = u_im.reshape(devices, pair, n_arr, width)
    v_re = u_re * mid_cos - u_im * mid_sin
    v_im = u_im * mid_cos + u_re * mid_sin
    v_all = jnp.stack([v_re, v_im]).reshape(2 * devices, -1)
    inv_mat = jnp.concatenate(
        [
            jnp.concatenate([q_cos, -q_sin], axis=1),
            jnp.concatenate([q_sin, q_cos], axis=1),
        ],
        axis=0,
    )
    w_all = mat_dot(inv_mat, v_all).reshape(2, devices, pair, n_arr, width)
    b_rows = dev_ids[:, None] * block_w + lane_blk[None, :]
    k1_own = rank_seq * pair + jnp.arange(pair, dtype=jnp.int32)
    ex_ang = (b_rows[:, None, :] * k1_own[None, :, None]) % fft_size
    ex_ang = ex_ang.astype(jnp.float32) * (2.0 * math.pi / fft_size)
    ex_cos = jnp.cos(ex_ang)[:, :, None, :]
    ex_sin = jnp.sin(ex_ang)[:, :, None, :]
    x_re = w_all[0] * ex_cos - w_all[1] * ex_sin
    x_im = w_all[0] * ex_sin + w_all[1] * ex_cos
    back = jnp.stack([x_re, x_im], axis=1)
    back = lax.all_to_all(back, "seq", split_axis=0, concat_axis=0, tiled=True)

    back = back.reshape(devices, 2, pair, n_arr * width)
    back = jnp.transpose(back, (1, 0, 2, 3)).reshape(2 * rows_all, n_arr * width)
    out_mat = jnp.concatenate([col_cos.T, -col_sin.T], axis=1)
    res = (mat_dot(out_mat, back) * inv_scale).reshape(devices, n_arr, width)

    rows_out = lax.all_to_all(
        res[:, 0:2].astype(jnp.bfloat16), "seq", split_axis=0, concat_axis=0, tiled=True
    )
    conv_out = rows_out[:, 0].reshape(1, seg_len // 2, 2 * channels)
    d_signal = rows_out[:, 1].reshape(1, seg_len // 2, 2 * channels)

    d_taps = res[:, 2].reshape(devices * block_w, channels)
    d_raw = d_taps * envelope
    d_preact = mat_dot(d_raw, w_out.T) * jnp.cos(preact)
    out_part = mat_dot(hidden.T, d_raw)
    embed_part = mat_dot(features.T, d_preact)
    bias_part = jnp.sum(d_preact, axis=0)
    rank_chan = lax.axis_index("chan")
    n_chan = lax.axis_size("chan")
    out_wide = jnp.zeros((out_part.shape[0], n_chan * channels), jnp.float32)
    out_wide = lax.dynamic_update_slice_in_dim(out_wide, out_part, rank_chan * channels, axis=1)
    n_all = devices * n_chan
    flat = jnp.concatenate([out_wide.reshape(-1), embed_part.reshape(-1), bias_part])
    piece = -(-flat.shape[0] // (n_all * 128)) * 128
    flat = jnp.pad(flat, (0, n_all * piece - flat.shape[0])).reshape(n_all, piece)
    mine = jnp.sum(lax.all_to_all(flat, ("seq", "chan"), 0, 0, tiled=True), axis=0)
    total = lax.all_to_all(
        jnp.broadcast_to(mine, (n_all, piece)), ("seq", "chan"), 0, 0, tiled=True
    ).reshape(-1)
    n_out = out_wide.size
    n_emb = embed_part.size
    wide_sum = total[:n_out].reshape(out_wide.shape)
    embed_all = total[n_out : n_out + n_emb].reshape(embed_part.shape)
    bias_all = total[n_out + n_emb : n_out + n_emb + bias_part.size]
    out_sum = lax.dynamic_slice_in_dim(wide_sum, rank_chan * channels, channels, axis=1)
    norm_scale = 1.0 / math.sqrt(seq_total)
    return (conv_out, d_signal, embed_all * norm_scale, bias_all * norm_scale, out_sum * norm_scale)


def solution(mesh):
    return jax.shard_map(
        local,
        mesh=mesh,
        in_specs=(
            P("chan", "seq", None),
            P("chan", "seq", None),
            P(),
            P(),
            P(),
            P(None, "chan"),
            P("chan"),
        ),
        out_specs=(P("chan", "seq", None), P("chan", "seq", None), P(), P(), P(None, "chan")),
        check_vma=False,
    )
```

```python
import math

import jax
import jax.numpy as jnp
from jax import lax
from jax.sharding import PartitionSpec as P

exact_mode = lax.Precision.HIGHEST


def mat_dot(lhs_mat, rhs_mat):
    return jnp.dot(lhs_mat, rhs_mat, preferred_element_type=jnp.float32, precision=exact_mode)


def band_phase(band_freq, places, seq_total):
    upper_part = places // 1024
    lower_part = places % 1024
    partial_turn = upper_part[:, None] * band_freq[None, :] % seq_total
    wrapped = (partial_turn * 1024 + lower_part[:, None] * band_freq[None, :]) % seq_total
    return wrapped.astype(jnp.float32) * (2.0 * math.pi / seq_total)


def filter_parts(places, band_freq, w_embed, b_embed, w_out, decay, seq_total):
    phases = band_phase(band_freq, places, seq_total)
    features = jnp.concatenate([jnp.cos(phases), jnp.sin(phases)], axis=1)
    preact = mat_dot(features, w_embed) + b_embed[None, :]
    hidden = jnp.sin(preact)
    fraction = places.astype(jnp.float32) / seq_total
    envelope = (
        jnp.exp(-decay[None, :] * fraction[:, None]) * jnp.sqrt((1.0 + decay) / seq_total)[None, :]
    )
    taps = mat_dot(hidden, w_out) * envelope
    return (features, preact, hidden, taps, envelope)


def angle_table(rows_idx, cols_idx, modulus):
    wrapped = rows_idx[:, None] * cols_idx[None, :] % modulus
    angles = wrapped.astype(jnp.float32) * (2.0 * math.pi / modulus)
    return (jnp.cos(angles), jnp.sin(angles))


def local(signal, cotangent, band_freq, w_embed, b_embed, w_out, decay):
    devices = lax.axis_size("seq")
    rank_seq = lax.axis_index("seq")
    seg_len = signal.shape[1] * 2
    channels = signal.shape[2] // 2
    block_w = seg_len // devices
    width = block_w * channels
    rows_all = 2 * devices
    pair = rows_all // devices
    seq_total = seg_len * devices
    fft_size = 2 * seq_total
    inv_scale = 1.0 / fft_size
    n_arr = 3

    dev_ids = jnp.arange(devices, dtype=jnp.int32)
    row_ids = jnp.arange(rows_all, dtype=jnp.int32)
    blk_ids = jnp.arange(block_w, dtype=jnp.int32)
    lane_blk = jnp.arange(width, dtype=jnp.int32) // channels
    b_lane = rank_seq * block_w + lane_blk

    src = jnp.stack(
        [signal.reshape(devices, width), cotangent.reshape(devices, width)], axis=1
    )
    cols = lax.all_to_all(src, "seq", split_axis=0, concat_axis=0, tiled=True)

    places = (
        dev_ids[:, None] * seg_len + rank_seq * block_w + blk_ids[None, :]
    ).reshape(-1)
    features, preact, hidden, taps, envelope = filter_parts(
        places, band_freq, w_embed, b_embed, w_out, decay, seq_total
    )
    stacked = jnp.concatenate(
        [cols.astype(jnp.float32), taps.reshape(devices, 1, width)], axis=1
    ).reshape(devices, n_arr * width)

    col_cos, col_sin = angle_table(row_ids, dev_ids, rows_all)
    y_re = mat_dot(col_cos, stacked).reshape(rows_all, n_arr, width)
    y_im = -mat_dot(col_sin, stacked).reshape(rows_all, n_arr, width)
    tw_cos, tw_sin = angle_table(row_ids, b_lane, fft_size)
    tw_cos = tw_cos[:, None, :]
    tw_sin = tw_sin[:, None, :]
    t_re = y_re * tw_cos + y_im * tw_sin
    t_im = y_im * tw_cos - y_re * tw_sin
    spec = jnp.stack([t_re, t_im], axis=1)
    spec = lax.all_to_all(spec, "seq", split_axis=0, concat_axis=0, tiled=True)

    q_cos, q_sin = angle_table(dev_ids, dev_ids, devices)
    stage_a = mat_dot(jnp.concatenate([q_cos, q_sin], axis=0), spec.reshape(devices, -1))
    stage_a = stage_a.reshape(2, devices, pair, 2, n_arr, width)
    a_re = stage_a[0, :, :, 0] + stage_a[1, :, :, 1]
    a_im = stage_a[0, :, :, 1] - stage_a[1, :, :, 0]
    mid_cos, mid_sin = angle_table(dev_ids, lane_blk, seg_len)
    mid_cos = mid_cos[:, None, None, :]
    mid_sin = mid_sin[:, None, None, :]
    b_re = a_re * mid_cos + a_im * mid_sin
    b_im = a_im * mid_cos - a_re * mid_sin
    m_cos, m_sin = angle_table(blk_ids, blk_ids, block_w)
    eye_c = jnp.eye(channels, dtype=jnp.float32)
    kron_cos = (m_cos[:, None, :, None] * eye_c[None, :, None, :]).reshape(width, width)
    kron_sin = (m_sin[:, None, :, None] * eye_c[None, :, None, :]).reshape(width, width)
    kron_tab = jnp.concatenate([kron_cos, kron_sin], axis=1)
    n_rows = devices * pair * n_arr

    def blk_mix(vals_re, vals_im):
        both = jnp.concatenate([vals_re.reshape(n_rows, width), vals_im.reshape(n_rows, width)])
        mixed = mat_dot(both, kron_tab).reshape(2, n_rows, 2, width)
        return mixed[0, :, 0], mixed[0, :, 1], mixed[1, :, 0], mixed[1, :, 1]

    rc, rs, ic, is_ = blk_mix(b_re, b_im)
    s_re = (rc + is_).reshape(devices, pair, n_arr, width)
    s_im = (ic - rs).reshape(devices, pair, n_arr, width)

    sig_r, cot_r, tap_r = s_re[:, :, 0], s_re[:, :, 1], s_re[:, :, 2]
    sig_i, cot_i, tap_i = s_im[:, :, 0], s_im[:, :, 1], s_im[:, :, 2]
    prod_r = jnp.stack(
        [sig_r * tap_r - sig_i * tap_i, cot_r * tap_r + cot_i * tap_i, cot_r * sig_r + cot_i * sig_i],
        axis=2,
    )
    prod_i = jnp.stack(
        [sig_r * tap_i + sig_i * tap_r, cot_i * tap_r - cot_r * tap_i, cot_i * sig_r - cot_r * sig_i],
        axis=2,
    )

    rc, rs, ic, is_ = blk_mix(prod_r, prod_i)
    u_re = (rc - is_).reshape(devices, pair, n_arr, width)
    u_im = (ic + rs).reshape(devices, pair, n_arr, width)
    v_re = u_re * mid_cos - u_im * mid_sin
    v_im = u_im * mid_cos + u_re * mid_sin
    v_all = jnp.stack([v_re, v_im]).reshape(2 * devices, -1)
    inv_mat = jnp.concatenate(
        [
            jnp.concatenate([q_cos, -q_sin], axis=1),
            jnp.concatenate([q_sin, q_cos], axis=1),
        ],
        axis=0,
    )
    w_all = mat_dot(inv_mat, v_all).reshape(2, devices, pair, n_arr, width)
    b_rows = dev_ids[:, None] * block_w + lane_blk[None, :]
    k1_own = rank_seq * pair + jnp.arange(pair, dtype=jnp.int32)
    ex_ang = (b_rows[:, None, :] * k1_own[None, :, None]) % fft_size
    ex_ang = ex_ang.astype(jnp.float32) * (2.0 * math.pi / fft_size)
    ex_cos = jnp.cos(ex_ang)[:, :, None, :]
    ex_sin = jnp.sin(ex_ang)[:, :, None, :]
    x_re = w_all[0] * ex_cos - w_all[1] * ex_sin
    x_im = w_all[0] * ex_sin + w_all[1] * ex_cos
    back = jnp.stack([x_re, x_im], axis=1)
    back = lax.all_to_all(back, "seq", split_axis=0, concat_axis=0, tiled=True)

    back = back.reshape(devices, 2, pair, n_arr * width)
    back = jnp.transpose(back, (1, 0, 2, 3)).reshape(2 * rows_all, n_arr * width)
    out_mat = jnp.concatenate([col_cos.T, -col_sin.T], axis=1)
    res = (mat_dot(out_mat, back) * inv_scale).reshape(devices, n_arr, width)

    rows_out = lax.all_to_all(
        res[:, 0:2].astype(jnp.bfloat16), "seq", split_axis=0, concat_axis=0, tiled=True
    )
    conv_out = rows_out[:, 0].reshape(1, seg_len // 2, 2 * channels)
    d_signal = rows_out[:, 1].reshape(1, seg_len // 2, 2 * channels)

    d_taps = res[:, 2].reshape(devices * block_w, channels)
    d_raw = d_taps * envelope
    d_preact = mat_dot(d_raw, w_out.T) * jnp.cos(preact)
    out_part = mat_dot(hidden.T, d_raw)
    embed_part = mat_dot(features.T, d_preact)
    bias_part = jnp.sum(d_preact, axis=0)
    rank_chan = lax.axis_index("chan")
    n_chan = lax.axis_size("chan")
    out_wide = jnp.zeros((out_part.shape[0], n_chan * channels), jnp.float32)
    out_wide = lax.dynamic_update_slice_in_dim(out_wide, out_part, rank_chan * channels, axis=1)
    n_all = devices * n_chan
    flat = jnp.concatenate([out_wide.reshape(-1), embed_part.reshape(-1), bias_part])
    piece = -(-flat.shape[0] // (n_all * 128)) * 128
    flat = jnp.pad(flat, (0, n_all * piece - flat.shape[0])).reshape(n_all, piece)
    mine = jnp.sum(lax.all_to_all(flat, ("seq", "chan"), 0, 0, tiled=True), axis=0)
    total = lax.all_to_all(
        jnp.broadcast_to(mine, (n_all, piece)), ("seq", "chan"), 0, 0, tiled=True
    ).reshape(-1)
    n_out = out_wide.size
    n_emb = embed_part.size
    wide_sum = total[:n_out].reshape(out_wide.shape)
    embed_all = total[n_out : n_out + n_emb].reshape(embed_part.shape)
    bias_all = total[n_out + n_emb : n_out + n_emb + bias_part.size]
    out_sum = lax.dynamic_slice_in_dim(wide_sum, rank_chan * channels, channels, axis=1)
    norm_scale = 1.0 / math.sqrt(seq_total)
    return (conv_out, d_signal, embed_all * norm_scale, bias_all * norm_scale, out_sum * norm_scale)


def solution(mesh):
    return jax.shard_map(
        local,
        mesh=mesh,
        in_specs=(
            P("chan", "seq", None),
            P("chan", "seq", None),
            P(),
            P(),
            P(),
            P(None, "chan"),
            P("chan"),
        ),
        out_specs=(P("chan", "seq", None), P("chan", "seq", None), P(), P(), P(None, "chan")),
        check_vma=False,
    )
```

```python
import math

import jax
import jax.numpy as jnp
from jax import lax
from jax.sharding import PartitionSpec as P

exact_mode = lax.Precision.HIGHEST


def mat_dot(lhs_mat, rhs_mat):
    return jnp.dot(lhs_mat, rhs_mat, preferred_element_type=jnp.float32, precision=exact_mode)


def band_phase(band_freq, places, seq_total):
    upper_part = places // 1024
    lower_part = places % 1024
    partial_turn = upper_part[:, None] * band_freq[None, :] % seq_total
    wrapped = (partial_turn * 1024 + lower_part[:, None] * band_freq[None, :]) % seq_total
    return wrapped.astype(jnp.float32) * (2.0 * math.pi / seq_total)


def filter_parts(places, band_freq, w_embed, b_embed, w_out, decay, seq_total):
    phases = band_phase(band_freq, places, seq_total)
    features = jnp.concatenate([jnp.cos(phases), jnp.sin(phases)], axis=1)
    preact = mat_dot(features, w_embed) + b_embed[None, :]
    hidden = jnp.sin(preact)
    fraction = places.astype(jnp.float32) / seq_total
    envelope = (
        jnp.exp(-decay[None, :] * fraction[:, None]) * jnp.sqrt((1.0 + decay) / seq_total)[None, :]
    )
    taps = mat_dot(hidden, w_out) * envelope
    return (features, preact, hidden, taps, envelope)


def angle_table(rows_idx, cols_idx, modulus):
    wrapped = rows_idx[:, None] * cols_idx[None, :] % modulus
    angles = wrapped.astype(jnp.float32) * (2.0 * math.pi / modulus)
    return (jnp.cos(angles), jnp.sin(angles))


def local(signal, cotangent, band_freq, w_embed, b_embed, w_out, decay):
    devices = lax.axis_size("seq")
    rank_seq = lax.axis_index("seq")
    seg_len = signal.shape[1] * 2
    channels = signal.shape[2] // 2
    block_w = seg_len // devices
    width = block_w * channels
    rows_all = 2 * devices
    pair = rows_all // devices
    seq_total = seg_len * devices
    fft_size = 2 * seq_total
    inv_scale = 1.0 / fft_size
    n_arr = 3

    dev_ids = jnp.arange(devices, dtype=jnp.int32)
    row_ids = jnp.arange(rows_all, dtype=jnp.int32)
    blk_ids = jnp.arange(block_w, dtype=jnp.int32)
    lane_blk = jnp.arange(width, dtype=jnp.int32) // channels
    b_lane = rank_seq * block_w + lane_blk

    src = jnp.stack(
        [signal.reshape(devices, width), cotangent.reshape(devices, width)], axis=1
    )
    cols = lax.all_to_all(src, "seq", split_axis=0, concat_axis=0, tiled=True)

    places = (
        dev_ids[:, None] * seg_len + rank_seq * block_w + blk_ids[None, :]
    ).reshape(-1)
    features, preact, hidden, taps, envelope = filter_parts(
        places, band_freq, w_embed, b_embed, w_out, decay, seq_total
    )
    stacked = jnp.concatenate(
        [cols.astype(jnp.float32), taps.reshape(devices, 1, width)], axis=1
    ).reshape(devices, n_arr * width)

    col_cos, col_sin = angle_table(row_ids, dev_ids, rows_all)
    y_re = mat_dot(col_cos, stacked).reshape(rows_all, n_arr, width)
    y_im = -mat_dot(col_sin, stacked).reshape(rows_all, n_arr, width)
    tw_cos, tw_sin = angle_table(row_ids, b_lane, fft_size)
    tw_cos = tw_cos[:, None, :]
    tw_sin = tw_sin[:, None, :]
    t_re = y_re * tw_cos + y_im * tw_sin
    t_im = y_im * tw_cos - y_re * tw_sin
    spec = jnp.stack([t_re, t_im], axis=1)
    spec = lax.all_to_all(
        spec.astype(jnp.bfloat16), "seq", split_axis=0, concat_axis=0, tiled=True
    ).astype(jnp.float32)

    q_cos, q_sin = angle_table(dev_ids, dev_ids, devices)
    stage_a = mat_dot(jnp.concatenate([q_cos, q_sin], axis=0), spec.reshape(devices, -1))
    stage_a = stage_a.reshape(2, devices, pair, 2, n_arr, width)
    a_re = stage_a[0, :, :, 0] + stage_a[1, :, :, 1]
    a_im = stage_a[0, :, :, 1] - stage_a[1, :, :, 0]
    mid_cos, mid_sin = angle_table(dev_ids, lane_blk, seg_len)
    mid_cos = mid_cos[:, None, None, :]
    mid_sin = mid_sin[:, None, None, :]
    b_re = (a_re * mid_cos + a_im * mid_sin).reshape(devices, pair, n_arr, block_w, channels)
    b_im = (a_im * mid_cos - a_re * mid_sin).reshape(devices, pair, n_arr, block_w, channels)
    m_cos, m_sin = angle_table(blk_ids, blk_ids, block_w)

    def blk_mix(table, vals):
        return jnp.einsum(
            "mb,qkzbc->qkzmc", table, vals, preferred_element_type=jnp.float32,
            precision=exact_mode,
        )

    s_re = blk_mix(m_cos, b_re) + blk_mix(m_sin, b_im)
    s_im = blk_mix(m_cos, b_im) - blk_mix(m_sin, b_re)

    sig_r, cot_r, tap_r = s_re[:, :, 0], s_re[:, :, 1], s_re[:, :, 2]
    sig_i, cot_i, tap_i = s_im[:, :, 0], s_im[:, :, 1], s_im[:, :, 2]
    prod_r = jnp.stack(
        [sig_r * tap_r - sig_i * tap_i, cot_r * tap_r + cot_i * tap_i, cot_r * sig_r + cot_i * sig_i],
        axis=2,
    )
    prod_i = jnp.stack(
        [sig_r * tap_i + sig_i * tap_r, cot_i * tap_r - cot_r * tap_i, cot_i * sig_r - cot_r * sig_i],
        axis=2,
    )

    u_re = blk_mix(m_cos, prod_r) - blk_mix(m_sin, prod_i)
    u_im = blk_mix(m_cos, prod_i) + blk_mix(m_sin, prod_r)
    u_re = u_re.reshape(devices, pair, n_arr, width)
    u_im = u_im.reshape(devices, pair, n_arr, width)
    v_re = u_re * mid_cos - u_im * mid_sin
    v_im = u_im * mid_cos + u_re * mid_sin
    v_all = jnp.stack([v_re, v_im]).reshape(2 * devices, -1)
    inv_mat = jnp.concatenate(
        [
            jnp.concatenate([q_cos, -q_sin], axis=1),
            jnp.concatenate([q_sin, q_cos], axis=1),
        ],
        axis=0,
    )
    w_all = mat_dot(inv_mat, v_all).reshape(2, devices, pair, n_arr, width)
    b_rows = dev_ids[:, None] * block_w + lane_blk[None, :]
    k1_own = rank_seq * pair + jnp.arange(pair, dtype=jnp.int32)
    ex_ang = (b_rows[:, None, :] * k1_own[None, :, None]) % fft_size
    ex_ang = ex_ang.astype(jnp.float32) * (2.0 * math.pi / fft_size)
    ex_cos = jnp.cos(ex_ang)[:, :, None, :]
    ex_sin = jnp.sin(ex_ang)[:, :, None, :]
    x_re = w_all[0] * ex_cos - w_all[1] * ex_sin
    x_im = w_all[0] * ex_sin + w_all[1] * ex_cos
    back = jnp.stack([x_re, x_im], axis=1)
    back = lax.all_to_all(
        back.astype(jnp.bfloat16), "seq", split_axis=0, concat_axis=0, tiled=True
    ).astype(jnp.float32)

    back = back.reshape(devices, 2, pair, n_arr * width)
    back = jnp.transpose(back, (1, 0, 2, 3)).reshape(2 * rows_all, n_arr * width)
    out_mat = jnp.concatenate([col_cos.T, -col_sin.T], axis=1)
    res = (mat_dot(out_mat, back) * inv_scale).reshape(devices, n_arr, width)

    rows_out = lax.all_to_all(
        res[:, 0:2].astype(jnp.bfloat16), "seq", split_axis=0, concat_axis=0, tiled=True
    )
    conv_out = rows_out[:, 0].reshape(1, seg_len // 2, 2 * channels)
    d_signal = rows_out[:, 1].reshape(1, seg_len // 2, 2 * channels)

    d_taps = res[:, 2].reshape(devices * block_w, channels)
    d_raw = d_taps * envelope
    d_preact = mat_dot(d_raw, w_out.T) * jnp.cos(preact)
    out_part = mat_dot(hidden.T, d_raw)
    embed_part = mat_dot(features.T, d_preact)
    bias_part = jnp.sum(d_preact, axis=0)
    rank_chan = lax.axis_index("chan")
    n_chan = lax.axis_size("chan")
    out_wide = jnp.zeros((out_part.shape[0], n_chan * channels), jnp.float32)
    out_wide = lax.dynamic_update_slice_in_dim(out_wide, out_part, rank_chan * channels, axis=1)
    n_all = devices * n_chan
    flat = jnp.concatenate([out_wide.reshape(-1), embed_part.reshape(-1), bias_part])
    piece = -(-flat.shape[0] // (n_all * 128)) * 128
    flat = jnp.pad(flat, (0, n_all * piece - flat.shape[0])).reshape(n_all, piece)
    mine = jnp.sum(lax.all_to_all(flat, ("seq", "chan"), 0, 0, tiled=True), axis=0)
    total = lax.all_to_all(
        jnp.broadcast_to(mine, (n_all, piece)), ("seq", "chan"), 0, 0, tiled=True
    ).reshape(-1)
    n_out = out_wide.size
    n_emb = embed_part.size
    wide_sum = total[:n_out].reshape(out_wide.shape)
    embed_all = total[n_out : n_out + n_emb].reshape(embed_part.shape)
    bias_all = total[n_out + n_emb : n_out + n_emb + bias_part.size]
    out_sum = lax.dynamic_slice_in_dim(wide_sum, rank_chan * channels, channels, axis=1)
    norm_scale = 1.0 / math.sqrt(seq_total)
    return (conv_out, d_signal, embed_all * norm_scale, bias_all * norm_scale, out_sum * norm_scale)


def solution(mesh):
    return jax.shard_map(
        local,
        mesh=mesh,
        in_specs=(
            P("chan", "seq", None),
            P("chan", "seq", None),
            P(),
            P(),
            P(),
            P(None, "chan"),
            P("chan"),
        ),
        out_specs=(P("chan", "seq", None), P("chan", "seq", None), P(), P(), P(None, "chan")),
        check_vma=False,
    )
```

```python
import math

import jax
import jax.numpy as jnp
from jax import lax
from jax.sharding import PartitionSpec as P

exact_mode = lax.Precision.HIGHEST


def mat_dot(lhs_mat, rhs_mat):
    return jnp.dot(lhs_mat, rhs_mat, preferred_element_type=jnp.float32, precision=exact_mode)


def band_phase(band_freq, places, seq_total):
    upper_part = places // 1024
    lower_part = places % 1024
    partial_turn = upper_part[:, None] * band_freq[None, :] % seq_total
    wrapped = (partial_turn * 1024 + lower_part[:, None] * band_freq[None, :]) % seq_total
    return wrapped.astype(jnp.float32) * (2.0 * math.pi / seq_total)


def filter_parts(places, band_freq, w_embed, b_embed, w_out, decay, seq_total):
    phases = band_phase(band_freq, places, seq_total)
    features = jnp.concatenate([jnp.cos(phases), jnp.sin(phases)], axis=1)
    preact = mat_dot(features, w_embed) + b_embed[None, :]
    hidden = jnp.sin(preact)
    fraction = places.astype(jnp.float32) / seq_total
    envelope = (
        jnp.exp(-decay[None, :] * fraction[:, None]) * jnp.sqrt((1.0 + decay) / seq_total)[None, :]
    )
    taps = mat_dot(hidden, w_out) * envelope
    return (features, preact, hidden, taps, envelope)


def angle_table(rows_idx, cols_idx, modulus):
    wrapped = rows_idx[:, None] * cols_idx[None, :] % modulus
    angles = wrapped.astype(jnp.float32) * (2.0 * math.pi / modulus)
    return (jnp.cos(angles), jnp.sin(angles))


def local(signal, cotangent, band_freq, w_embed, b_embed, w_out, decay):
    devices = lax.axis_size("seq")
    rank_seq = lax.axis_index("seq")
    seg_len = signal.shape[1] * 2
    channels = signal.shape[2] // 2
    block_w = seg_len // devices
    width = block_w * channels
    rows_all = 2 * devices
    pair = rows_all // devices
    seq_total = seg_len * devices
    fft_size = 2 * seq_total
    inv_scale = 1.0 / fft_size
    n_arr = 3

    dev_ids = jnp.arange(devices, dtype=jnp.int32)
    row_ids = jnp.arange(rows_all, dtype=jnp.int32)
    blk_ids = jnp.arange(block_w, dtype=jnp.int32)
    lane_blk = jnp.arange(width, dtype=jnp.int32) // channels
    b_lane = rank_seq * block_w + lane_blk

    src = jnp.stack(
        [signal.reshape(devices, width), cotangent.reshape(devices, width)], axis=1
    )
    cols = lax.all_to_all(src, "seq", split_axis=0, concat_axis=0, tiled=True)

    places = (
        dev_ids[:, None] * seg_len + rank_seq * block_w + blk_ids[None, :]
    ).reshape(-1)
    features, preact, hidden, taps, envelope = filter_parts(
        places, band_freq, w_embed, b_embed, w_out, decay, seq_total
    )
    stacked = jnp.concatenate(
        [cols.astype(jnp.float32), taps.reshape(devices, 1, width)], axis=1
    ).reshape(devices, n_arr * width)

    col_cos, col_sin = angle_table(row_ids, dev_ids, rows_all)
    y_re = mat_dot(col_cos, stacked).reshape(rows_all, n_arr, width)
    y_im = -mat_dot(col_sin, stacked).reshape(rows_all, n_arr, width)
    tw_cos, tw_sin = angle_table(row_ids, b_lane, fft_size)
    tw_cos = tw_cos[:, None, :]
    tw_sin = tw_sin[:, None, :]
    t_re = y_re * tw_cos + y_im * tw_sin
    t_im = y_im * tw_cos - y_re * tw_sin
    spec = jnp.stack([t_re, t_im], axis=1)
    spec = lax.all_to_all(
        spec.astype(jnp.bfloat16), "seq", split_axis=0, concat_axis=0, tiled=True
    ).astype(jnp.float32)

    q_cos, q_sin = angle_table(dev_ids, dev_ids, devices)
    stage_a = mat_dot(jnp.concatenate([q_cos, q_sin], axis=0), spec.reshape(devices, -1))
    stage_a = stage_a.reshape(2, devices, pair, 2, n_arr, width)
    a_re = stage_a[0, :, :, 0] + stage_a[1, :, :, 1]
    a_im = stage_a[0, :, :, 1] - stage_a[1, :, :, 0]
    mid_cos, mid_sin = angle_table(dev_ids, lane_blk, seg_len)
    mid_cos = mid_cos[:, None, None, :]
    mid_sin = mid_sin[:, None, None, :]
    b_re = (a_re * mid_cos + a_im * mid_sin).reshape(devices, pair, n_arr, block_w, channels)
    b_im = (a_im * mid_cos - a_re * mid_sin).reshape(devices, pair, n_arr, block_w, channels)
    m_cos, m_sin = angle_table(blk_ids, blk_ids, block_w)

    def blk_mix(table, vals):
        return jnp.einsum(
            "mb,qkzbc->qkzmc", table, vals, preferred_element_type=jnp.float32,
            precision=exact_mode,
        )

    s_re = blk_mix(m_cos, b_re) + blk_mix(m_sin, b_im)
    s_im = blk_mix(m_cos, b_im) - blk_mix(m_sin, b_re)

    sig_r, cot_r, tap_r = s_re[:, :, 0], s_re[:, :, 1], s_re[:, :, 2]
    sig_i, cot_i, tap_i = s_im[:, :, 0], s_im[:, :, 1], s_im[:, :, 2]
    prod_r = jnp.stack(
        [sig_r * tap_r - sig_i * tap_i, cot_r * tap_r + cot_i * tap_i, cot_r * sig_r + cot_i * sig_i],
        axis=2,
    )
    prod_i = jnp.stack(
        [sig_r * tap_i + sig_i * tap_r, cot_i * tap_r - cot_r * tap_i, cot_i * sig_r - cot_r * sig_i],
        axis=2,
    )

    u_re = blk_mix(m_cos, prod_r) - blk_mix(m_sin, prod_i)
    u_im = blk_mix(m_cos, prod_i) + blk_mix(m_sin, prod_r)
    u_re = u_re.reshape(devices, pair, n_arr, width)
    u_im = u_im.reshape(devices, pair, n_arr, width)
    v_re = u_re * mid_cos - u_im * mid_sin
    v_im = u_im * mid_cos + u_re * mid_sin
    v_all = jnp.stack([v_re, v_im]).reshape(2 * devices, -1)
    inv_mat = jnp.concatenate(
        [
            jnp.concatenate([q_cos, -q_sin], axis=1),
            jnp.concatenate([q_sin, q_cos], axis=1),
        ],
        axis=0,
    )
    w_all = mat_dot(inv_mat, v_all).reshape(2, devices, pair, n_arr, width)
    b_rows = dev_ids[:, None] * block_w + lane_blk[None, :]
    k1_own = rank_seq * pair + jnp.arange(pair, dtype=jnp.int32)
    ex_ang = (b_rows[:, None, :] * k1_own[None, :, None]) % fft_size
    ex_ang = ex_ang.astype(jnp.float32) * (2.0 * math.pi / fft_size)
    ex_cos = jnp.cos(ex_ang)[:, :, None, :]
    ex_sin = jnp.sin(ex_ang)[:, :, None, :]
    x_re = w_all[0] * ex_cos - w_all[1] * ex_sin
    x_im = w_all[0] * ex_sin + w_all[1] * ex_cos
    back = jnp.stack([x_re, x_im], axis=1)
    back = lax.all_to_all(
        back.astype(jnp.bfloat16), "seq", split_axis=0, concat_axis=0, tiled=True
    ).astype(jnp.float32)

    back = back.reshape(devices, 2, pair, n_arr * width)
    back = jnp.transpose(back, (1, 0, 2, 3)).reshape(2 * rows_all, n_arr * width)
    out_mat = jnp.concatenate([col_cos.T, -col_sin.T], axis=1)
    res = (mat_dot(out_mat, back) * inv_scale).reshape(devices, n_arr, width)

    d_taps = res[:, 2].reshape(devices * block_w, channels)
    d_raw = d_taps * envelope
    d_preact = mat_dot(d_raw, w_out.T) * jnp.cos(preact)
    out_part = mat_dot(hidden.T, d_raw)
    embed_part = mat_dot(features.T, d_preact)
    bias_part = jnp.sum(d_preact, axis=0)
    rank_chan = lax.axis_index("chan")
    n_chan = lax.axis_size("chan")
    out_wide = jnp.zeros((out_part.shape[0], n_chan * channels), jnp.float32)
    out_wide = lax.dynamic_update_slice_in_dim(out_wide, out_part, rank_chan * channels, axis=1)
    flat = jnp.concatenate([out_wide.reshape(-1), embed_part.reshape(-1), bias_part])
    piece = -(-flat.shape[0] // (devices * 128)) * 128
    flat = jnp.pad(flat, (0, devices * piece - flat.shape[0])).reshape(devices, piece)

    outgoing = jnp.concatenate([res[:, 0:2].reshape(devices, 2 * width), flat], axis=1)
    incoming = lax.all_to_all(outgoing, "seq", split_axis=0, concat_axis=0, tiled=True)
    rows_out = incoming[:, : 2 * width].reshape(devices, 2, width).astype(jnp.bfloat16)
    conv_out = rows_out[:, 0].reshape(1, seg_len // 2, 2 * channels)
    d_signal = rows_out[:, 1].reshape(1, seg_len // 2, 2 * channels)
    mine = jnp.sum(incoming[:, 2 * width :], axis=0)

    n_all = devices * n_chan
    total = lax.all_to_all(
        jnp.broadcast_to(mine, (n_all, piece)), ("seq", "chan"), 0, 0, tiled=True
    )
    total = jnp.sum(total.reshape(devices, n_chan, piece), axis=1).reshape(-1)
    n_out = out_wide.size
    n_emb = embed_part.size
    wide_sum = total[:n_out].reshape(out_wide.shape)
    embed_all = total[n_out : n_out + n_emb].reshape(embed_part.shape)
    bias_all = total[n_out + n_emb : n_out + n_emb + bias_part.size]
    out_sum = lax.dynamic_slice_in_dim(wide_sum, rank_chan * channels, channels, axis=1)
    norm_scale = 1.0 / math.sqrt(seq_total)
    return (conv_out, d_signal, embed_all * norm_scale, bias_all * norm_scale, out_sum * norm_scale)


def solution(mesh):
    return jax.shard_map(
        local,
        mesh=mesh,
        in_specs=(
            P("chan", "seq", None),
            P("chan", "seq", None),
            P(),
            P(),
            P(),
            P(None, "chan"),
            P("chan"),
        ),
        out_specs=(P("chan", "seq", None), P("chan", "seq", None), P(), P(), P(None, "chan")),
        check_vma=False,
    )
```

```python
import math

import jax
import jax.numpy as jnp
from jax import lax
from jax.sharding import PartitionSpec as P

exact_mode = lax.Precision.HIGHEST


def mat_dot(lhs_mat, rhs_mat):
    return jnp.dot(lhs_mat, rhs_mat, preferred_element_type=jnp.float32, precision=exact_mode)


def band_phase(band_freq, places, seq_total):
    upper_part = places // 1024
    lower_part = places % 1024
    partial_turn = upper_part[:, None] * band_freq[None, :] % seq_total
    wrapped = (partial_turn * 1024 + lower_part[:, None] * band_freq[None, :]) % seq_total
    return wrapped.astype(jnp.float32) * (2.0 * math.pi / seq_total)


def filter_parts(places, band_freq, w_embed, b_embed, w_out, decay, seq_total):
    phases = band_phase(band_freq, places, seq_total)
    features = jnp.concatenate([jnp.cos(phases), jnp.sin(phases)], axis=1)
    preact = mat_dot(features, w_embed) + b_embed[None, :]
    hidden = jnp.sin(preact)
    fraction = places.astype(jnp.float32) / seq_total
    envelope = (
        jnp.exp(-decay[None, :] * fraction[:, None]) * jnp.sqrt((1.0 + decay) / seq_total)[None, :]
    )
    taps = mat_dot(hidden, w_out) * envelope
    return (features, preact, hidden, taps, envelope)


def angle_table(rows_idx, cols_idx, modulus):
    wrapped = rows_idx[:, None] * cols_idx[None, :] % modulus
    angles = wrapped.astype(jnp.float32) * (2.0 * math.pi / modulus)
    return (jnp.cos(angles), jnp.sin(angles))


def local(signal, cotangent, band_freq, w_embed, b_embed, w_out, decay):
    devices = lax.axis_size("seq")
    rank_seq = lax.axis_index("seq")
    seg_len = signal.shape[1] * 2
    channels = signal.shape[2] // 2
    block_w = seg_len // devices
    width = block_w * channels
    rows_all = 2 * devices
    pair = rows_all // devices
    seq_total = seg_len * devices
    fft_size = 2 * seq_total
    inv_scale = 1.0 / fft_size
    n_arr = 3

    dev_ids = jnp.arange(devices, dtype=jnp.int32)
    row_ids = jnp.arange(rows_all, dtype=jnp.int32)
    blk_ids = jnp.arange(block_w, dtype=jnp.int32)
    lane_blk = jnp.arange(width, dtype=jnp.int32) // channels
    b_lane = rank_seq * block_w + lane_blk

    src = jnp.stack(
        [signal.reshape(devices, width), cotangent.reshape(devices, width)], axis=1
    )
    cols = lax.all_to_all(src, "seq", split_axis=0, concat_axis=0, tiled=True)

    places = (
        dev_ids[:, None] * seg_len + rank_seq * block_w + blk_ids[None, :]
    ).reshape(-1)
    features, preact, hidden, taps, envelope = filter_parts(
        places, band_freq, w_embed, b_embed, w_out, decay, seq_total
    )
    stacked = jnp.concatenate(
        [cols.astype(jnp.float32), taps.reshape(devices, 1, width)], axis=1
    ).reshape(devices, n_arr * width)

    col_cos, col_sin = angle_table(row_ids, dev_ids, rows_all)
    y_re = mat_dot(col_cos, stacked).reshape(rows_all, n_arr, width)
    y_im = -mat_dot(col_sin, stacked).reshape(rows_all, n_arr, width)
    tw_cos, tw_sin = angle_table(row_ids, b_lane, fft_size)
    tw_cos = tw_cos[:, None, :]
    tw_sin = tw_sin[:, None, :]
    t_re = y_re * tw_cos + y_im * tw_sin
    t_im = y_im * tw_cos - y_re * tw_sin
    spec = jnp.stack([t_re, t_im], axis=1)
    spec = lax.all_to_all(
        spec.astype(jnp.bfloat16), "seq", split_axis=0, concat_axis=0, tiled=True
    ).astype(jnp.float32)

    q_cos, q_sin = angle_table(dev_ids, dev_ids, devices)
    stage_a = mat_dot(jnp.concatenate([q_cos, q_sin], axis=0), spec.reshape(devices, -1))
    lanes = 2 * channels
    n_grp = width // lanes
    blocks = [(z, k1l) for z in range(n_arr) for k1l in range(pair)]
    n_blk = len(blocks)
    lane_h = jnp.arange(lanes, dtype=jnp.int32) // channels
    flip = jnp.where(lane_h == 0, 1.0, -1.0).astype(jnp.float32)

    def col(k1l, ri, z, p):
        return ((k1l * 2 + ri) * n_arr + z) * width + p * lanes

    def rows_of(part, ri, p):
        return jnp.concatenate(
            [part[:, col(k1l, ri, z, p) : col(k1l, ri, z, p) + lanes] for z, k1l in blocks], axis=0
        )

    def mid_tab(p):
        c_t, s_t = angle_table(dev_ids, 2 * p + lane_h, seg_len)
        c_t = jnp.broadcast_to(c_t[None], (n_blk, devices, lanes)).reshape(n_blk * devices, lanes)
        s_t = jnp.broadcast_to(s_t[None], (n_blk, devices, lanes)).reshape(n_blk * devices, lanes)
        return c_t, s_t

    def lin(coefs, vals):
        acc = None
        for w, v in zip(coefs, vals):
            if abs(w) < 1e-12:
                continue
            term = v if w == 1.0 else (-v if w == -1.0 else v * w)
            acc = term if acc is None else acc + term
        return acc

    def w8(p, m):
        k = (p * m) % n_grp
        return (round(math.cos(2 * math.pi * k / n_grp), 15), round(math.sin(2 * math.pi * k / n_grp), 15))

    def half_tw(m):
        ang = 2 * math.pi * m / (2 * n_grp)
        c_t = jnp.where(lane_h == 1, math.cos(ang), 1.0).astype(jnp.float32)
        s_t = jnp.where(lane_h == 1, math.sin(ang), 0.0).astype(jnp.float32)
        return c_t, s_t

    def halves(x):
        return flip * x + jnp.roll(x, channels, axis=1)

    top = stage_a[:devices]
    bot = stage_a[devices:]
    x_re, x_im = [], []
    for p in range(n_grp):
        a_re = rows_of(top, 0, p) + rows_of(bot, 1, p)
        a_im = rows_of(top, 1, p) - rows_of(bot, 0, p)
        c_t, s_t = mid_tab(p)
        x_re.append(a_re * c_t + a_im * s_t)
        x_im.append(a_im * c_t - a_re * s_t)
    spec_re, spec_im = [], []
    for m in range(n_grp):
        cs = [w8(p, m) for p in range(n_grp)]
        g_re = lin([c for c, _ in cs] + [s for _, s in cs], x_re + x_im)
        g_im = lin([c for c, _ in cs] + [-s for _, s in cs], x_im + x_re)
        c_t, s_t = half_tw(m)
        h_re = g_re * c_t + g_im * s_t
        h_im = g_im * c_t - g_re * s_t
        spec_re.append(halves(h_re))
        spec_im.append(halves(h_im))

    span = pair * devices
    prod_re, prod_im = [], []
    for m in range(n_grp):
        sig_r, cot_r, tap_r = [spec_re[m][z * span : (z + 1) * span] for z in range(n_arr)]
        sig_i, cot_i, tap_i = [spec_im[m][z * span : (z + 1) * span] for z in range(n_arr)]
        prod_re.append(jnp.concatenate(
            [sig_r * tap_r - sig_i * tap_i, cot_r * tap_r + cot_i * tap_i, cot_r * sig_r + cot_i * sig_i]
        ))
        prod_im.append(jnp.concatenate(
            [sig_r * tap_i + sig_i * tap_r, cot_i * tap_r - cot_r * tap_i, cot_i * sig_r - cot_r * sig_i]
        ))

    hh_re, hh_im = [], []
    for m in range(n_grp):
        g_re = halves(prod_re[m])
        g_im = halves(prod_im[m])
        c_t, s_t = half_tw(m)
        hh_re.append(g_re * c_t - g_im * s_t)
        hh_im.append(g_im * c_t + g_re * s_t)
    v_cols_re, v_cols_im = {}, {}
    for p in range(n_grp):
        cs = [w8(p, m) for m in range(n_grp)]
        u_re = lin([c for c, _ in cs] + [-s for _, s in cs], hh_re + hh_im)
        u_im = lin([c for c, _ in cs] + [s for _, s in cs], hh_im + hh_re)
        c_t, s_t = mid_tab(p)
        v_re = u_re * c_t - u_im * s_t
        v_im = u_im * c_t + u_re * s_t
        for idx, (z, k1l) in enumerate(blocks):
            v_cols_re[(k1l, z, p)] = v_re[idx * devices : (idx + 1) * devices]
            v_cols_im[(k1l, z, p)] = v_im[idx * devices : (idx + 1) * devices]
    order = [(k1l, z, p) for k1l in range(pair) for z in range(n_arr) for p in range(n_grp)]
    v_all = jnp.concatenate(
        [
            jnp.concatenate([v_cols_re[key] for key in order], axis=1),
            jnp.concatenate([v_cols_im[key] for key in order], axis=1),
        ],
        axis=0,
    )
    inv_mat = jnp.concatenate(
        [
            jnp.concatenate([q_cos, -q_sin], axis=1),
            jnp.concatenate([q_sin, q_cos], axis=1),
        ],
        axis=0,
    )
    w_all = mat_dot(inv_mat, v_all).reshape(2, devices, pair, n_arr, width)
    b_rows = dev_ids[:, None] * block_w + lane_blk[None, :]
    k1_own = rank_seq * pair + jnp.arange(pair, dtype=jnp.int32)
    ex_ang = (b_rows[:, None, :] * k1_own[None, :, None]) % fft_size
    ex_ang = ex_ang.astype(jnp.float32) * (2.0 * math.pi / fft_size)
    ex_cos = jnp.cos(ex_ang)[:, :, None, :]
    ex_sin = jnp.sin(ex_ang)[:, :, None, :]
    x_re = w_all[0] * ex_cos - w_all[1] * ex_sin
    x_im = w_all[0] * ex_sin + w_all[1] * ex_cos
    back = jnp.stack([x_re, x_im], axis=1)
    back = lax.all_to_all(
        back.astype(jnp.bfloat16), "seq", split_axis=0, concat_axis=0, tiled=True
    ).astype(jnp.float32)

    back = back.reshape(devices, 2, pair, n_arr * width)
    back = jnp.transpose(back, (1, 0, 2, 3)).reshape(2 * rows_all, n_arr * width)
    out_mat = jnp.concatenate([col_cos.T, -col_sin.T], axis=1)
    res = (mat_dot(out_mat, back) * inv_scale).reshape(devices, n_arr, width)

    d_taps = res[:, 2].reshape(devices * block_w, channels)
    d_raw = d_taps * envelope
    d_preact = mat_dot(d_raw, w_out.T) * jnp.cos(preact)
    out_part = mat_dot(hidden.T, d_raw)
    embed_part = mat_dot(features.T, d_preact)
    bias_part = jnp.sum(d_preact, axis=0)
    rank_chan = lax.axis_index("chan")
    n_chan = lax.axis_size("chan")
    out_wide = jnp.zeros((out_part.shape[0], n_chan * channels), jnp.float32)
    out_wide = lax.dynamic_update_slice_in_dim(out_wide, out_part, rank_chan * channels, axis=1)
    flat = jnp.concatenate([out_wide.reshape(-1), embed_part.reshape(-1), bias_part])
    piece = -(-flat.shape[0] // (devices * 128)) * 128
    flat = jnp.pad(flat, (0, devices * piece - flat.shape[0])).reshape(devices, piece)

    outgoing = jnp.concatenate([res[:, 0:2].reshape(devices, 2 * width), flat], axis=1)
    incoming = lax.all_to_all(outgoing, "seq", split_axis=0, concat_axis=0, tiled=True)
    rows_out = incoming[:, : 2 * width].reshape(devices, 2, width).astype(jnp.bfloat16)
    conv_out = rows_out[:, 0].reshape(1, seg_len // 2, 2 * channels)
    d_signal = rows_out[:, 1].reshape(1, seg_len // 2, 2 * channels)
    mine = jnp.sum(incoming[:, 2 * width :], axis=0)

    n_all = devices * n_chan
    total = lax.all_to_all(
        jnp.broadcast_to(mine, (n_all, piece)), ("seq", "chan"), 0, 0, tiled=True
    )
    total = jnp.sum(total.reshape(devices, n_chan, piece), axis=1).reshape(-1)
    n_out = out_wide.size
    n_emb = embed_part.size
    wide_sum = total[:n_out].reshape(out_wide.shape)
    embed_all = total[n_out : n_out + n_emb].reshape(embed_part.shape)
    bias_all = total[n_out + n_emb : n_out + n_emb + bias_part.size]
    out_sum = lax.dynamic_slice_in_dim(wide_sum, rank_chan * channels, channels, axis=1)
    norm_scale = 1.0 / math.sqrt(seq_total)
    return (conv_out, d_signal, embed_all * norm_scale, bias_all * norm_scale, out_sum * norm_scale)


def solution(mesh):
    return jax.shard_map(
        local,
        mesh=mesh,
        in_specs=(
            P("chan", "seq", None),
            P("chan", "seq", None),
            P(),
            P(),
            P(),
            P(None, "chan"),
            P("chan"),
        ),
        out_specs=(P("chan", "seq", None), P("chan", "seq", None), P(), P(), P(None, "chan")),
        check_vma=False,
    )
```

```python
import math

import jax
import jax.numpy as jnp
from jax import lax
from jax.sharding import PartitionSpec as P

exact_mode = lax.Precision.HIGHEST


def mat_dot(lhs_mat, rhs_mat):
    return jnp.dot(lhs_mat, rhs_mat, preferred_element_type=jnp.float32, precision=exact_mode)


def band_phase(band_freq, places, seq_total):
    upper_part = places // 1024
    lower_part = places % 1024
    partial_turn = upper_part[:, None] * band_freq[None, :] % seq_total
    wrapped = (partial_turn * 1024 + lower_part[:, None] * band_freq[None, :]) % seq_total
    return wrapped.astype(jnp.float32) * (2.0 * math.pi / seq_total)


def filter_parts(places, band_freq, w_embed, b_embed, w_out, decay, seq_total):
    phases = band_phase(band_freq, places, seq_total)
    features = jnp.concatenate([jnp.cos(phases), jnp.sin(phases)], axis=1)
    preact = mat_dot(features, w_embed) + b_embed[None, :]
    hidden = jnp.sin(preact)
    fraction = places.astype(jnp.float32) / seq_total
    envelope = (
        jnp.exp(-decay[None, :] * fraction[:, None]) * jnp.sqrt((1.0 + decay) / seq_total)[None, :]
    )
    taps = mat_dot(hidden, w_out) * envelope
    return (features, preact, hidden, taps, envelope)


def angle_table(rows_idx, cols_idx, modulus):
    wrapped = rows_idx[:, None] * cols_idx[None, :] % modulus
    angles = wrapped.astype(jnp.float32) * (2.0 * math.pi / modulus)
    return (jnp.cos(angles), jnp.sin(angles))


def local(signal, cotangent, band_freq, w_embed, b_embed, w_out, decay):
    devices = lax.axis_size("seq")
    rank_seq = lax.axis_index("seq")
    seg_len = signal.shape[1] * 2
    channels = signal.shape[2] // 2
    block_w = seg_len // devices
    width = block_w * channels
    rows_all = 2 * devices
    pair = rows_all // devices
    seq_total = seg_len * devices
    fft_size = 2 * seq_total
    inv_scale = 1.0 / fft_size
    n_arr = 3

    dev_ids = jnp.arange(devices, dtype=jnp.int32)
    row_ids = jnp.arange(rows_all, dtype=jnp.int32)
    blk_ids = jnp.arange(block_w, dtype=jnp.int32)
    lane_blk = jnp.arange(width, dtype=jnp.int32) // channels
    b_lane = rank_seq * block_w + lane_blk

    src = jnp.stack(
        [signal.reshape(devices, width), cotangent.reshape(devices, width)], axis=1
    )
    cols = lax.all_to_all(src, "seq", split_axis=0, concat_axis=0, tiled=True)

    places = (
        dev_ids[:, None] * seg_len + rank_seq * block_w + blk_ids[None, :]
    ).reshape(-1)
    features, preact, hidden, taps, envelope = filter_parts(
        places, band_freq, w_embed, b_embed, w_out, decay, seq_total
    )
    stacked = jnp.concatenate(
        [cols.astype(jnp.float32), taps.reshape(devices, 1, width)], axis=1
    ).reshape(devices, n_arr * width)

    col_cos, col_sin = angle_table(row_ids, dev_ids, rows_all)
    tw_cos, tw_sin = angle_table(row_ids, b_lane, fft_size)
    send_parts = []
    for k1l in range(pair):
        y_re = mat_dot(col_cos[k1l::pair], stacked).reshape(devices, n_arr, width)
        y_im = -mat_dot(col_sin[k1l::pair], stacked).reshape(devices, n_arr, width)
        c_t = tw_cos[k1l::pair][:, None, :]
        s_t = tw_sin[k1l::pair][:, None, :]
        send_parts.append((y_re * c_t + y_im * s_t).reshape(devices, n_arr * width))
        send_parts.append((y_im * c_t - y_re * s_t).reshape(devices, n_arr * width))
    spec = jnp.concatenate(send_parts, axis=1).astype(jnp.bfloat16)
    spec = lax.all_to_all(spec, "seq", split_axis=0, concat_axis=0, tiled=True)
    spec = spec.astype(jnp.float32)

    q_cos, q_sin = angle_table(dev_ids, dev_ids, devices)
    stage_a = mat_dot(jnp.concatenate([q_cos, q_sin], axis=0), spec)
    lanes = 2 * channels
    n_grp = width // lanes
    blocks = [(z, k1l) for z in range(n_arr) for k1l in range(pair)]
    n_blk = len(blocks)
    lane_h = jnp.arange(lanes, dtype=jnp.int32) // channels
    flip = jnp.where(lane_h == 0, 1.0, -1.0).astype(jnp.float32)

    def col(k1l, ri, z, p):
        return ((k1l * 2 + ri) * n_arr + z) * width + p * lanes

    def rows_of(part, ri, p):
        return jnp.concatenate(
            [part[:, col(k1l, ri, z, p) : col(k1l, ri, z, p) + lanes] for z, k1l in blocks], axis=0
        )

    def mid_tab(p):
        c_t, s_t = angle_table(dev_ids, 2 * p + lane_h, seg_len)
        c_t = jnp.broadcast_to(c_t[None], (n_blk, devices, lanes)).reshape(n_blk * devices, lanes)
        s_t = jnp.broadcast_to(s_t[None], (n_blk, devices, lanes)).reshape(n_blk * devices, lanes)
        return c_t, s_t

    def lin(coefs, vals):
        acc = None
        for w, v in zip(coefs, vals):
            if abs(w) < 1e-12:
                continue
            term = v if w == 1.0 else (-v if w == -1.0 else v * w)
            acc = term if acc is None else acc + term
        return acc

    def w8(p, m):
        k = (p * m) % n_grp
        return (round(math.cos(2 * math.pi * k / n_grp), 15), round(math.sin(2 * math.pi * k / n_grp), 15))

    def half_tw(m):
        ang = 2 * math.pi * m / (2 * n_grp)
        c_t = jnp.where(lane_h == 1, math.cos(ang), 1.0).astype(jnp.float32)
        s_t = jnp.where(lane_h == 1, math.sin(ang), 0.0).astype(jnp.float32)
        return c_t, s_t

    def halves(x):
        return flip * x + jnp.roll(x, channels, axis=1)

    top = stage_a[:devices]
    bot = stage_a[devices:]
    x_re, x_im = [], []
    for p in range(n_grp):
        a_re = rows_of(top, 0, p) + rows_of(bot, 1, p)
        a_im = rows_of(top, 1, p) - rows_of(bot, 0, p)
        c_t, s_t = mid_tab(p)
        x_re.append(a_re * c_t + a_im * s_t)
        x_im.append(a_im * c_t - a_re * s_t)
    spec_re, spec_im = [], []
    for m in range(n_grp):
        cs = [w8(p, m) for p in range(n_grp)]
        g_re = lin([c for c, _ in cs] + [s for _, s in cs], x_re + x_im)
        g_im = lin([c for c, _ in cs] + [-s for _, s in cs], x_im + x_re)
        c_t, s_t = half_tw(m)
        h_re = g_re * c_t + g_im * s_t
        h_im = g_im * c_t - g_re * s_t
        spec_re.append(halves(h_re))
        spec_im.append(halves(h_im))

    span = pair * devices
    prod_re, prod_im = [], []
    for m in range(n_grp):
        sig_r, cot_r, tap_r = [spec_re[m][z * span : (z + 1) * span] for z in range(n_arr)]
        sig_i, cot_i, tap_i = [spec_im[m][z * span : (z + 1) * span] for z in range(n_arr)]
        prod_re.append(jnp.concatenate(
            [sig_r * tap_r - sig_i * tap_i, cot_r * tap_r + cot_i * tap_i, cot_r * sig_r + cot_i * sig_i]
        ))
        prod_im.append(jnp.concatenate(
            [sig_r * tap_i + sig_i * tap_r, cot_i * tap_r - cot_r * tap_i, cot_i * sig_r - cot_r * sig_i]
        ))

    hh_re, hh_im = [], []
    for m in range(n_grp):
        g_re = halves(prod_re[m])
        g_im = halves(prod_im[m])
        c_t, s_t = half_tw(m)
        hh_re.append(g_re * c_t - g_im * s_t)
        hh_im.append(g_im * c_t + g_re * s_t)
    v_cols_re, v_cols_im = {}, {}
    for p in range(n_grp):
        cs = [w8(p, m) for m in range(n_grp)]
        u_re = lin([c for c, _ in cs] + [-s for _, s in cs], hh_re + hh_im)
        u_im = lin([c for c, _ in cs] + [s for _, s in cs], hh_im + hh_re)
        c_t, s_t = mid_tab(p)
        v_re = u_re * c_t - u_im * s_t
        v_im = u_im * c_t + u_re * s_t
        for idx, (z, k1l) in enumerate(blocks):
            v_cols_re[(k1l, z, p)] = v_re[idx * devices : (idx + 1) * devices]
            v_cols_im[(k1l, z, p)] = v_im[idx * devices : (idx + 1) * devices]
    order = [(k1l, z, p) for k1l in range(pair) for z in range(n_arr) for p in range(n_grp)]
    v_all = jnp.concatenate(
        [
            jnp.concatenate([v_cols_re[key] for key in order], axis=1),
            jnp.concatenate([v_cols_im[key] for key in order], axis=1),
        ],
        axis=0,
    )
    inv_mat = jnp.concatenate(
        [
            jnp.concatenate([q_cos, -q_sin], axis=1),
            jnp.concatenate([q_sin, q_cos], axis=1),
        ],
        axis=0,
    )
    w_all = mat_dot(inv_mat, v_all)
    b_rows = dev_ids[:, None] * block_w + lane_blk[None, :]
    back_re, back_im = [], []
    for k1l in range(pair):
        ex_ang = (b_rows * (rank_seq * pair + k1l)) % fft_size
        ex_ang = ex_ang.astype(jnp.float32) * (2.0 * math.pi / fft_size)
        ex_cos = jnp.tile(jnp.cos(ex_ang), (1, n_arr))
        ex_sin = jnp.tile(jnp.sin(ex_ang), (1, n_arr))
        span_c = slice(k1l * n_arr * width, (k1l + 1) * n_arr * width)
        w_re = w_all[:devices, span_c]
        w_im = w_all[devices:, span_c]
        back_re.append(w_re * ex_cos - w_im * ex_sin)
        back_im.append(w_re * ex_sin + w_im * ex_cos)
    back = jnp.concatenate(back_re + back_im, axis=1).astype(jnp.bfloat16)
    back = lax.all_to_all(back, "seq", split_axis=0, concat_axis=0, tiled=True)
    back = back.astype(jnp.float32)

    res = None
    for ri in range(2):
        for k1l in range(pair):
            k1_cols = dev_ids * pair + k1l
            c_t, s_t = angle_table(dev_ids, k1_cols, rows_all)
            mat = c_t if ri == 0 else -s_t
            cols0 = (ri * pair + k1l) * n_arr * width
            term = mat_dot(mat, back[:, cols0 : cols0 + n_arr * width])
            res = term if res is None else res + term
    res = (res * inv_scale).reshape(devices, n_arr, width)

    d_taps = res[:, 2].reshape(devices * block_w, channels)
    d_raw = d_taps * envelope
    d_preact = mat_dot(d_raw, w_out.T) * jnp.cos(preact)
    out_part = mat_dot(hidden.T, d_raw)
    embed_part = mat_dot(features.T, d_preact)
    bias_part = jnp.sum(d_preact, axis=0)
    rank_chan = lax.axis_index("chan")
    n_chan = lax.axis_size("chan")
    out_wide = jnp.zeros((out_part.shape[0], n_chan * channels), jnp.float32)
    out_wide = lax.dynamic_update_slice_in_dim(out_wide, out_part, rank_chan * channels, axis=1)
    flat = jnp.concatenate([out_wide.reshape(-1), embed_part.reshape(-1), bias_part])
    piece = -(-flat.shape[0] // (devices * 128)) * 128
    flat = jnp.pad(flat, (0, devices * piece - flat.shape[0])).reshape(devices, piece)

    outgoing = jnp.concatenate([res[:, 0:2].reshape(devices, 2 * width), flat], axis=1)
    incoming = lax.all_to_all(outgoing, "seq", split_axis=0, concat_axis=0, tiled=True)
    rows_out = incoming[:, : 2 * width].reshape(devices, 2, width).astype(jnp.bfloat16)
    conv_out = rows_out[:, 0].reshape(1, seg_len // 2, 2 * channels)
    d_signal = rows_out[:, 1].reshape(1, seg_len // 2, 2 * channels)
    mine = jnp.sum(incoming[:, 2 * width :], axis=0)

    n_all = devices * n_chan
    total = lax.all_to_all(
        jnp.broadcast_to(mine, (n_all, piece)), ("seq", "chan"), 0, 0, tiled=True
    )
    total = jnp.sum(total.reshape(devices, n_chan, piece), axis=1).reshape(-1)
    n_out = out_wide.size
    n_emb = embed_part.size
    wide_sum = total[:n_out].reshape(out_wide.shape)
    embed_all = total[n_out : n_out + n_emb].reshape(embed_part.shape)
    bias_all = total[n_out + n_emb : n_out + n_emb + bias_part.size]
    out_sum = lax.dynamic_slice_in_dim(wide_sum, rank_chan * channels, channels, axis=1)
    norm_scale = 1.0 / math.sqrt(seq_total)
    return (conv_out, d_signal, embed_all * norm_scale, bias_all * norm_scale, out_sum * norm_scale)


def solution(mesh):
    return jax.shard_map(
        local,
        mesh=mesh,
        in_specs=(
            P("chan", "seq", None),
            P("chan", "seq", None),
            P(),
            P(),
            P(),
            P(None, "chan"),
            P("chan"),
        ),
        out_specs=(P("chan", "seq", None), P("chan", "seq", None), P(), P(), P(None, "chan")),
        check_vma=False,
    )
```

```python
import math

import jax
import jax.numpy as jnp
from jax import lax
from jax.sharding import PartitionSpec as P

exact_mode = lax.Precision.HIGHEST


def mat_dot(lhs_mat, rhs_mat):
    return jnp.dot(lhs_mat, rhs_mat, preferred_element_type=jnp.float32, precision=exact_mode)


def fft_dot(lhs_mat, rhs_mat):
    return jnp.dot(
        lhs_mat, rhs_mat, preferred_element_type=jnp.float32, precision=lax.Precision.HIGH
    )


def band_phase(band_freq, places, seq_total):
    upper_part = places // 1024
    lower_part = places % 1024
    partial_turn = upper_part[:, None] * band_freq[None, :] % seq_total
    wrapped = (partial_turn * 1024 + lower_part[:, None] * band_freq[None, :]) % seq_total
    return wrapped.astype(jnp.float32) * (2.0 * math.pi / seq_total)


def filter_parts(places, band_freq, w_embed, b_embed, w_out, decay, seq_total):
    phases = band_phase(band_freq, places, seq_total)
    features = jnp.concatenate([jnp.cos(phases), jnp.sin(phases)], axis=1)
    preact = mat_dot(features, w_embed) + b_embed[None, :]
    hidden = jnp.sin(preact)
    fraction = places.astype(jnp.float32) / seq_total
    envelope = (
        jnp.exp(-decay[None, :] * fraction[:, None]) * jnp.sqrt((1.0 + decay) / seq_total)[None, :]
    )
    taps = mat_dot(hidden, w_out) * envelope
    return (features, preact, hidden, taps, envelope)


def angle_table(rows_idx, cols_idx, modulus):
    wrapped = rows_idx[:, None] * cols_idx[None, :] % modulus
    angles = wrapped.astype(jnp.float32) * (2.0 * math.pi / modulus)
    return (jnp.cos(angles), jnp.sin(angles))


def local(signal, cotangent, band_freq, w_embed, b_embed, w_out, decay):
    devices = lax.axis_size("seq")
    rank_seq = lax.axis_index("seq")
    seg_len = signal.shape[1] * 2
    channels = signal.shape[2] // 2
    block_w = seg_len // devices
    width = block_w * channels
    rows_all = 2 * devices
    pair = rows_all // devices
    seq_total = seg_len * devices
    fft_size = 2 * seq_total
    inv_scale = 1.0 / fft_size
    n_arr = 3

    dev_ids = jnp.arange(devices, dtype=jnp.int32)
    row_ids = jnp.arange(rows_all, dtype=jnp.int32)
    blk_ids = jnp.arange(block_w, dtype=jnp.int32)
    lane_blk = jnp.arange(width, dtype=jnp.int32) // channels
    b_lane = rank_seq * block_w + lane_blk

    src = jnp.stack(
        [signal.reshape(devices, width), cotangent.reshape(devices, width)], axis=1
    )
    cols = lax.all_to_all(src, "seq", split_axis=0, concat_axis=0, tiled=True)

    places = (
        dev_ids[:, None] * seg_len + rank_seq * block_w + blk_ids[None, :]
    ).reshape(-1)
    features, preact, hidden, taps, envelope = filter_parts(
        places, band_freq, w_embed, b_embed, w_out, decay, seq_total
    )
    stacked = jnp.concatenate(
        [cols.astype(jnp.float32), taps.reshape(devices, 1, width)], axis=1
    ).reshape(devices, n_arr * width)

    col_cos, col_sin = angle_table(row_ids, dev_ids, rows_all)
    y_re = fft_dot(col_cos, stacked).reshape(rows_all, n_arr, width)
    y_im = -fft_dot(col_sin, stacked).reshape(rows_all, n_arr, width)
    tw_cos, tw_sin = angle_table(row_ids, b_lane, fft_size)
    tw_cos = tw_cos[:, None, :]
    tw_sin = tw_sin[:, None, :]
    t_re = y_re * tw_cos + y_im * tw_sin
    t_im = y_im * tw_cos - y_re * tw_sin
    spec = jnp.stack([t_re, t_im], axis=1)
    spec = lax.all_to_all(
        spec.astype(jnp.bfloat16), "seq", split_axis=0, concat_axis=0, tiled=True
    ).astype(jnp.float32)

    q_cos, q_sin = angle_table(dev_ids, dev_ids, devices)
    stage_a = fft_dot(jnp.concatenate([q_cos, q_sin], axis=0), spec.reshape(devices, -1))
    lanes = 2 * channels
    n_grp = width // lanes
    blocks = [(z, k1l) for z in range(n_arr) for k1l in range(pair)]
    n_blk = len(blocks)
    lane_h = jnp.arange(lanes, dtype=jnp.int32) // channels
    flip = jnp.where(lane_h == 0, 1.0, -1.0).astype(jnp.float32)

    def col(k1l, ri, z, p):
        return ((k1l * 2 + ri) * n_arr + z) * width + p * lanes

    def rows_of(part, ri, p):
        return jnp.concatenate(
            [part[:, col(k1l, ri, z, p) : col(k1l, ri, z, p) + lanes] for z, k1l in blocks], axis=0
        )

    def mid_tab(p):
        c_t, s_t = angle_table(dev_ids, 2 * p + lane_h, seg_len)
        c_t = jnp.broadcast_to(c_t[None], (n_blk, devices, lanes)).reshape(n_blk * devices, lanes)
        s_t = jnp.broadcast_to(s_t[None], (n_blk, devices, lanes)).reshape(n_blk * devices, lanes)
        return c_t, s_t

    def lin(coefs, vals):
        acc = None
        for w, v in zip(coefs, vals):
            if abs(w) < 1e-12:
                continue
            term = v if w == 1.0 else (-v if w == -1.0 else v * w)
            acc = term if acc is None else acc + term
        return acc

    def w8(p, m):
        k = (p * m) % n_grp
        return (round(math.cos(2 * math.pi * k / n_grp), 15), round(math.sin(2 * math.pi * k / n_grp), 15))

    def half_tw(m):
        ang = 2 * math.pi * m / (2 * n_grp)
        c_t = jnp.where(lane_h == 1, math.cos(ang), 1.0).astype(jnp.float32)
        s_t = jnp.where(lane_h == 1, math.sin(ang), 0.0).astype(jnp.float32)
        return c_t, s_t

    def halves(x):
        return flip * x + jnp.roll(x, channels, axis=1)

    top = stage_a[:devices]
    bot = stage_a[devices:]
    x_re, x_im = [], []
    for p in range(n_grp):
        a_re = rows_of(top, 0, p) + rows_of(bot, 1, p)
        a_im = rows_of(top, 1, p) - rows_of(bot, 0, p)
        c_t, s_t = mid_tab(p)
        x_re.append(a_re * c_t + a_im * s_t)
        x_im.append(a_im * c_t - a_re * s_t)
    spec_re, spec_im = [], []
    for m in range(n_grp):
        cs = [w8(p, m) for p in range(n_grp)]
        g_re = lin([c for c, _ in cs] + [s for _, s in cs], x_re + x_im)
        g_im = lin([c for c, _ in cs] + [-s for _, s in cs], x_im + x_re)
        c_t, s_t = half_tw(m)
        h_re = g_re * c_t + g_im * s_t
        h_im = g_im * c_t - g_re * s_t
        spec_re.append(halves(h_re))
        spec_im.append(halves(h_im))

    span = pair * devices
    prod_re, prod_im = [], []
    for m in range(n_grp):
        sig_r, cot_r, tap_r = [spec_re[m][z * span : (z + 1) * span] for z in range(n_arr)]
        sig_i, cot_i, tap_i = [spec_im[m][z * span : (z + 1) * span] for z in range(n_arr)]
        prod_re.append(jnp.concatenate(
            [sig_r * tap_r - sig_i * tap_i, cot_r * tap_r + cot_i * tap_i, cot_r * sig_r + cot_i * sig_i]
        ))
        prod_im.append(jnp.concatenate(
            [sig_r * tap_i + sig_i * tap_r, cot_i * tap_r - cot_r * tap_i, cot_i * sig_r - cot_r * sig_i]
        ))

    hh_re, hh_im = [], []
    for m in range(n_grp):
        g_re = halves(prod_re[m])
        g_im = halves(prod_im[m])
        c_t, s_t = half_tw(m)
        hh_re.append(g_re * c_t - g_im * s_t)
        hh_im.append(g_im * c_t + g_re * s_t)
    v_cols_re, v_cols_im = {}, {}
    for p in range(n_grp):
        cs = [w8(p, m) for m in range(n_grp)]
        u_re = lin([c for c, _ in cs] + [-s for _, s in cs], hh_re + hh_im)
        u_im = lin([c for c, _ in cs] + [s for _, s in cs], hh_im + hh_re)
        c_t, s_t = mid_tab(p)
        v_re = u_re * c_t - u_im * s_t
        v_im = u_im * c_t + u_re * s_t
        for idx, (z, k1l) in enumerate(blocks):
            v_cols_re[(k1l, z, p)] = v_re[idx * devices : (idx + 1) * devices]
            v_cols_im[(k1l, z, p)] = v_im[idx * devices : (idx + 1) * devices]
    order = [(k1l, z, p) for k1l in range(pair) for z in range(n_arr) for p in range(n_grp)]
    v_all = jnp.concatenate(
        [
            jnp.concatenate([v_cols_re[key] for key in order], axis=1),
            jnp.concatenate([v_cols_im[key] for key in order], axis=1),
        ],
        axis=0,
    )
    inv_mat = jnp.concatenate(
        [
            jnp.concatenate([q_cos, -q_sin], axis=1),
            jnp.concatenate([q_sin, q_cos], axis=1),
        ],
        axis=0,
    )
    w_all = fft_dot(inv_mat, v_all).reshape(2, devices, pair, n_arr, width)
    b_rows = dev_ids[:, None] * block_w + lane_blk[None, :]
    k1_own = rank_seq * pair + jnp.arange(pair, dtype=jnp.int32)
    ex_ang = (b_rows[:, None, :] * k1_own[None, :, None]) % fft_size
    ex_ang = ex_ang.astype(jnp.float32) * (2.0 * math.pi / fft_size)
    ex_cos = jnp.cos(ex_ang)[:, :, None, :]
    ex_sin = jnp.sin(ex_ang)[:, :, None, :]
    x_re = w_all[0] * ex_cos - w_all[1] * ex_sin
    x_im = w_all[0] * ex_sin + w_all[1] * ex_cos
    back = jnp.stack([x_re, x_im], axis=1)
    back = lax.all_to_all(
        back.astype(jnp.bfloat16), "seq", split_axis=0, concat_axis=0, tiled=True
    ).astype(jnp.float32)

    back = back.reshape(devices, 2, pair, n_arr * width)
    back = jnp.transpose(back, (1, 0, 2, 3)).reshape(2 * rows_all, n_arr * width)
    out_mat = jnp.concatenate([col_cos.T, -col_sin.T], axis=1)
    res = (fft_dot(out_mat, back) * inv_scale).reshape(devices, n_arr, width)

    d_taps = res[:, 2].reshape(devices * block_w, channels)
    d_raw = d_taps * envelope
    d_preact = mat_dot(d_raw, w_out.T) * jnp.cos(preact)
    out_part = mat_dot(hidden.T, d_raw)
    embed_part = mat_dot(features.T, d_preact)
    bias_part = jnp.sum(d_preact, axis=0)
    rank_chan = lax.axis_index("chan")
    n_chan = lax.axis_size("chan")
    out_wide = jnp.zeros((out_part.shape[0], n_chan * channels), jnp.float32)
    out_wide = lax.dynamic_update_slice_in_dim(out_wide, out_part, rank_chan * channels, axis=1)
    flat = jnp.concatenate([out_wide.reshape(-1), embed_part.reshape(-1), bias_part])
    piece = -(-flat.shape[0] // (devices * 128)) * 128
    flat = jnp.pad(flat, (0, devices * piece - flat.shape[0])).reshape(devices, piece)

    outgoing = jnp.concatenate([res[:, 0:2].reshape(devices, 2 * width), flat], axis=1)
    incoming = lax.all_to_all(outgoing, "seq", split_axis=0, concat_axis=0, tiled=True)
    rows_out = incoming[:, : 2 * width].reshape(devices, 2, width).astype(jnp.bfloat16)
    conv_out = rows_out[:, 0].reshape(1, seg_len // 2, 2 * channels)
    d_signal = rows_out[:, 1].reshape(1, seg_len // 2, 2 * channels)
    mine = jnp.sum(incoming[:, 2 * width :], axis=0)

    n_all = devices * n_chan
    total = lax.all_to_all(
        jnp.broadcast_to(mine, (n_all, piece)), ("seq", "chan"), 0, 0, tiled=True
    )
    total = jnp.sum(total.reshape(devices, n_chan, piece), axis=1).reshape(-1)
    n_out = out_wide.size
    n_emb = embed_part.size
    wide_sum = total[:n_out].reshape(out_wide.shape)
    embed_all = total[n_out : n_out + n_emb].reshape(embed_part.shape)
    bias_all = total[n_out + n_emb : n_out + n_emb + bias_part.size]
    out_sum = lax.dynamic_slice_in_dim(wide_sum, rank_chan * channels, channels, axis=1)
    norm_scale = 1.0 / math.sqrt(seq_total)
    return (conv_out, d_signal, embed_all * norm_scale, bias_all * norm_scale, out_sum * norm_scale)


def solution(mesh):
    return jax.shard_map(
        local,
        mesh=mesh,
        in_specs=(
            P("chan", "seq", None),
            P("chan", "seq", None),
            P(),
            P(),
            P(),
            P(None, "chan"),
            P("chan"),
        ),
        out_specs=(P("chan", "seq", None), P("chan", "seq", None), P(), P(), P(None, "chan")),
        check_vma=False,
    )
```

```python
import math

import jax
import jax.numpy as jnp
from jax import lax
from jax.sharding import PartitionSpec as P

exact_mode = lax.Precision.HIGHEST


def mat_dot(lhs_mat, rhs_mat):
    return jnp.dot(lhs_mat, rhs_mat, preferred_element_type=jnp.float32, precision=exact_mode)


def fft_dot(lhs_mat, rhs_mat):
    return jnp.dot(
        lhs_mat, rhs_mat, preferred_element_type=jnp.float32, precision=lax.Precision.HIGH
    )


def band_phase(band_freq, places, seq_total):
    upper_part = places // 1024
    lower_part = places % 1024
    partial_turn = upper_part[:, None] * band_freq[None, :] % seq_total
    wrapped = (partial_turn * 1024 + lower_part[:, None] * band_freq[None, :]) % seq_total
    return wrapped.astype(jnp.float32) * (2.0 * math.pi / seq_total)


def filter_parts(places, band_freq, w_embed, b_embed, w_out, decay, seq_total):
    phases = band_phase(band_freq, places, seq_total)
    features = jnp.concatenate([jnp.cos(phases), jnp.sin(phases)], axis=1)
    preact = mat_dot(features, w_embed) + b_embed[None, :]
    hidden = jnp.sin(preact)
    fraction = places.astype(jnp.float32) / seq_total
    envelope = (
        jnp.exp(-decay[None, :] * fraction[:, None]) * jnp.sqrt((1.0 + decay) / seq_total)[None, :]
    )
    taps = mat_dot(hidden, w_out) * envelope
    return (features, preact, hidden, taps, envelope)


def angle_table(rows_idx, cols_idx, modulus):
    wrapped = rows_idx[:, None] * cols_idx[None, :] % modulus
    angles = wrapped.astype(jnp.float32) * (2.0 * math.pi / modulus)
    return (jnp.cos(angles), jnp.sin(angles))


def local(signal, cotangent, band_freq, w_embed, b_embed, w_out, decay):
    devices = lax.axis_size("seq")
    rank_seq = lax.axis_index("seq")
    seg_len = signal.shape[1] * 2
    channels = signal.shape[2] // 2
    block_w = seg_len // devices
    width = block_w * channels
    rows_all = 2 * devices
    pair = rows_all // devices
    seq_total = seg_len * devices
    fft_size = 2 * seq_total
    inv_scale = 1.0 / fft_size
    n_arr = 3

    dev_ids = jnp.arange(devices, dtype=jnp.int32)
    row_ids = jnp.arange(rows_all, dtype=jnp.int32)
    blk_ids = jnp.arange(block_w, dtype=jnp.int32)
    lane_blk = jnp.arange(width, dtype=jnp.int32) // channels
    b_lane = rank_seq * block_w + lane_blk

    src = jnp.stack(
        [signal.reshape(devices, width), cotangent.reshape(devices, width)], axis=1
    )
    cols = lax.all_to_all(src, "seq", split_axis=0, concat_axis=0, tiled=True)

    places = (
        dev_ids[:, None] * seg_len + rank_seq * block_w + blk_ids[None, :]
    ).reshape(-1)
    features, preact, hidden, taps, envelope = filter_parts(
        places, band_freq, w_embed, b_embed, w_out, decay, seq_total
    )
    stacked = jnp.concatenate(
        [cols.astype(jnp.float32), taps.reshape(devices, 1, width)], axis=1
    ).reshape(devices, n_arr * width)

    col_cos, col_sin = angle_table(row_ids, dev_ids, rows_all)
    y_re = fft_dot(col_cos, stacked).reshape(rows_all, n_arr, width)
    y_im = -fft_dot(col_sin, stacked).reshape(rows_all, n_arr, width)
    tw_cos, tw_sin = angle_table(row_ids, b_lane, fft_size)
    tw_cos = tw_cos[:, None, :]
    tw_sin = tw_sin[:, None, :]
    t_re = y_re * tw_cos + y_im * tw_sin
    t_im = y_im * tw_cos - y_re * tw_sin
    spec = jnp.stack([t_re, t_im], axis=1)
    spec = lax.all_to_all(
        spec.astype(jnp.bfloat16), "seq", split_axis=0, concat_axis=0, tiled=True
    ).astype(jnp.float32)

    q_cos, q_sin = angle_table(dev_ids, dev_ids, devices)
    stage_a = fft_dot(jnp.concatenate([q_cos, q_sin], axis=0), spec.reshape(devices, -1))
    lanes = 2 * channels
    n_grp = width // lanes
    blocks = [(z, k1l) for z in range(n_arr) for k1l in range(pair)]
    n_blk = len(blocks)
    lane_h = jnp.arange(lanes, dtype=jnp.int32) // channels
    flip = jnp.where(lane_h == 0, 1.0, -1.0).astype(jnp.float32)

    def col(k1l, ri, z, p):
        return ((k1l * 2 + ri) * n_arr + z) * width + p * lanes

    def rows_of(part, ri, p):
        return jnp.concatenate(
            [part[:, col(k1l, ri, z, p) : col(k1l, ri, z, p) + lanes] for z, k1l in blocks], axis=0
        )

    def mid_tab(p):
        c_t, s_t = angle_table(dev_ids, 2 * p + lane_h, seg_len)
        c_t = jnp.broadcast_to(c_t[None], (n_blk, devices, lanes)).reshape(n_blk * devices, lanes)
        s_t = jnp.broadcast_to(s_t[None], (n_blk, devices, lanes)).reshape(n_blk * devices, lanes)
        return c_t, s_t

    def lin(coefs, vals):
        acc = None
        for w, v in zip(coefs, vals):
            if abs(w) < 1e-12:
                continue
            term = v if w == 1.0 else (-v if w == -1.0 else v * w)
            acc = term if acc is None else acc + term
        return acc

    def w8(p, m):
        k = (p * m) % n_grp
        return (round(math.cos(2 * math.pi * k / n_grp), 15), round(math.sin(2 * math.pi * k / n_grp), 15))

    def half_tw(m):
        ang = 2 * math.pi * m / (2 * n_grp)
        c_t = jnp.where(lane_h == 1, math.cos(ang), 1.0).astype(jnp.float32)
        s_t = jnp.where(lane_h == 1, math.sin(ang), 0.0).astype(jnp.float32)
        return c_t, s_t

    def halves(x):
        return flip * x + jnp.roll(x, channels, axis=1)

    top = stage_a[:devices]
    bot = stage_a[devices:]
    x_re, x_im = [], []
    for p in range(n_grp):
        a_re = rows_of(top, 0, p) + rows_of(bot, 1, p)
        a_im = rows_of(top, 1, p) - rows_of(bot, 0, p)
        c_t, s_t = mid_tab(p)
        x_re.append(a_re * c_t + a_im * s_t)
        x_im.append(a_im * c_t - a_re * s_t)
    spec_re, spec_im = [], []
    for m in range(n_grp):
        cs = [w8(p, m) for p in range(n_grp)]
        g_re = lin([c for c, _ in cs] + [s for _, s in cs], x_re + x_im)
        g_im = lin([c for c, _ in cs] + [-s for _, s in cs], x_im + x_re)
        c_t, s_t = half_tw(m)
        h_re = g_re * c_t + g_im * s_t
        h_im = g_im * c_t - g_re * s_t
        spec_re.append(halves(h_re))
        spec_im.append(halves(h_im))

    span = pair * devices
    prod_re, prod_im = [], []
    for m in range(n_grp):
        sig_r, cot_r, tap_r = [spec_re[m][z * span : (z + 1) * span] for z in range(n_arr)]
        sig_i, cot_i, tap_i = [spec_im[m][z * span : (z + 1) * span] for z in range(n_arr)]
        prod_re.append(jnp.concatenate(
            [sig_r * tap_r - sig_i * tap_i, cot_r * tap_r + cot_i * tap_i, cot_r * sig_r + cot_i * sig_i]
        ))
        prod_im.append(jnp.concatenate(
            [sig_r * tap_i + sig_i * tap_r, cot_i * tap_r - cot_r * tap_i, cot_i * sig_r - cot_r * sig_i]
        ))

    hh_re, hh_im = [], []
    for m in range(n_grp):
        g_re = halves(prod_re[m])
        g_im = halves(prod_im[m])
        c_t, s_t = half_tw(m)
        hh_re.append(g_re * c_t - g_im * s_t)
        hh_im.append(g_im * c_t + g_re * s_t)
    v_cols_re, v_cols_im = {}, {}
    for p in range(n_grp):
        cs = [w8(p, m) for m in range(n_grp)]
        u_re = lin([c for c, _ in cs] + [-s for _, s in cs], hh_re + hh_im)
        u_im = lin([c for c, _ in cs] + [s for _, s in cs], hh_im + hh_re)
        c_t, s_t = mid_tab(p)
        v_re = u_re * c_t - u_im * s_t
        v_im = u_im * c_t + u_re * s_t
        for idx, (z, k1l) in enumerate(blocks):
            v_cols_re[(k1l, z, p)] = v_re[idx * devices : (idx + 1) * devices]
            v_cols_im[(k1l, z, p)] = v_im[idx * devices : (idx + 1) * devices]
    order = [(k1l, z, p) for k1l in range(pair) for z in range(n_arr) for p in range(n_grp)]
    v_all = jnp.concatenate(
        [
            jnp.concatenate([v_cols_re[key] for key in order], axis=1),
            jnp.concatenate([v_cols_im[key] for key in order], axis=1),
        ],
        axis=0,
    )
    inv_mat = jnp.concatenate(
        [
            jnp.concatenate([q_cos, -q_sin], axis=1),
            jnp.concatenate([q_sin, q_cos], axis=1),
        ],
        axis=0,
    )
    w_all = fft_dot(inv_mat, v_all).reshape(2, devices, pair, n_arr, width)
    b_rows = dev_ids[:, None] * block_w + lane_blk[None, :]
    k1_own = rank_seq * pair + jnp.arange(pair, dtype=jnp.int32)
    ex_ang = (b_rows[:, None, :] * k1_own[None, :, None]) % fft_size
    ex_ang = ex_ang.astype(jnp.float32) * (2.0 * math.pi / fft_size)
    ex_cos = jnp.cos(ex_ang)[:, :, None, :]
    ex_sin = jnp.sin(ex_ang)[:, :, None, :]
    x_re = w_all[0] * ex_cos - w_all[1] * ex_sin
    x_im = w_all[0] * ex_sin + w_all[1] * ex_cos
    back = jnp.stack([x_re, x_im], axis=1)
    back = lax.all_to_all(
        back.astype(jnp.bfloat16), "seq", split_axis=0, concat_axis=0, tiled=True
    ).astype(jnp.float32)

    back = back.reshape(devices, 2, pair, n_arr * width)
    back = jnp.transpose(back, (1, 0, 2, 3)).reshape(2 * rows_all, n_arr * width)
    out_mat = jnp.concatenate([col_cos.T, -col_sin.T], axis=1)
    res = (fft_dot(out_mat, back) * inv_scale).reshape(devices, n_arr, width)

    d_taps = res[:, 2].reshape(devices * block_w, channels)
    d_raw = d_taps * envelope
    d_preact = mat_dot(d_raw, w_out.T) * jnp.cos(preact)
    out_part = mat_dot(hidden.T, d_raw)
    embed_part = mat_dot(features.T, d_preact)
    bias_part = jnp.sum(d_preact, axis=0)
    rank_chan = lax.axis_index("chan")
    n_chan = lax.axis_size("chan")
    out_wide = jnp.zeros((out_part.shape[0], n_chan * channels), jnp.float32)
    out_wide = lax.dynamic_update_slice_in_dim(out_wide, out_part, rank_chan * channels, axis=1)
    flat = jnp.concatenate([out_wide.reshape(-1), embed_part.reshape(-1), bias_part])
    piece = -(-flat.shape[0] // (devices * 128)) * 128
    flat = jnp.pad(flat, (0, devices * piece - flat.shape[0])).reshape(devices, piece)

    outgoing = jnp.concatenate([res[:, 0:2].reshape(devices, 2 * width), flat], axis=1)
    incoming = lax.all_to_all(outgoing, "seq", split_axis=0, concat_axis=0, tiled=True)
    rows_out = incoming[:, : 2 * width].reshape(devices, 2, width).astype(jnp.bfloat16)
    conv_out = rows_out[:, 0].reshape(1, seg_len // 2, 2 * channels)
    d_signal = rows_out[:, 1].reshape(1, seg_len // 2, 2 * channels)
    mine = jnp.sum(incoming[:, 2 * width :], axis=0)

    n_all = devices * n_chan
    total = lax.all_gather(mine, ("seq", "chan"), tiled=True)
    total = jnp.sum(total.reshape(devices, n_chan, piece), axis=1).reshape(-1)
    n_out = out_wide.size
    n_emb = embed_part.size
    wide_sum = total[:n_out].reshape(out_wide.shape)
    embed_all = total[n_out : n_out + n_emb].reshape(embed_part.shape)
    bias_all = total[n_out + n_emb : n_out + n_emb + bias_part.size]
    out_sum = lax.dynamic_slice_in_dim(wide_sum, rank_chan * channels, channels, axis=1)
    norm_scale = 1.0 / math.sqrt(seq_total)
    return (conv_out, d_signal, embed_all * norm_scale, bias_all * norm_scale, out_sum * norm_scale)


def solution(mesh):
    return jax.shard_map(
        local,
        mesh=mesh,
        in_specs=(
            P("chan", "seq", None),
            P("chan", "seq", None),
            P(),
            P(),
            P(),
            P(None, "chan"),
            P("chan"),
        ),
        out_specs=(P("chan", "seq", None), P("chan", "seq", None), P(), P(), P(None, "chan")),
        check_vma=False,
    )
```

```python
import math

import jax
import jax.numpy as jnp
from jax import lax
from jax.sharding import PartitionSpec as P

exact_mode = lax.Precision.HIGHEST


def mat_dot(lhs_mat, rhs_mat):
    return jnp.dot(lhs_mat, rhs_mat, preferred_element_type=jnp.float32, precision=exact_mode)


def fft_dot(lhs_mat, rhs_mat):
    return jnp.dot(
        lhs_mat, rhs_mat, preferred_element_type=jnp.float32, precision=lax.Precision.HIGH
    )


def band_phase(band_freq, places, seq_total):
    upper_part = places // 1024
    lower_part = places % 1024
    partial_turn = upper_part[:, None] * band_freq[None, :] % seq_total
    wrapped = (partial_turn * 1024 + lower_part[:, None] * band_freq[None, :]) % seq_total
    return wrapped.astype(jnp.float32) * (2.0 * math.pi / seq_total)


def filter_parts(places, band_freq, w_embed, b_embed, w_out, decay, seq_total):
    phases = band_phase(band_freq, places, seq_total)
    features = jnp.concatenate([jnp.cos(phases), jnp.sin(phases)], axis=1)
    preact = mat_dot(features, w_embed) + b_embed[None, :]
    hidden = jnp.sin(preact)
    fraction = places.astype(jnp.float32) / seq_total
    envelope = (
        jnp.exp(-decay[None, :] * fraction[:, None]) * jnp.sqrt((1.0 + decay) / seq_total)[None, :]
    )
    taps = mat_dot(hidden, w_out) * envelope
    return (features, preact, hidden, taps, envelope)


def angle_table(rows_idx, cols_idx, modulus):
    wrapped = rows_idx[:, None] * cols_idx[None, :] % modulus
    angles = wrapped.astype(jnp.float32) * (2.0 * math.pi / modulus)
    return (jnp.cos(angles), jnp.sin(angles))


def local(signal, cotangent, band_freq, w_embed, b_embed, w_out, decay):
    devices = lax.axis_size("seq")
    rank_seq = lax.axis_index("seq")
    seg_len = signal.shape[1] * 2
    channels = signal.shape[2] // 2
    block_w = seg_len // devices
    width = block_w * channels
    rows_all = 2 * devices
    pair = rows_all // devices
    seq_total = seg_len * devices
    fft_size = 2 * seq_total
    inv_scale = 1.0 / fft_size
    n_arr = 3

    dev_ids = jnp.arange(devices, dtype=jnp.int32)
    row_ids = jnp.arange(rows_all, dtype=jnp.int32)
    blk_ids = jnp.arange(block_w, dtype=jnp.int32)
    lane_blk = jnp.arange(width, dtype=jnp.int32) // channels
    b_lane = rank_seq * block_w + lane_blk

    src = jnp.stack(
        [signal.reshape(devices, width), cotangent.reshape(devices, width)], axis=1
    )
    cols = lax.all_to_all(src, "seq", split_axis=0, concat_axis=0, tiled=True)

    places = (
        dev_ids[:, None] * seg_len + rank_seq * block_w + blk_ids[None, :]
    ).reshape(-1)
    features, preact, hidden, taps, envelope = filter_parts(
        places, band_freq, w_embed, b_embed, w_out, decay, seq_total
    )
    stacked = jnp.concatenate(
        [cols.astype(jnp.float32), taps.reshape(devices, 1, width)], axis=1
    ).reshape(devices, n_arr * width)

    col_cos, col_sin = angle_table(row_ids, dev_ids, rows_all)
    y_re = fft_dot(col_cos, stacked).reshape(rows_all, n_arr, width)
    y_im = -fft_dot(col_sin, stacked).reshape(rows_all, n_arr, width)
    tw_cos, tw_sin = angle_table(row_ids, b_lane, fft_size)
    tw_cos = tw_cos[:, None, :]
    tw_sin = tw_sin[:, None, :]
    t_re = y_re * tw_cos + y_im * tw_sin
    t_im = y_im * tw_cos - y_re * tw_sin
    spec = jnp.stack([t_re, t_im], axis=1)
    spec = lax.all_to_all(
        spec.astype(jnp.bfloat16), "seq", split_axis=0, concat_axis=0, tiled=True
    ).astype(jnp.float32)

    q_cos, q_sin = angle_table(dev_ids, dev_ids, devices)
    stage_a = fft_dot(jnp.concatenate([q_cos, q_sin], axis=0), spec.reshape(devices, -1))
    lanes = 2 * channels
    n_grp = width // lanes
    blocks = [(z, k1l) for z in range(n_arr) for k1l in range(pair)]
    n_blk = len(blocks)
    lane_h = jnp.arange(lanes, dtype=jnp.int32) // channels
    flip = jnp.where(lane_h == 0, 1.0, -1.0).astype(jnp.float32)

    def col(k1l, ri, z, p):
        return ((k1l * 2 + ri) * n_arr + z) * width + p * lanes

    def rows_of(part, ri, p):
        return jnp.concatenate(
            [part[:, col(k1l, ri, z, p) : col(k1l, ri, z, p) + lanes] for z, k1l in blocks], axis=0
        )

    def mid_tab(p):
        c_t, s_t = angle_table(dev_ids, 2 * p + lane_h, seg_len)
        c_t = jnp.broadcast_to(c_t[None], (n_blk, devices, lanes)).reshape(n_blk * devices, lanes)
        s_t = jnp.broadcast_to(s_t[None], (n_blk, devices, lanes)).reshape(n_blk * devices, lanes)
        return c_t, s_t

    def lin(coefs, vals):
        acc = None
        for w, v in zip(coefs, vals):
            if abs(w) < 1e-12:
                continue
            term = v if w == 1.0 else (-v if w == -1.0 else v * w)
            acc = term if acc is None else acc + term
        return acc

    def w8(p, m):
        k = (p * m) % n_grp
        return (round(math.cos(2 * math.pi * k / n_grp), 15), round(math.sin(2 * math.pi * k / n_grp), 15))

    def half_tw(m):
        ang = 2 * math.pi * m / (2 * n_grp)
        c_t = jnp.where(lane_h == 1, math.cos(ang), 1.0).astype(jnp.float32)
        s_t = jnp.where(lane_h == 1, math.sin(ang), 0.0).astype(jnp.float32)
        return c_t, s_t

    def halves(x):
        return flip * x + jnp.roll(x, channels, axis=1)

    top = stage_a[:devices]
    bot = stage_a[devices:]
    x_re, x_im = [], []
    for p in range(n_grp):
        a_re = rows_of(top, 0, p) + rows_of(bot, 1, p)
        a_im = rows_of(top, 1, p) - rows_of(bot, 0, p)
        c_t, s_t = mid_tab(p)
        x_re.append(a_re * c_t + a_im * s_t)
        x_im.append(a_im * c_t - a_re * s_t)
    spec_re, spec_im = [], []
    for m in range(n_grp):
        cs = [w8(p, m) for p in range(n_grp)]
        g_re = lin([c for c, _ in cs] + [s for _, s in cs], x_re + x_im)
        g_im = lin([c for c, _ in cs] + [-s for _, s in cs], x_im + x_re)
        c_t, s_t = half_tw(m)
        h_re = g_re * c_t + g_im * s_t
        h_im = g_im * c_t - g_re * s_t
        spec_re.append(halves(h_re))
        spec_im.append(halves(h_im))

    span = pair * devices
    prod_re, prod_im = [], []
    for m in range(n_grp):
        sig_r, cot_r, tap_r = [spec_re[m][z * span : (z + 1) * span] for z in range(n_arr)]
        sig_i, cot_i, tap_i = [spec_im[m][z * span : (z + 1) * span] for z in range(n_arr)]
        prod_re.append(jnp.concatenate(
            [sig_r * tap_r - sig_i * tap_i, cot_r * tap_r + cot_i * tap_i, cot_r * sig_r + cot_i * sig_i]
        ))
        prod_im.append(jnp.concatenate(
            [sig_r * tap_i + sig_i * tap_r, cot_i * tap_r - cot_r * tap_i, cot_i * sig_r - cot_r * sig_i]
        ))

    hh_re, hh_im = [], []
    for m in range(n_grp):
        g_re = halves(prod_re[m])
        g_im = halves(prod_im[m])
        c_t, s_t = half_tw(m)
        hh_re.append(g_re * c_t - g_im * s_t)
        hh_im.append(g_im * c_t + g_re * s_t)
    v_cols_re, v_cols_im = {}, {}
    for p in range(n_grp):
        cs = [w8(p, m) for m in range(n_grp)]
        u_re = lin([c for c, _ in cs] + [-s for _, s in cs], hh_re + hh_im)
        u_im = lin([c for c, _ in cs] + [s for _, s in cs], hh_im + hh_re)
        c_t, s_t = mid_tab(p)
        v_re = u_re * c_t - u_im * s_t
        v_im = u_im * c_t + u_re * s_t
        for idx, (z, k1l) in enumerate(blocks):
            v_cols_re[(k1l, z, p)] = v_re[idx * devices : (idx + 1) * devices]
            v_cols_im[(k1l, z, p)] = v_im[idx * devices : (idx + 1) * devices]
    order = [(k1l, z, p) for k1l in range(pair) for z in range(n_arr) for p in range(n_grp)]
    v_all = jnp.concatenate(
        [
            jnp.concatenate([v_cols_re[key] for key in order], axis=1),
            jnp.concatenate([v_cols_im[key] for key in order], axis=1),
        ],
        axis=0,
    )
    inv_mat = jnp.concatenate(
        [
            jnp.concatenate([q_cos, -q_sin], axis=1),
            jnp.concatenate([q_sin, q_cos], axis=1),
        ],
        axis=0,
    )
    w_all = fft_dot(inv_mat, v_all).reshape(2, devices, pair, n_arr, width)
    b_rows = dev_ids[:, None] * block_w + lane_blk[None, :]
    k1_own = rank_seq * pair + jnp.arange(pair, dtype=jnp.int32)
    ex_ang = (b_rows[:, None, :] * k1_own[None, :, None]) % fft_size
    ex_ang = ex_ang.astype(jnp.float32) * (2.0 * math.pi / fft_size)
    ex_cos = jnp.cos(ex_ang)[:, :, None, :]
    ex_sin = jnp.sin(ex_ang)[:, :, None, :]
    x_re = w_all[0] * ex_cos - w_all[1] * ex_sin
    x_im = w_all[0] * ex_sin + w_all[1] * ex_cos
    back = jnp.stack([x_re, x_im], axis=1)
    back = lax.all_to_all(
        back.astype(jnp.bfloat16), "seq", split_axis=0, concat_axis=0, tiled=True
    ).astype(jnp.float32)

    back = back.reshape(devices, 2, pair, n_arr * width)
    back = jnp.transpose(back, (1, 0, 2, 3)).reshape(2 * rows_all, n_arr * width)
    out_mat = jnp.concatenate([col_cos.T, -col_sin.T], axis=1)
    res = (fft_dot(out_mat, back) * inv_scale).reshape(devices, n_arr, width)

    d_taps = res[:, 2].reshape(devices * block_w, channels)
    d_raw = d_taps * envelope
    d_preact = mat_dot(d_raw, w_out.T) * jnp.cos(preact)
    out_part = mat_dot(hidden.T, d_raw)
    embed_part = mat_dot(features.T, d_preact)
    bias_part = jnp.sum(d_preact, axis=0)
    rank_chan = lax.axis_index("chan")
    n_chan = lax.axis_size("chan")
    out_wide = jnp.zeros((out_part.shape[0], n_chan * channels), jnp.float32)
    out_wide = lax.dynamic_update_slice_in_dim(out_wide, out_part, rank_chan * channels, axis=1)
    flat = jnp.concatenate([out_wide.reshape(-1), embed_part.reshape(-1), bias_part])
    piece = -(-flat.shape[0] // (devices * 128)) * 128
    flat = jnp.pad(flat, (0, devices * piece - flat.shape[0])).reshape(devices, piece)

    flat_hi = flat.astype(jnp.bfloat16)
    flat_lo = (flat - flat_hi.astype(jnp.float32)).astype(jnp.bfloat16)
    outgoing = jnp.concatenate(
        [res[:, 0:2].reshape(devices, 2 * width).astype(jnp.bfloat16), flat_hi, flat_lo], axis=1
    )
    incoming = lax.all_to_all(outgoing, "seq", split_axis=0, concat_axis=0, tiled=True)
    rows_out = incoming[:, : 2 * width].reshape(devices, 2, width)
    conv_out = rows_out[:, 0].reshape(1, seg_len // 2, 2 * channels)
    d_signal = rows_out[:, 1].reshape(1, seg_len // 2, 2 * channels)
    got_hi = incoming[:, 2 * width : 2 * width + piece].astype(jnp.float32)
    got_lo = incoming[:, 2 * width + piece :].astype(jnp.float32)
    mine = jnp.sum(got_hi + got_lo, axis=0)

    n_all = devices * n_chan
    total = lax.all_to_all(
        jnp.broadcast_to(mine, (n_all, piece)), ("seq", "chan"), 0, 0, tiled=True
    )
    total = jnp.sum(total.reshape(devices, n_chan, piece), axis=1).reshape(-1)
    n_out = out_wide.size
    n_emb = embed_part.size
    wide_sum = total[:n_out].reshape(out_wide.shape)
    embed_all = total[n_out : n_out + n_emb].reshape(embed_part.shape)
    bias_all = total[n_out + n_emb : n_out + n_emb + bias_part.size]
    out_sum = lax.dynamic_slice_in_dim(wide_sum, rank_chan * channels, channels, axis=1)
    norm_scale = 1.0 / math.sqrt(seq_total)
    return (conv_out, d_signal, embed_all * norm_scale, bias_all * norm_scale, out_sum * norm_scale)


def solution(mesh):
    return jax.shard_map(
        local,
        mesh=mesh,
        in_specs=(
            P("chan", "seq", None),
            P("chan", "seq", None),
            P(),
            P(),
            P(),
            P(None, "chan"),
            P("chan"),
        ),
        out_specs=(P("chan", "seq", None), P("chan", "seq", None), P(), P(), P(None, "chan")),
        check_vma=False,
    )
```

```python
import math

import jax
import jax.numpy as jnp
from jax import lax
from jax.sharding import PartitionSpec as P

exact_mode = lax.Precision.HIGHEST


def mat_dot(lhs_mat, rhs_mat):
    return jnp.dot(lhs_mat, rhs_mat, preferred_element_type=jnp.float32, precision=exact_mode)


def fft_dot(lhs_mat, rhs_mat):
    return jnp.dot(
        lhs_mat, rhs_mat, preferred_element_type=jnp.float32, precision=lax.Precision.HIGH
    )


def band_phase(band_freq, places, seq_total):
    upper_part = places // 1024
    lower_part = places % 1024
    partial_turn = upper_part[:, None] * band_freq[None, :] % seq_total
    wrapped = (partial_turn * 1024 + lower_part[:, None] * band_freq[None, :]) % seq_total
    return wrapped.astype(jnp.float32) * (2.0 * math.pi / seq_total)


def filter_parts(places, band_freq, w_embed, b_embed, w_out, decay, seq_total):
    phases = band_phase(band_freq, places, seq_total)
    features = jnp.concatenate([jnp.cos(phases), jnp.sin(phases)], axis=1)
    preact = mat_dot(features, w_embed) + b_embed[None, :]
    hidden = jnp.sin(preact)
    fraction = places.astype(jnp.float32) / seq_total
    envelope = (
        jnp.exp(-decay[None, :] * fraction[:, None]) * jnp.sqrt((1.0 + decay) / seq_total)[None, :]
    )
    taps = mat_dot(hidden, w_out) * envelope
    return (features, preact, hidden, taps, envelope)


def angle_table(rows_idx, cols_idx, modulus):
    wrapped = rows_idx[:, None] * cols_idx[None, :] % modulus
    angles = wrapped.astype(jnp.float32) * (2.0 * math.pi / modulus)
    return (jnp.cos(angles), jnp.sin(angles))


def local(signal, cotangent, band_freq, w_embed, b_embed, w_out, decay):
    devices = lax.axis_size("seq")
    rank_seq = lax.axis_index("seq")
    seg_len = signal.shape[1] * 2
    channels = signal.shape[2] // 2
    block_w = seg_len // devices
    width = block_w * channels
    rows_all = 2 * devices
    pair = rows_all // devices
    seq_total = seg_len * devices
    fft_size = 2 * seq_total
    inv_scale = 1.0 / fft_size
    n_arr = 3

    dev_ids = jnp.arange(devices, dtype=jnp.int32)
    row_ids = jnp.arange(rows_all, dtype=jnp.int32)
    blk_ids = jnp.arange(block_w, dtype=jnp.int32)
    lane_blk = jnp.arange(width, dtype=jnp.int32) // channels
    b_lane = rank_seq * block_w + lane_blk

    src = jnp.stack(
        [signal.reshape(devices, width), cotangent.reshape(devices, width)], axis=1
    )
    cols = lax.all_to_all(src, "seq", split_axis=0, concat_axis=0, tiled=True)

    places = (
        dev_ids[:, None] * seg_len + rank_seq * block_w + blk_ids[None, :]
    ).reshape(-1)
    features, preact, hidden, taps, envelope = filter_parts(
        places, band_freq, w_embed, b_embed, w_out, decay, seq_total
    )
    stacked = jnp.concatenate(
        [cols.astype(jnp.float32), taps.reshape(devices, 1, width)], axis=1
    ).reshape(devices, n_arr * width)

    col_cos, col_sin = angle_table(row_ids, dev_ids, rows_all)
    y_re = fft_dot(col_cos, stacked).reshape(rows_all, n_arr, width)
    y_im = -fft_dot(col_sin, stacked).reshape(rows_all, n_arr, width)
    tw_cos, tw_sin = angle_table(row_ids, b_lane, fft_size)
    tw_cos = tw_cos[:, None, :]
    tw_sin = tw_sin[:, None, :]
    t_re = y_re * tw_cos + y_im * tw_sin
    t_im = y_im * tw_cos - y_re * tw_sin
    spec = jnp.stack([t_re, t_im], axis=1)
    spec = lax.all_to_all(
        spec.astype(jnp.bfloat16), "seq", split_axis=0, concat_axis=0, tiled=True
    ).astype(jnp.float32)

    q_cos, q_sin = angle_table(dev_ids, dev_ids, devices)
    stage_a = fft_dot(jnp.concatenate([q_cos, q_sin], axis=0), spec.reshape(devices, -1))
    lanes = 2 * channels
    n_grp = width // lanes
    blocks = [(z, k1l) for z in range(n_arr) for k1l in range(pair)]
    n_blk = len(blocks)
    lane_h = jnp.arange(lanes, dtype=jnp.int32) // channels
    flip = jnp.where(lane_h == 0, 1.0, -1.0).astype(jnp.float32)

    def col(k1l, ri, z, p):
        return ((k1l * 2 + ri) * n_arr + z) * width + p * lanes

    def rows_of(part, ri, p):
        return jnp.concatenate(
            [part[:, col(k1l, ri, z, p) : col(k1l, ri, z, p) + lanes] for z, k1l in blocks], axis=0
        )

    def mid_tab(p, count):
        c_t, s_t = angle_table(dev_ids, 2 * p + lane_h, seg_len)
        c_t = jnp.broadcast_to(c_t[None], (count, devices, lanes)).reshape(count * devices, lanes)
        s_t = jnp.broadcast_to(s_t[None], (count, devices, lanes)).reshape(count * devices, lanes)
        return c_t, s_t

    def lin(coefs, vals):
        acc = None
        for w, v in zip(coefs, vals):
            if abs(w) < 1e-12:
                continue
            term = v if w == 1.0 else (-v if w == -1.0 else v * w)
            acc = term if acc is None else acc + term
        return acc

    def w8(p, m):
        k = (p * m) % n_grp
        return (round(math.cos(2 * math.pi * k / n_grp), 15), round(math.sin(2 * math.pi * k / n_grp), 15))

    def half_tw(m):
        ang = 2 * math.pi * m / (2 * n_grp)
        c_t = jnp.where(lane_h == 1, math.cos(ang), 1.0).astype(jnp.float32)
        s_t = jnp.where(lane_h == 1, math.sin(ang), 0.0).astype(jnp.float32)
        return c_t, s_t

    def halves(x):
        return flip * x + jnp.roll(x, channels, axis=1)

    top = stage_a[:devices]
    bot = stage_a[devices:]
    x_re, x_im = [], []
    for p in range(n_grp):
        a_re = rows_of(top, 0, p) + rows_of(bot, 1, p)
        a_im = rows_of(top, 1, p) - rows_of(bot, 0, p)
        c_t, s_t = mid_tab(p, n_blk)
        x_re.append(a_re * c_t + a_im * s_t)
        x_im.append(a_im * c_t - a_re * s_t)
    spec_re, spec_im = [], []
    for m in range(n_grp):
        cs = [w8(p, m) for p in range(n_grp)]
        g_re = lin([c for c, _ in cs] + [s for _, s in cs], x_re + x_im)
        g_im = lin([c for c, _ in cs] + [-s for _, s in cs], x_im + x_re)
        c_t, s_t = half_tw(m)
        h_re = g_re * c_t + g_im * s_t
        h_im = g_im * c_t - g_re * s_t
        spec_re.append(halves(h_re))
        spec_im.append(halves(h_im))

    span = pair * devices
    prod_re, prod_im = [], []
    for m in range(n_grp):
        sig_r, cot_r, tap_r = [spec_re[m][z * span : (z + 1) * span] for z in range(n_arr)]
        sig_i, cot_i, tap_i = [spec_im[m][z * span : (z + 1) * span] for z in range(n_arr)]
        prod_re.append(jnp.concatenate(
            [sig_r * tap_r - sig_i * tap_i, cot_r * tap_r + cot_i * tap_i, cot_r * sig_r + cot_i * sig_i]
        ))
        prod_im.append(jnp.concatenate(
            [sig_r * tap_i + sig_i * tap_r, cot_i * tap_r - cot_r * tap_i, cot_i * sig_r - cot_r * sig_i]
        ))

    inv_mat = jnp.concatenate(
        [
            jnp.concatenate([q_cos, -q_sin], axis=1),
            jnp.concatenate([q_sin, q_cos], axis=1),
        ],
        axis=0,
    )
    b_rows = dev_ids[:, None] * block_w + lane_blk[None, :]
    k1_own = rank_seq * pair + jnp.arange(pair, dtype=jnp.int32)
    ex_ang = (b_rows[:, None, :] * k1_own[None, :, None]) % fft_size
    ex_ang = ex_ang.astype(jnp.float32) * (2.0 * math.pi / fft_size)
    ex_cos = jnp.cos(ex_ang)[:, :, None, :]
    ex_sin = jnp.sin(ex_ang)[:, :, None, :]
    out_mat = jnp.concatenate([col_cos.T, -col_sin.T], axis=1)

    def inverse_part(z_list):
        n_out = len(z_list)
        blocks_out = [(zi, k1l) for zi in range(n_out) for k1l in range(pair)]
        hh_re, hh_im = [], []
        for m in range(n_grp):
            pr = jnp.concatenate([prod_re[m][z * span : (z + 1) * span] for z in z_list])
            pi = jnp.concatenate([prod_im[m][z * span : (z + 1) * span] for z in z_list])
            g_re = halves(pr)
            g_im = halves(pi)
            c_t, s_t = half_tw(m)
            hh_re.append(g_re * c_t - g_im * s_t)
            hh_im.append(g_im * c_t + g_re * s_t)
        v_cols_re, v_cols_im = {}, {}
        for p in range(n_grp):
            cs = [w8(p, m) for m in range(n_grp)]
            u_re = lin([c for c, _ in cs] + [-s for _, s in cs], hh_re + hh_im)
            u_im = lin([c for c, _ in cs] + [s for _, s in cs], hh_im + hh_re)
            c_t, s_t = mid_tab(p, len(blocks_out))
            v_re = u_re * c_t - u_im * s_t
            v_im = u_im * c_t + u_re * s_t
            for idx, (zi, k1l) in enumerate(blocks_out):
                v_cols_re[(k1l, zi, p)] = v_re[idx * devices : (idx + 1) * devices]
                v_cols_im[(k1l, zi, p)] = v_im[idx * devices : (idx + 1) * devices]
        order = [(k1l, zi, p) for k1l in range(pair) for zi in range(n_out) for p in range(n_grp)]
        v_all = jnp.concatenate(
            [
                jnp.concatenate([v_cols_re[key] for key in order], axis=1),
                jnp.concatenate([v_cols_im[key] for key in order], axis=1),
            ],
            axis=0,
        )
        w_all = fft_dot(inv_mat, v_all).reshape(2, devices, pair, n_out, width)
        x_re = w_all[0] * ex_cos - w_all[1] * ex_sin
        x_im = w_all[0] * ex_sin + w_all[1] * ex_cos
        back = jnp.stack([x_re, x_im], axis=1)
        back = lax.all_to_all(
            back.astype(jnp.bfloat16), "seq", split_axis=0, concat_axis=0, tiled=True
        ).astype(jnp.float32)
        back = back.reshape(devices, 2, pair, n_out * width)
        back = jnp.transpose(back, (1, 0, 2, 3)).reshape(2 * rows_all, n_out * width)
        return (fft_dot(out_mat, back) * inv_scale).reshape(devices, n_out, width)

    res_taps = inverse_part([2])
    res_rows = inverse_part([0, 1])

    d_taps = res_taps[:, 0].reshape(devices * block_w, channels)
    d_raw = d_taps * envelope
    d_preact = mat_dot(d_raw, w_out.T) * jnp.cos(preact)
    out_part = mat_dot(hidden.T, d_raw)
    embed_part = mat_dot(features.T, d_preact)
    bias_part = jnp.sum(d_preact, axis=0)
    rank_chan = lax.axis_index("chan")
    n_chan = lax.axis_size("chan")
    out_wide = jnp.zeros((out_part.shape[0], n_chan * channels), jnp.float32)
    out_wide = lax.dynamic_update_slice_in_dim(out_wide, out_part, rank_chan * channels, axis=1)
    flat = jnp.concatenate([out_wide.reshape(-1), embed_part.reshape(-1), bias_part])
    piece = -(-flat.shape[0] // (devices * 128)) * 128
    flat = jnp.pad(flat, (0, devices * piece - flat.shape[0])).reshape(devices, piece)

    flat_hi = flat.astype(jnp.bfloat16)
    flat_lo = (flat - flat_hi.astype(jnp.float32)).astype(jnp.bfloat16)
    outgoing = jnp.concatenate(
        [res_rows.reshape(devices, 2 * width).astype(jnp.bfloat16), flat_hi, flat_lo], axis=1
    )
    incoming = lax.all_to_all(outgoing, "seq", split_axis=0, concat_axis=0, tiled=True)
    rows_out = incoming[:, : 2 * width].reshape(devices, 2, width)
    conv_out = rows_out[:, 0].reshape(1, seg_len // 2, 2 * channels)
    d_signal = rows_out[:, 1].reshape(1, seg_len // 2, 2 * channels)
    got_hi = incoming[:, 2 * width : 2 * width + piece].astype(jnp.float32)
    got_lo = incoming[:, 2 * width + piece :].astype(jnp.float32)
    mine = jnp.sum(got_hi + got_lo, axis=0)

    n_all = devices * n_chan
    total = lax.all_to_all(
        jnp.broadcast_to(mine, (n_all, piece)), ("seq", "chan"), 0, 0, tiled=True
    )
    total = jnp.sum(total.reshape(devices, n_chan, piece), axis=1).reshape(-1)
    n_out = out_wide.size
    n_emb = embed_part.size
    wide_sum = total[:n_out].reshape(out_wide.shape)
    embed_all = total[n_out : n_out + n_emb].reshape(embed_part.shape)
    bias_all = total[n_out + n_emb : n_out + n_emb + bias_part.size]
    out_sum = lax.dynamic_slice_in_dim(wide_sum, rank_chan * channels, channels, axis=1)
    norm_scale = 1.0 / math.sqrt(seq_total)
    return (conv_out, d_signal, embed_all * norm_scale, bias_all * norm_scale, out_sum * norm_scale)


def solution(mesh):
    return jax.shard_map(
        local,
        mesh=mesh,
        in_specs=(
            P("chan", "seq", None),
            P("chan", "seq", None),
            P(),
            P(),
            P(),
            P(None, "chan"),
            P("chan"),
        ),
        out_specs=(P("chan", "seq", None), P("chan", "seq", None), P(), P(), P(None, "chan")),
        check_vma=False,
    )
```

```python
import math

import jax
import jax.numpy as jnp
from jax import lax
from jax.sharding import PartitionSpec as P

exact_mode = lax.Precision.HIGHEST


def mat_dot(lhs_mat, rhs_mat):
    return jnp.dot(lhs_mat, rhs_mat, preferred_element_type=jnp.float32, precision=exact_mode)


def fft_dot(lhs_mat, rhs_mat):
    return jnp.dot(
        lhs_mat, rhs_mat, preferred_element_type=jnp.float32, precision=lax.Precision.HIGH
    )


def band_phase(band_freq, places, seq_total):
    upper_part = places // 1024
    lower_part = places % 1024
    partial_turn = upper_part[:, None] * band_freq[None, :] % seq_total
    wrapped = (partial_turn * 1024 + lower_part[:, None] * band_freq[None, :]) % seq_total
    return wrapped.astype(jnp.float32) * (2.0 * math.pi / seq_total)


def filter_parts(places, band_freq, w_embed, b_embed, w_out, decay, seq_total):
    phases = band_phase(band_freq, places, seq_total)
    features = jnp.concatenate([jnp.cos(phases), jnp.sin(phases)], axis=1)
    preact = mat_dot(features, w_embed) + b_embed[None, :]
    hidden = jnp.sin(preact)
    fraction = places.astype(jnp.float32) / seq_total
    envelope = (
        jnp.exp(-decay[None, :] * fraction[:, None]) * jnp.sqrt((1.0 + decay) / seq_total)[None, :]
    )
    taps = mat_dot(hidden, w_out) * envelope
    return (features, preact, hidden, taps, envelope)


def angle_table(rows_idx, cols_idx, modulus):
    wrapped = rows_idx[:, None] * cols_idx[None, :] % modulus
    angles = wrapped.astype(jnp.float32) * (2.0 * math.pi / modulus)
    return (jnp.cos(angles), jnp.sin(angles))


def local(signal, cotangent, band_freq, w_embed, b_embed, w_out, decay):
    devices = lax.axis_size("seq")
    rank_seq = lax.axis_index("seq")
    seg_len = signal.shape[1] * 2
    channels = signal.shape[2] // 2
    block_w = seg_len // devices
    width = block_w * channels
    rows_all = 2 * devices
    pair = rows_all // devices
    seq_total = seg_len * devices
    fft_size = 2 * seq_total
    inv_scale = 1.0 / fft_size
    n_arr = 3

    dev_ids = jnp.arange(devices, dtype=jnp.int32)
    row_ids = jnp.arange(rows_all, dtype=jnp.int32)
    blk_ids = jnp.arange(block_w, dtype=jnp.int32)
    lane_blk = jnp.arange(width, dtype=jnp.int32) // channels
    b_lane = rank_seq * block_w + lane_blk

    src = jnp.stack(
        [signal.reshape(devices, width), cotangent.reshape(devices, width)], axis=1
    )
    cols = lax.all_to_all(src, "seq", split_axis=0, concat_axis=0, tiled=True)

    places = (
        dev_ids[:, None] * seg_len + rank_seq * block_w + blk_ids[None, :]
    ).reshape(-1)
    features, preact, hidden, taps, envelope = filter_parts(
        places, band_freq, w_embed, b_embed, w_out, decay, seq_total
    )
    col_cos, col_sin = angle_table(row_ids, dev_ids, rows_all)
    tw_cos, tw_sin = angle_table(row_ids, b_lane, fft_size)
    tw_cos = tw_cos[:, None, :]
    tw_sin = tw_sin[:, None, :]

    def column_send(vals):
        n_z = vals.shape[1]
        flat_v = vals.reshape(devices, n_z * width)
        y_re = fft_dot(col_cos, flat_v).reshape(rows_all, n_z, width)
        y_im = -fft_dot(col_sin, flat_v).reshape(rows_all, n_z, width)
        t_re = y_re * tw_cos + y_im * tw_sin
        t_im = y_im * tw_cos - y_re * tw_sin
        sent = jnp.stack([t_re, t_im], axis=1).astype(jnp.bfloat16)
        return lax.all_to_all(sent, "seq", split_axis=0, concat_axis=0, tiled=True)

    spec_sc = column_send(cols.astype(jnp.float32))
    spec_tp = column_send(taps.reshape(devices, 1, width))
    spec = jnp.concatenate([spec_sc, spec_tp], axis=2).astype(jnp.float32)

    q_cos, q_sin = angle_table(dev_ids, dev_ids, devices)
    stage_a = fft_dot(jnp.concatenate([q_cos, q_sin], axis=0), spec.reshape(devices, -1))
    lanes = 2 * channels
    n_grp = width // lanes
    blocks = [(z, k1l) for z in range(n_arr) for k1l in range(pair)]
    n_blk = len(blocks)
    lane_h = jnp.arange(lanes, dtype=jnp.int32) // channels
    flip = jnp.where(lane_h == 0, 1.0, -1.0).astype(jnp.float32)

    def col(k1l, ri, z, p):
        return ((k1l * 2 + ri) * n_arr + z) * width + p * lanes

    def rows_of(part, ri, p):
        return jnp.concatenate(
            [part[:, col(k1l, ri, z, p) : col(k1l, ri, z, p) + lanes] for z, k1l in blocks], axis=0
        )

    def mid_tab(p, count):
        c_t, s_t = angle_table(dev_ids, 2 * p + lane_h, seg_len)
        c_t = jnp.broadcast_to(c_t[None], (count, devices, lanes)).reshape(count * devices, lanes)
        s_t = jnp.broadcast_to(s_t[None], (count, devices, lanes)).reshape(count * devices, lanes)
        return c_t, s_t

    def lin(coefs, vals):
        acc = None
        for w, v in zip(coefs, vals):
            if abs(w) < 1e-12:
                continue
            term = v if w == 1.0 else (-v if w == -1.0 else v * w)
            acc = term if acc is None else acc + term
        return acc

    def w8(p, m):
        k = (p * m) % n_grp
        return (round(math.cos(2 * math.pi * k / n_grp), 15), round(math.sin(2 * math.pi * k / n_grp), 15))

    def half_tw(m):
        ang = 2 * math.pi * m / (2 * n_grp)
        c_t = jnp.where(lane_h == 1, math.cos(ang), 1.0).astype(jnp.float32)
        s_t = jnp.where(lane_h == 1, math.sin(ang), 0.0).astype(jnp.float32)
        return c_t, s_t

    def halves(x):
        return flip * x + jnp.roll(x, channels, axis=1)

    top = stage_a[:devices]
    bot = stage_a[devices:]
    x_re, x_im = [], []
    for p in range(n_grp):
        a_re = rows_of(top, 0, p) + rows_of(bot, 1, p)
        a_im = rows_of(top, 1, p) - rows_of(bot, 0, p)
        c_t, s_t = mid_tab(p, n_blk)
        x_re.append(a_re * c_t + a_im * s_t)
        x_im.append(a_im * c_t - a_re * s_t)
    spec_re, spec_im = [], []
    for m in range(n_grp):
        cs = [w8(p, m) for p in range(n_grp)]
        g_re = lin([c for c, _ in cs] + [s for _, s in cs], x_re + x_im)
        g_im = lin([c for c, _ in cs] + [-s for _, s in cs], x_im + x_re)
        c_t, s_t = half_tw(m)
        h_re = g_re * c_t + g_im * s_t
        h_im = g_im * c_t - g_re * s_t
        spec_re.append(halves(h_re))
        spec_im.append(halves(h_im))

    span = pair * devices
    prod_re, prod_im = [], []
    for m in range(n_grp):
        sig_r, cot_r, tap_r = [spec_re[m][z * span : (z + 1) * span] for z in range(n_arr)]
        sig_i, cot_i, tap_i = [spec_im[m][z * span : (z + 1) * span] for z in range(n_arr)]
        prod_re.append(jnp.concatenate(
            [sig_r * tap_r - sig_i * tap_i, cot_r * tap_r + cot_i * tap_i, cot_r * sig_r + cot_i * sig_i]
        ))
        prod_im.append(jnp.concatenate(
            [sig_r * tap_i + sig_i * tap_r, cot_i * tap_r - cot_r * tap_i, cot_i * sig_r - cot_r * sig_i]
        ))

    inv_mat = jnp.concatenate(
        [
            jnp.concatenate([q_cos, -q_sin], axis=1),
            jnp.concatenate([q_sin, q_cos], axis=1),
        ],
        axis=0,
    )
    b_rows = dev_ids[:, None] * block_w + lane_blk[None, :]
    k1_own = rank_seq * pair + jnp.arange(pair, dtype=jnp.int32)
    ex_ang = (b_rows[:, None, :] * k1_own[None, :, None]) % fft_size
    ex_ang = ex_ang.astype(jnp.float32) * (2.0 * math.pi / fft_size)
    ex_cos = jnp.cos(ex_ang)[:, :, None, :]
    ex_sin = jnp.sin(ex_ang)[:, :, None, :]
    out_mat = jnp.concatenate([col_cos.T, -col_sin.T], axis=1)

    def inverse_part(z_list):
        n_out = len(z_list)
        blocks_out = [(zi, k1l) for zi in range(n_out) for k1l in range(pair)]
        hh_re, hh_im = [], []
        for m in range(n_grp):
            pr = jnp.concatenate([prod_re[m][z * span : (z + 1) * span] for z in z_list])
            pi = jnp.concatenate([prod_im[m][z * span : (z + 1) * span] for z in z_list])
            g_re = halves(pr)
            g_im = halves(pi)
            c_t, s_t = half_tw(m)
            hh_re.append(g_re * c_t - g_im * s_t)
            hh_im.append(g_im * c_t + g_re * s_t)
        v_cols_re, v_cols_im = {}, {}
        for p in range(n_grp):
            cs = [w8(p, m) for m in range(n_grp)]
            u_re = lin([c for c, _ in cs] + [-s for _, s in cs], hh_re + hh_im)
            u_im = lin([c for c, _ in cs] + [s for _, s in cs], hh_im + hh_re)
            c_t, s_t = mid_tab(p, len(blocks_out))
            v_re = u_re * c_t - u_im * s_t
            v_im = u_im * c_t + u_re * s_t
            for idx, (zi, k1l) in enumerate(blocks_out):
                v_cols_re[(k1l, zi, p)] = v_re[idx * devices : (idx + 1) * devices]
                v_cols_im[(k1l, zi, p)] = v_im[idx * devices : (idx + 1) * devices]
        order = [(k1l, zi, p) for k1l in range(pair) for zi in range(n_out) for p in range(n_grp)]
        v_all = jnp.concatenate(
            [
                jnp.concatenate([v_cols_re[key] for key in order], axis=1),
                jnp.concatenate([v_cols_im[key] for key in order], axis=1),
            ],
            axis=0,
        )
        w_all = fft_dot(inv_mat, v_all).reshape(2, devices, pair, n_out, width)
        x_re = w_all[0] * ex_cos - w_all[1] * ex_sin
        x_im = w_all[0] * ex_sin + w_all[1] * ex_cos
        back = jnp.stack([x_re, x_im], axis=1)
        back = lax.all_to_all(
            back.astype(jnp.bfloat16), "seq", split_axis=0, concat_axis=0, tiled=True
        ).astype(jnp.float32)
        back = back.reshape(devices, 2, pair, n_out * width)
        back = jnp.transpose(back, (1, 0, 2, 3)).reshape(2 * rows_all, n_out * width)
        return (fft_dot(out_mat, back) * inv_scale).reshape(devices, n_out, width)

    res_taps = inverse_part([2])
    res_rows = inverse_part([0, 1])

    d_taps = res_taps[:, 0].reshape(devices * block_w, channels)
    d_raw = d_taps * envelope
    d_preact = mat_dot(d_raw, w_out.T) * jnp.cos(preact)
    out_part = mat_dot(hidden.T, d_raw)
    embed_part = mat_dot(features.T, d_preact)
    bias_part = jnp.sum(d_preact, axis=0)
    rank_chan = lax.axis_index("chan")
    n_chan = lax.axis_size("chan")
    out_wide = jnp.zeros((out_part.shape[0], n_chan * channels), jnp.float32)
    out_wide = lax.dynamic_update_slice_in_dim(out_wide, out_part, rank_chan * channels, axis=1)
    flat = jnp.concatenate([out_wide.reshape(-1), embed_part.reshape(-1), bias_part])
    piece = -(-flat.shape[0] // (devices * 128)) * 128
    flat = jnp.pad(flat, (0, devices * piece - flat.shape[0])).reshape(devices, piece)

    flat_hi = flat.astype(jnp.bfloat16)
    flat_lo = (flat - flat_hi.astype(jnp.float32)).astype(jnp.bfloat16)
    outgoing = jnp.concatenate(
        [res_rows.reshape(devices, 2 * width).astype(jnp.bfloat16), flat_hi, flat_lo], axis=1
    )
    incoming = lax.all_to_all(outgoing, "seq", split_axis=0, concat_axis=0, tiled=True)
    rows_out = incoming[:, : 2 * width].reshape(devices, 2, width)
    conv_out = rows_out[:, 0].reshape(1, seg_len // 2, 2 * channels)
    d_signal = rows_out[:, 1].reshape(1, seg_len // 2, 2 * channels)
    got_hi = incoming[:, 2 * width : 2 * width + piece].astype(jnp.float32)
    got_lo = incoming[:, 2 * width + piece :].astype(jnp.float32)
    mine = jnp.sum(got_hi + got_lo, axis=0)

    n_all = devices * n_chan
    total = lax.all_to_all(
        jnp.broadcast_to(mine, (n_all, piece)), ("seq", "chan"), 0, 0, tiled=True
    )
    total = jnp.sum(total.reshape(devices, n_chan, piece), axis=1).reshape(-1)
    n_out = out_wide.size
    n_emb = embed_part.size
    wide_sum = total[:n_out].reshape(out_wide.shape)
    embed_all = total[n_out : n_out + n_emb].reshape(embed_part.shape)
    bias_all = total[n_out + n_emb : n_out + n_emb + bias_part.size]
    out_sum = lax.dynamic_slice_in_dim(wide_sum, rank_chan * channels, channels, axis=1)
    norm_scale = 1.0 / math.sqrt(seq_total)
    return (conv_out, d_signal, embed_all * norm_scale, bias_all * norm_scale, out_sum * norm_scale)


def solution(mesh):
    return jax.shard_map(
        local,
        mesh=mesh,
        in_specs=(
            P("chan", "seq", None),
            P("chan", "seq", None),
            P(),
            P(),
            P(),
            P(None, "chan"),
            P("chan"),
        ),
        out_specs=(P("chan", "seq", None), P("chan", "seq", None), P(), P(), P(None, "chan")),
        check_vma=False,
    )
```

```python
import math

import jax
import jax.numpy as jnp
from jax import lax
from jax.sharding import PartitionSpec as P

exact_mode = lax.Precision.HIGHEST


def mat_dot(lhs_mat, rhs_mat):
    return jnp.dot(lhs_mat, rhs_mat, preferred_element_type=jnp.float32, precision=exact_mode)


def fft_dot(lhs_mat, rhs_mat):
    return jnp.dot(
        lhs_mat, rhs_mat, preferred_element_type=jnp.float32, precision=lax.Precision.HIGH
    )


def band_phase(band_freq, places, seq_total):
    upper_part = places // 1024
    lower_part = places % 1024
    partial_turn = upper_part[:, None] * band_freq[None, :] % seq_total
    wrapped = (partial_turn * 1024 + lower_part[:, None] * band_freq[None, :]) % seq_total
    return wrapped.astype(jnp.float32) * (2.0 * math.pi / seq_total)


def filter_parts(places, band_freq, w_embed, b_embed, w_out, decay, seq_total):
    phases = band_phase(band_freq, places, seq_total)
    features = jnp.concatenate([jnp.cos(phases), jnp.sin(phases)], axis=1)
    preact = mat_dot(features, w_embed) + b_embed[None, :]
    hidden = jnp.sin(preact)
    fraction = places.astype(jnp.float32) / seq_total
    envelope = (
        jnp.exp(-decay[None, :] * fraction[:, None]) * jnp.sqrt((1.0 + decay) / seq_total)[None, :]
    )
    taps = mat_dot(hidden, w_out) * envelope
    return (features, preact, hidden, taps, envelope)


def angle_table(rows_idx, cols_idx, modulus):
    wrapped = rows_idx[:, None] * cols_idx[None, :] % modulus
    angles = wrapped.astype(jnp.float32) * (2.0 * math.pi / modulus)
    return (jnp.cos(angles), jnp.sin(angles))


def local(signal, cotangent, band_freq, w_embed, b_embed, w_out, decay):
    devices = lax.axis_size("seq")
    rank_seq = lax.axis_index("seq")
    seg_len = signal.shape[1] * 2
    channels = signal.shape[2] // 2
    block_w = seg_len // devices
    width = block_w * channels
    rows_all = 2 * devices
    pair = rows_all // devices
    seq_total = seg_len * devices
    fft_size = 2 * seq_total
    inv_scale = 1.0 / fft_size
    n_arr = 3

    dev_ids = jnp.arange(devices, dtype=jnp.int32)
    row_ids = jnp.arange(rows_all, dtype=jnp.int32)
    blk_ids = jnp.arange(block_w, dtype=jnp.int32)
    lane_blk = jnp.arange(width, dtype=jnp.int32) // channels
    b_lane = rank_seq * block_w + lane_blk

    src = jnp.stack(
        [signal.reshape(devices, width), cotangent.reshape(devices, width)], axis=1
    )
    cols = lax.all_to_all(src, "seq", split_axis=0, concat_axis=0, tiled=True)

    places = (
        dev_ids[:, None] * seg_len + rank_seq * block_w + blk_ids[None, :]
    ).reshape(-1)
    features, preact, hidden, taps, envelope = filter_parts(
        places, band_freq, w_embed, b_embed, w_out, decay, seq_total
    )
    stacked = jnp.concatenate(
        [cols.astype(jnp.float32), taps.reshape(devices, 1, width)], axis=1
    ).reshape(devices, n_arr * width)

    col_cos, col_sin = angle_table(row_ids, dev_ids, rows_all)
    y_re = fft_dot(col_cos, stacked).reshape(rows_all, n_arr, width)
    y_im = -fft_dot(col_sin, stacked).reshape(rows_all, n_arr, width)
    tw_cos, tw_sin = angle_table(row_ids, b_lane, fft_size)
    tw_cos = tw_cos[:, None, :]
    tw_sin = tw_sin[:, None, :]
    t_re = y_re * tw_cos + y_im * tw_sin
    t_im = y_im * tw_cos - y_re * tw_sin
    spec = jnp.stack([t_re, t_im], axis=1)
    spec = lax.all_to_all(
        spec.astype(jnp.bfloat16), "seq", split_axis=0, concat_axis=0, tiled=True
    ).astype(jnp.float32)

    q_cos, q_sin = angle_table(dev_ids, dev_ids, devices)
    stage_a = fft_dot(jnp.concatenate([q_cos, q_sin], axis=0), spec.reshape(devices, -1))
    lanes = 2 * channels
    n_grp = width // lanes
    blocks = [(z, k1l) for z in range(n_arr) for k1l in range(pair)]
    n_blk = len(blocks)
    lane_h = jnp.arange(lanes, dtype=jnp.int32) // channels
    flip = jnp.where(lane_h == 0, 1.0, -1.0).astype(jnp.float32)

    def col(k1l, ri, z, p):
        return ((k1l * 2 + ri) * n_arr + z) * width + p * lanes

    def rows_of(part, ri, p):
        return jnp.concatenate(
            [part[:, col(k1l, ri, z, p) : col(k1l, ri, z, p) + lanes] for z, k1l in blocks], axis=0
        )

    def mid_tab(p, count):
        c_t, s_t = angle_table(dev_ids, 2 * p + lane_h, seg_len)
        c_t = jnp.broadcast_to(c_t[None], (count, devices, lanes)).reshape(count * devices, lanes)
        s_t = jnp.broadcast_to(s_t[None], (count, devices, lanes)).reshape(count * devices, lanes)
        return c_t, s_t

    def lin(coefs, vals):
        acc = None
        for w, v in zip(coefs, vals):
            if abs(w) < 1e-12:
                continue
            term = v if w == 1.0 else (-v if w == -1.0 else v * w)
            acc = term if acc is None else acc + term
        return acc

    def w8(p, m):
        k = (p * m) % n_grp
        return (round(math.cos(2 * math.pi * k / n_grp), 15), round(math.sin(2 * math.pi * k / n_grp), 15))

    def half_tw(m):
        ang = 2 * math.pi * m / (2 * n_grp)
        c_t = jnp.where(lane_h == 1, math.cos(ang), 1.0).astype(jnp.float32)
        s_t = jnp.where(lane_h == 1, math.sin(ang), 0.0).astype(jnp.float32)
        return c_t, s_t

    def halves(x):
        return flip * x + jnp.roll(x, channels, axis=1)

    top = stage_a[:devices]
    bot = stage_a[devices:]
    x_re, x_im = [], []
    for p in range(n_grp):
        a_re = rows_of(top, 0, p) + rows_of(bot, 1, p)
        a_im = rows_of(top, 1, p) - rows_of(bot, 0, p)
        c_t, s_t = mid_tab(p, n_blk)
        x_re.append(a_re * c_t + a_im * s_t)
        x_im.append(a_im * c_t - a_re * s_t)
    spec_re, spec_im = [], []
    for m in range(n_grp):
        cs = [w8(p, m) for p in range(n_grp)]
        g_re = lin([c for c, _ in cs] + [s for _, s in cs], x_re + x_im)
        g_im = lin([c for c, _ in cs] + [-s for _, s in cs], x_im + x_re)
        c_t, s_t = half_tw(m)
        h_re = g_re * c_t + g_im * s_t
        h_im = g_im * c_t - g_re * s_t
        spec_re.append(halves(h_re))
        spec_im.append(halves(h_im))

    span = pair * devices
    prod_re, prod_im = [], []
    for m in range(n_grp):
        sig_r, cot_r, tap_r = [spec_re[m][z * span : (z + 1) * span] for z in range(n_arr)]
        sig_i, cot_i, tap_i = [spec_im[m][z * span : (z + 1) * span] for z in range(n_arr)]
        prod_re.append(jnp.concatenate(
            [sig_r * tap_r - sig_i * tap_i, cot_r * tap_r + cot_i * tap_i, cot_r * sig_r + cot_i * sig_i]
        ))
        prod_im.append(jnp.concatenate(
            [sig_r * tap_i + sig_i * tap_r, cot_i * tap_r - cot_r * tap_i, cot_i * sig_r - cot_r * sig_i]
        ))

    inv_mat = jnp.concatenate(
        [
            jnp.concatenate([q_cos, -q_sin], axis=1),
            jnp.concatenate([q_sin, q_cos], axis=1),
        ],
        axis=0,
    )
    b_rows = dev_ids[:, None] * block_w + lane_blk[None, :]
    k1_own = rank_seq * pair + jnp.arange(pair, dtype=jnp.int32)
    ex_ang = (b_rows[:, None, :] * k1_own[None, :, None]) % fft_size
    ex_ang = ex_ang.astype(jnp.float32) * (2.0 * math.pi / fft_size)
    ex_cos = jnp.cos(ex_ang)[:, :, None, :]
    ex_sin = jnp.sin(ex_ang)[:, :, None, :]
    out_mat = jnp.concatenate([col_cos.T, -col_sin.T], axis=1)

    def inverse_part(z_list):
        n_out = len(z_list)
        blocks_out = [(zi, k1l) for zi in range(n_out) for k1l in range(pair)]
        hh_re, hh_im = [], []
        for m in range(n_grp):
            pr = jnp.concatenate([prod_re[m][z * span : (z + 1) * span] for z in z_list])
            pi = jnp.concatenate([prod_im[m][z * span : (z + 1) * span] for z in z_list])
            g_re = halves(pr)
            g_im = halves(pi)
            c_t, s_t = half_tw(m)
            hh_re.append(g_re * c_t - g_im * s_t)
            hh_im.append(g_im * c_t + g_re * s_t)
        v_cols_re, v_cols_im = {}, {}
        for p in range(n_grp):
            cs = [w8(p, m) for m in range(n_grp)]
            u_re = lin([c for c, _ in cs] + [-s for _, s in cs], hh_re + hh_im)
            u_im = lin([c for c, _ in cs] + [s for _, s in cs], hh_im + hh_re)
            c_t, s_t = mid_tab(p, len(blocks_out))
            v_re = u_re * c_t - u_im * s_t
            v_im = u_im * c_t + u_re * s_t
            for idx, (zi, k1l) in enumerate(blocks_out):
                v_cols_re[(k1l, zi, p)] = v_re[idx * devices : (idx + 1) * devices]
                v_cols_im[(k1l, zi, p)] = v_im[idx * devices : (idx + 1) * devices]
        order = [(k1l, zi, p) for k1l in range(pair) for zi in range(n_out) for p in range(n_grp)]
        v_all = jnp.concatenate(
            [
                jnp.concatenate([v_cols_re[key] for key in order], axis=1),
                jnp.concatenate([v_cols_im[key] for key in order], axis=1),
            ],
            axis=0,
        )
        w_all = fft_dot(inv_mat, v_all).reshape(2, devices, pair, n_out, width)
        x_re = w_all[0] * ex_cos - w_all[1] * ex_sin
        x_im = w_all[0] * ex_sin + w_all[1] * ex_cos
        back = jnp.stack([x_re, x_im], axis=1)
        back = lax.all_to_all(
            back.astype(jnp.bfloat16), "seq", split_axis=0, concat_axis=0, tiled=True
        ).astype(jnp.float32)
        back = back.reshape(devices, 2, pair, n_out * width)
        back = jnp.transpose(back, (1, 0, 2, 3)).reshape(2 * rows_all, n_out * width)
        return (fft_dot(out_mat, back) * inv_scale).reshape(devices, n_out, width)

    res_taps = inverse_part([2])
    res_rows = inverse_part([0, 1])

    d_taps = res_taps[:, 0].reshape(devices * block_w, channels)
    d_raw = d_taps * envelope
    d_preact = mat_dot(d_raw, w_out.T) * jnp.cos(preact)
    out_part = mat_dot(hidden.T, d_raw)
    embed_part = mat_dot(features.T, d_preact)
    bias_part = jnp.sum(d_preact, axis=0)
    rank_chan = lax.axis_index("chan")
    n_chan = lax.axis_size("chan")
    out_wide = jnp.zeros((out_part.shape[0], n_chan * channels), jnp.float32)
    out_wide = lax.dynamic_update_slice_in_dim(out_wide, out_part, rank_chan * channels, axis=1)
    flat = jnp.concatenate([out_wide.reshape(-1), embed_part.reshape(-1), bias_part])
    piece = -(-flat.shape[0] // (devices * 128)) * 128
    flat = jnp.pad(flat, (0, devices * piece - flat.shape[0])).reshape(devices, piece)

    flat_hi = flat.astype(jnp.bfloat16)
    flat_lo = (flat - flat_hi.astype(jnp.float32)).astype(jnp.bfloat16)
    incoming = lax.all_to_all(
        jnp.concatenate([flat_hi, flat_lo], axis=1), "seq", split_axis=0, concat_axis=0, tiled=True
    )
    mine = jnp.sum(
        incoming[:, :piece].astype(jnp.float32) + incoming[:, piece:].astype(jnp.float32), axis=0
    )

    rows_out = lax.all_to_all(
        res_rows.astype(jnp.bfloat16), "seq", split_axis=0, concat_axis=0, tiled=True
    )
    conv_out = rows_out[:, 0].reshape(1, seg_len // 2, 2 * channels)
    d_signal = rows_out[:, 1].reshape(1, seg_len // 2, 2 * channels)

    n_all = devices * n_chan
    total = lax.all_to_all(
        jnp.broadcast_to(mine, (n_all, piece)), ("seq", "chan"), 0, 0, tiled=True
    )
    total = jnp.sum(total.reshape(devices, n_chan, piece), axis=1).reshape(-1)
    n_out = out_wide.size
    n_emb = embed_part.size
    wide_sum = total[:n_out].reshape(out_wide.shape)
    embed_all = total[n_out : n_out + n_emb].reshape(embed_part.shape)
    bias_all = total[n_out + n_emb : n_out + n_emb + bias_part.size]
    out_sum = lax.dynamic_slice_in_dim(wide_sum, rank_chan * channels, channels, axis=1)
    norm_scale = 1.0 / math.sqrt(seq_total)
    return (conv_out, d_signal, embed_all * norm_scale, bias_all * norm_scale, out_sum * norm_scale)


def solution(mesh):
    return jax.shard_map(
        local,
        mesh=mesh,
        in_specs=(
            P("chan", "seq", None),
            P("chan", "seq", None),
            P(),
            P(),
            P(),
            P(None, "chan"),
            P("chan"),
        ),
        out_specs=(P("chan", "seq", None), P("chan", "seq", None), P(), P(), P(None, "chan")),
        check_vma=False,
    )
```

```python
import math

import jax
import jax.numpy as jnp
from jax import lax
from jax.sharding import PartitionSpec as P

exact_mode = lax.Precision.HIGHEST


def mat_dot(lhs_mat, rhs_mat):
    return jnp.dot(lhs_mat, rhs_mat, preferred_element_type=jnp.float32, precision=exact_mode)


def fft_dot(lhs_mat, rhs_mat):
    return jnp.dot(
        lhs_mat, rhs_mat, preferred_element_type=jnp.float32, precision=lax.Precision.HIGH
    )


def band_phase(band_freq, places, seq_total):
    upper_part = places // 1024
    lower_part = places % 1024
    partial_turn = upper_part[:, None] * band_freq[None, :] % seq_total
    wrapped = (partial_turn * 1024 + lower_part[:, None] * band_freq[None, :]) % seq_total
    return wrapped.astype(jnp.float32) * (2.0 * math.pi / seq_total)


def filter_parts(places, band_freq, w_embed, b_embed, w_out, decay, seq_total):
    phases = band_phase(band_freq, places, seq_total)
    features = jnp.concatenate([jnp.cos(phases), jnp.sin(phases)], axis=1)
    preact = mat_dot(features, w_embed) + b_embed[None, :]
    hidden = jnp.sin(preact)
    fraction = places.astype(jnp.float32) / seq_total
    envelope = (
        jnp.exp(-decay[None, :] * fraction[:, None]) * jnp.sqrt((1.0 + decay) / seq_total)[None, :]
    )
    taps = mat_dot(hidden, w_out) * envelope
    return (features, preact, hidden, taps, envelope)


def angle_table(rows_idx, cols_idx, modulus):
    wrapped = rows_idx[:, None] * cols_idx[None, :] % modulus
    angles = wrapped.astype(jnp.float32) * (2.0 * math.pi / modulus)
    return (jnp.cos(angles), jnp.sin(angles))


def local(signal, cotangent, band_freq, w_embed, b_embed, w_out, decay):
    devices = lax.axis_size("seq")
    rank_seq = lax.axis_index("seq")
    seg_len = signal.shape[1] * 2
    channels = signal.shape[2] // 2
    block_w = seg_len // devices
    width = block_w * channels
    rows_all = 2 * devices
    pair = rows_all // devices
    seq_total = seg_len * devices
    fft_size = 2 * seq_total
    inv_scale = 1.0 / fft_size
    n_arr = 3

    dev_ids = jnp.arange(devices, dtype=jnp.int32)
    row_ids = jnp.arange(rows_all, dtype=jnp.int32)
    blk_ids = jnp.arange(block_w, dtype=jnp.int32)
    lane_blk = jnp.arange(width, dtype=jnp.int32) // channels
    b_lane = rank_seq * block_w + lane_blk

    src = jnp.stack(
        [signal.reshape(devices, width), cotangent.reshape(devices, width)], axis=1
    )
    cols = lax.all_to_all(src, "seq", split_axis=0, concat_axis=0, tiled=True)

    places = (
        dev_ids[:, None] * seg_len + rank_seq * block_w + blk_ids[None, :]
    ).reshape(-1)
    features, preact, hidden, taps, envelope = filter_parts(
        places, band_freq, w_embed, b_embed, w_out, decay, seq_total
    )
    stacked = jnp.concatenate(
        [cols.astype(jnp.float32), taps.reshape(devices, 1, width)], axis=1
    ).reshape(devices, n_arr * width)

    col_cos, col_sin = angle_table(row_ids, dev_ids, rows_all)
    y_re = fft_dot(col_cos, stacked).reshape(rows_all, n_arr, width)
    y_im = -fft_dot(col_sin, stacked).reshape(rows_all, n_arr, width)
    tw_cos, tw_sin = angle_table(row_ids, b_lane, fft_size)
    tw_cos = tw_cos[:, None, :]
    tw_sin = tw_sin[:, None, :]
    t_re = y_re * tw_cos + y_im * tw_sin
    t_im = y_im * tw_cos - y_re * tw_sin
    spec = jnp.stack([t_re, t_im], axis=1)
    spec = lax.all_to_all(
        spec.astype(jnp.bfloat16), "seq", split_axis=0, concat_axis=0, tiled=True
    ).astype(jnp.float32)

    q_cos, q_sin = angle_table(dev_ids, dev_ids, devices)
    stage_a = fft_dot(jnp.concatenate([q_cos, q_sin], axis=0), spec.reshape(devices, -1))
    lanes = 2 * channels
    n_grp = width // lanes
    blocks = [(z, k1l) for z in range(n_arr) for k1l in range(pair)]
    n_blk = len(blocks)
    lane_h = jnp.arange(lanes, dtype=jnp.int32) // channels
    flip = jnp.where(lane_h == 0, 1.0, -1.0).astype(jnp.float32)

    def col(k1l, ri, z, p):
        return ((k1l * 2 + ri) * n_arr + z) * width + p * lanes

    def rows_of(part, ri, p):
        return jnp.concatenate(
            [part[:, col(k1l, ri, z, p) : col(k1l, ri, z, p) + lanes] for z, k1l in blocks], axis=0
        )

    def mid_tab(p, count):
        c_t, s_t = angle_table(dev_ids, 2 * p + lane_h, seg_len)
        c_t = jnp.broadcast_to(c_t[None], (count, devices, lanes)).reshape(count * devices, lanes)
        s_t = jnp.broadcast_to(s_t[None], (count, devices, lanes)).reshape(count * devices, lanes)
        return c_t, s_t

    def lin(coefs, vals):
        acc = None
        for w, v in zip(coefs, vals):
            if abs(w) < 1e-12:
                continue
            term = v if w == 1.0 else (-v if w == -1.0 else v * w)
            acc = term if acc is None else acc + term
        return acc

    def w8(p, m):
        k = (p * m) % n_grp
        return (round(math.cos(2 * math.pi * k / n_grp), 15), round(math.sin(2 * math.pi * k / n_grp), 15))

    def half_tw(m):
        ang = 2 * math.pi * m / (2 * n_grp)
        c_t = jnp.where(lane_h == 1, math.cos(ang), 1.0).astype(jnp.float32)
        s_t = jnp.where(lane_h == 1, math.sin(ang), 0.0).astype(jnp.float32)
        return c_t, s_t

    def halves(x):
        return flip * x + jnp.roll(x, channels, axis=1)

    top = stage_a[:devices]
    bot = stage_a[devices:]
    x_re, x_im = [], []
    for p in range(n_grp):
        a_re = rows_of(top, 0, p) + rows_of(bot, 1, p)
        a_im = rows_of(top, 1, p) - rows_of(bot, 0, p)
        c_t, s_t = mid_tab(p, n_blk)
        x_re.append(a_re * c_t + a_im * s_t)
        x_im.append(a_im * c_t - a_re * s_t)
    spec_re, spec_im = [], []
    for m in range(n_grp):
        cs = [w8(p, m) for p in range(n_grp)]
        g_re = lin([c for c, _ in cs] + [s for _, s in cs], x_re + x_im)
        g_im = lin([c for c, _ in cs] + [-s for _, s in cs], x_im + x_re)
        c_t, s_t = half_tw(m)
        h_re = g_re * c_t + g_im * s_t
        h_im = g_im * c_t - g_re * s_t
        spec_re.append(halves(h_re))
        spec_im.append(halves(h_im))

    span = pair * devices
    prod_re, prod_im = [], []
    for m in range(n_grp):
        sig_r, cot_r, tap_r = [spec_re[m][z * span : (z + 1) * span] for z in range(n_arr)]
        sig_i, cot_i, tap_i = [spec_im[m][z * span : (z + 1) * span] for z in range(n_arr)]
        prod_re.append(jnp.concatenate(
            [sig_r * tap_r - sig_i * tap_i, cot_r * tap_r + cot_i * tap_i, cot_r * sig_r + cot_i * sig_i]
        ))
        prod_im.append(jnp.concatenate(
            [sig_r * tap_i + sig_i * tap_r, cot_i * tap_r - cot_r * tap_i, cot_i * sig_r - cot_r * sig_i]
        ))

    inv_mat = jnp.concatenate(
        [
            jnp.concatenate([q_cos, -q_sin], axis=1),
            jnp.concatenate([q_sin, q_cos], axis=1),
        ],
        axis=0,
    )
    b_rows = dev_ids[:, None] * block_w + lane_blk[None, :]
    k1_own = rank_seq * pair + jnp.arange(pair, dtype=jnp.int32)
    ex_ang = (b_rows[:, None, :] * k1_own[None, :, None]) % fft_size
    ex_ang = ex_ang.astype(jnp.float32) * (2.0 * math.pi / fft_size)
    ex_cos = jnp.cos(ex_ang)[:, :, None, :]
    ex_sin = jnp.sin(ex_ang)[:, :, None, :]
    out_mat = jnp.concatenate([col_cos.T, -col_sin.T], axis=1)

    def inverse_part(z_list):
        n_out = len(z_list)
        blocks_out = [(zi, k1l) for zi in range(n_out) for k1l in range(pair)]
        hh_re, hh_im = [], []
        for m in range(n_grp):
            pr = jnp.concatenate([prod_re[m][z * span : (z + 1) * span] for z in z_list])
            pi = jnp.concatenate([prod_im[m][z * span : (z + 1) * span] for z in z_list])
            g_re = halves(pr)
            g_im = halves(pi)
            c_t, s_t = half_tw(m)
            hh_re.append(g_re * c_t - g_im * s_t)
            hh_im.append(g_im * c_t + g_re * s_t)
        v_cols_re, v_cols_im = {}, {}
        for p in range(n_grp):
            cs = [w8(p, m) for m in range(n_grp)]
            u_re = lin([c for c, _ in cs] + [-s for _, s in cs], hh_re + hh_im)
            u_im = lin([c for c, _ in cs] + [s for _, s in cs], hh_im + hh_re)
            c_t, s_t = mid_tab(p, len(blocks_out))
            v_re = u_re * c_t - u_im * s_t
            v_im = u_im * c_t + u_re * s_t
            for idx, (zi, k1l) in enumerate(blocks_out):
                v_cols_re[(k1l, zi, p)] = v_re[idx * devices : (idx + 1) * devices]
                v_cols_im[(k1l, zi, p)] = v_im[idx * devices : (idx + 1) * devices]
        order = [(k1l, zi, p) for k1l in range(pair) for zi in range(n_out) for p in range(n_grp)]
        v_all = jnp.concatenate(
            [
                jnp.concatenate([v_cols_re[key] for key in order], axis=1),
                jnp.concatenate([v_cols_im[key] for key in order], axis=1),
            ],
            axis=0,
        )
        w_all = fft_dot(inv_mat, v_all).reshape(2, devices, pair, n_out, width)
        x_re = w_all[0] * ex_cos - w_all[1] * ex_sin
        x_im = w_all[0] * ex_sin + w_all[1] * ex_cos
        back = jnp.stack([x_re, x_im], axis=1).reshape(devices, 2, pair, n_out * width)
        back = lax.all_to_all(
            back.astype(jnp.bfloat16), "seq", split_axis=0, concat_axis=0, tiled=True
        ).astype(jnp.float32)
        back = back.reshape(devices, 2, pair, n_out * width)
        back = jnp.transpose(back, (1, 0, 2, 3)).reshape(2 * rows_all, n_out * width)
        return (fft_dot(out_mat, back) * inv_scale).reshape(devices, n_out, width)

    res_taps = inverse_part([2])
    res_rows = inverse_part([0, 1])

    d_taps = res_taps[:, 0].reshape(devices * block_w, channels)
    d_raw = d_taps * envelope
    d_preact = mat_dot(d_raw, w_out.T) * jnp.cos(preact)
    out_part = mat_dot(hidden.T, d_raw)
    embed_part = mat_dot(features.T, d_preact)
    bias_part = jnp.sum(d_preact, axis=0)
    rank_chan = lax.axis_index("chan")
    n_chan = lax.axis_size("chan")
    out_wide = jnp.zeros((out_part.shape[0], n_chan * channels), jnp.float32)
    out_wide = lax.dynamic_update_slice_in_dim(out_wide, out_part, rank_chan * channels, axis=1)
    flat = jnp.concatenate([out_wide.reshape(-1), embed_part.reshape(-1), bias_part])
    piece = -(-flat.shape[0] // (devices * 128)) * 128
    flat = jnp.pad(flat, (0, devices * piece - flat.shape[0])).reshape(devices, piece)

    flat_hi = flat.astype(jnp.bfloat16)
    flat_lo = (flat - flat_hi.astype(jnp.float32)).astype(jnp.bfloat16)
    outgoing = jnp.concatenate(
        [res_rows.reshape(devices, 2 * width).astype(jnp.bfloat16), flat_hi, flat_lo], axis=1
    )
    incoming = lax.all_to_all(outgoing, "seq", split_axis=0, concat_axis=0, tiled=True)
    rows_out = incoming[:, : 2 * width].reshape(devices, 2, width)
    conv_out = rows_out[:, 0].reshape(1, seg_len // 2, 2 * channels)
    d_signal = rows_out[:, 1].reshape(1, seg_len // 2, 2 * channels)
    got_hi = incoming[:, 2 * width : 2 * width + piece].astype(jnp.float32)
    got_lo = incoming[:, 2 * width + piece :].astype(jnp.float32)
    mine = jnp.sum(got_hi + got_lo, axis=0)

    n_all = devices * n_chan
    total = lax.all_to_all(
        jnp.broadcast_to(mine, (n_all, piece)), ("seq", "chan"), 0, 0, tiled=True
    )
    total = jnp.sum(total.reshape(devices, n_chan, piece), axis=1).reshape(-1)
    n_out = out_wide.size
    n_emb = embed_part.size
    wide_sum = total[:n_out].reshape(out_wide.shape)
    embed_all = total[n_out : n_out + n_emb].reshape(embed_part.shape)
    bias_all = total[n_out + n_emb : n_out + n_emb + bias_part.size]
    out_sum = lax.dynamic_slice_in_dim(wide_sum, rank_chan * channels, channels, axis=1)
    norm_scale = 1.0 / math.sqrt(seq_total)
    return (conv_out, d_signal, embed_all * norm_scale, bias_all * norm_scale, out_sum * norm_scale)


def solution(mesh):
    return jax.shard_map(
        local,
        mesh=mesh,
        in_specs=(
            P("chan", "seq", None),
            P("chan", "seq", None),
            P(),
            P(),
            P(),
            P(None, "chan"),
            P("chan"),
        ),
        out_specs=(P("chan", "seq", None), P("chan", "seq", None), P(), P(), P(None, "chan")),
        check_vma=False,
    )
```

```python
import math

import jax
import jax.numpy as jnp
from jax import lax
from jax.sharding import PartitionSpec as P

exact_mode = lax.Precision.HIGHEST


def mat_dot(lhs_mat, rhs_mat):
    return jnp.dot(lhs_mat, rhs_mat, preferred_element_type=jnp.float32, precision=exact_mode)


def fft_dot(lhs_mat, rhs_mat):
    return jnp.dot(
        lhs_mat, rhs_mat, preferred_element_type=jnp.float32, precision=lax.Precision.HIGH
    )


def band_phase(band_freq, places, seq_total):
    upper_part = places // 1024
    lower_part = places % 1024
    partial_turn = upper_part[:, None] * band_freq[None, :] % seq_total
    wrapped = (partial_turn * 1024 + lower_part[:, None] * band_freq[None, :]) % seq_total
    return wrapped.astype(jnp.float32) * (2.0 * math.pi / seq_total)


def filter_parts(places, band_freq, w_embed, b_embed, w_out, decay, seq_total):
    phases = band_phase(band_freq, places, seq_total)
    features = jnp.concatenate([jnp.cos(phases), jnp.sin(phases)], axis=1)
    preact = mat_dot(features, w_embed) + b_embed[None, :]
    hidden = jnp.sin(preact)
    fraction = places.astype(jnp.float32) / seq_total
    envelope = (
        jnp.exp(-decay[None, :] * fraction[:, None]) * jnp.sqrt((1.0 + decay) / seq_total)[None, :]
    )
    taps = mat_dot(hidden, w_out) * envelope
    return (features, preact, hidden, taps, envelope)


def angle_table(rows_idx, cols_idx, modulus):
    wrapped = rows_idx[:, None] * cols_idx[None, :] % modulus
    angles = wrapped.astype(jnp.float32) * (2.0 * math.pi / modulus)
    return (jnp.cos(angles), jnp.sin(angles))


def local(signal, cotangent, band_freq, w_embed, b_embed, w_out, decay):
    devices = lax.axis_size("seq")
    rank_seq = lax.axis_index("seq")
    seg_len = signal.shape[1] * 2
    channels = signal.shape[2] // 2
    block_w = seg_len // devices
    width = block_w * channels
    rows_all = 2 * devices
    pair = rows_all // devices
    seq_total = seg_len * devices
    fft_size = 2 * seq_total
    inv_scale = 1.0 / fft_size
    n_arr = 3

    dev_ids = jnp.arange(devices, dtype=jnp.int32)
    row_ids = jnp.arange(rows_all, dtype=jnp.int32)
    blk_ids = jnp.arange(block_w, dtype=jnp.int32)
    lane_blk = jnp.arange(width, dtype=jnp.int32) // channels
    b_lane = rank_seq * block_w + lane_blk

    src = jnp.stack(
        [signal.reshape(devices, width), cotangent.reshape(devices, width)], axis=1
    )
    cols = lax.all_to_all(src, "seq", split_axis=0, concat_axis=0, tiled=True)

    places = (
        dev_ids[:, None] * seg_len + rank_seq * block_w + blk_ids[None, :]
    ).reshape(-1)
    features, preact, hidden, taps, envelope = filter_parts(
        places, band_freq, w_embed, b_embed, w_out, decay, seq_total
    )
    stacked = jnp.concatenate(
        [cols.astype(jnp.float32), taps.reshape(devices, 1, width)], axis=1
    ).reshape(devices, n_arr * width)

    col_cos, col_sin = angle_table(row_ids, dev_ids, rows_all)
    y_re = fft_dot(col_cos, stacked).reshape(rows_all, n_arr, width)
    y_im = -fft_dot(col_sin, stacked).reshape(rows_all, n_arr, width)
    tw_cos, tw_sin = angle_table(row_ids, b_lane, fft_size)
    tw_cos = tw_cos[:, None, :]
    tw_sin = tw_sin[:, None, :]
    t_re = y_re * tw_cos + y_im * tw_sin
    t_im = y_im * tw_cos - y_re * tw_sin
    spec = jnp.stack([t_re, t_im], axis=1)
    spec = lax.all_to_all(
        spec.astype(jnp.bfloat16), "seq", split_axis=0, concat_axis=0, tiled=True
    ).astype(jnp.float32)

    q_cos, q_sin = angle_table(dev_ids, dev_ids, devices)
    stage_a = fft_dot(jnp.concatenate([q_cos, q_sin], axis=0), spec.reshape(devices, -1))
    lanes = 2 * channels
    n_grp = width // lanes
    blocks = [(z, k1l) for z in range(n_arr) for k1l in range(pair)]
    n_blk = len(blocks)
    lane_h = jnp.arange(lanes, dtype=jnp.int32) // channels
    flip = jnp.where(lane_h == 0, 1.0, -1.0).astype(jnp.float32)

    def col(k1l, ri, z, p):
        return ((k1l * 2 + ri) * n_arr + z) * width + p * lanes

    def rows_of(part, ri, p):
        return jnp.concatenate(
            [part[:, col(k1l, ri, z, p) : col(k1l, ri, z, p) + lanes] for z, k1l in blocks], axis=0
        )

    def mid_tab(p, count):
        c_t, s_t = angle_table(dev_ids, 2 * p + lane_h, seg_len)
        c_t = jnp.broadcast_to(c_t[None], (count, devices, lanes)).reshape(count * devices, lanes)
        s_t = jnp.broadcast_to(s_t[None], (count, devices, lanes)).reshape(count * devices, lanes)
        return c_t, s_t

    def lin(coefs, vals):
        acc = None
        for w, v in zip(coefs, vals):
            if abs(w) < 1e-12:
                continue
            term = v if w == 1.0 else (-v if w == -1.0 else v * w)
            acc = term if acc is None else acc + term
        return acc

    def w8(p, m):
        k = (p * m) % n_grp
        return (round(math.cos(2 * math.pi * k / n_grp), 15), round(math.sin(2 * math.pi * k / n_grp), 15))

    def half_tw(m):
        ang = 2 * math.pi * m / (2 * n_grp)
        c_t = jnp.where(lane_h == 1, math.cos(ang), 1.0).astype(jnp.float32)
        s_t = jnp.where(lane_h == 1, math.sin(ang), 0.0).astype(jnp.float32)
        return c_t, s_t

    def halves(x):
        return flip * x + jnp.roll(x, channels, axis=1)

    top = stage_a[:devices]
    bot = stage_a[devices:]
    x_re, x_im = [], []
    for p in range(n_grp):
        a_re = rows_of(top, 0, p) + rows_of(bot, 1, p)
        a_im = rows_of(top, 1, p) - rows_of(bot, 0, p)
        c_t, s_t = mid_tab(p, n_blk)
        x_re.append(a_re * c_t + a_im * s_t)
        x_im.append(a_im * c_t - a_re * s_t)
    spec_re, spec_im = [], []
    for m in range(n_grp):
        cs = [w8(p, m) for p in range(n_grp)]
        g_re = lin([c for c, _ in cs] + [s for _, s in cs], x_re + x_im)
        g_im = lin([c for c, _ in cs] + [-s for _, s in cs], x_im + x_re)
        c_t, s_t = half_tw(m)
        h_re = g_re * c_t + g_im * s_t
        h_im = g_im * c_t - g_re * s_t
        spec_re.append(halves(h_re))
        spec_im.append(halves(h_im))

    span = pair * devices
    prod_re, prod_im = [], []
    for m in range(n_grp):
        sig_r, cot_r, tap_r = [spec_re[m][z * span : (z + 1) * span] for z in range(n_arr)]
        sig_i, cot_i, tap_i = [spec_im[m][z * span : (z + 1) * span] for z in range(n_arr)]
        prod_re.append(jnp.concatenate(
            [sig_r * tap_r - sig_i * tap_i, cot_r * tap_r + cot_i * tap_i, cot_r * sig_r + cot_i * sig_i]
        ))
        prod_im.append(jnp.concatenate(
            [sig_r * tap_i + sig_i * tap_r, cot_i * tap_r - cot_r * tap_i, cot_i * sig_r - cot_r * sig_i]
        ))

    inv_mat = jnp.concatenate(
        [
            jnp.concatenate([q_cos, -q_sin], axis=1),
            jnp.concatenate([q_sin, q_cos], axis=1),
        ],
        axis=0,
    )
    b_rows = dev_ids[:, None] * block_w + lane_blk[None, :]
    k1_own = rank_seq * pair + jnp.arange(pair, dtype=jnp.int32)
    ex_ang = (b_rows[:, None, :] * k1_own[None, :, None]) % fft_size
    ex_ang = ex_ang.astype(jnp.float32) * (2.0 * math.pi / fft_size)
    ex_cos = jnp.cos(ex_ang)[:, :, None, :]
    ex_sin = jnp.sin(ex_ang)[:, :, None, :]
    out_mat = jnp.concatenate([col_cos.T, -col_sin.T], axis=1)

    def inverse_part(z_list):
        n_out = len(z_list)
        blocks_out = [(zi, k1l) for zi in range(n_out) for k1l in range(pair)]
        hh_re, hh_im = [], []
        for m in range(n_grp):
            pr = jnp.concatenate([prod_re[m][z * span : (z + 1) * span] for z in z_list])
            pi = jnp.concatenate([prod_im[m][z * span : (z + 1) * span] for z in z_list])
            g_re = halves(pr)
            g_im = halves(pi)
            c_t, s_t = half_tw(m)
            hh_re.append(g_re * c_t - g_im * s_t)
            hh_im.append(g_im * c_t + g_re * s_t)
        v_cols_re, v_cols_im = {}, {}
        for p in range(n_grp):
            cs = [w8(p, m) for m in range(n_grp)]
            u_re = lin([c for c, _ in cs] + [-s for _, s in cs], hh_re + hh_im)
            u_im = lin([c for c, _ in cs] + [s for _, s in cs], hh_im + hh_re)
            c_t, s_t = mid_tab(p, len(blocks_out))
            v_re = u_re * c_t - u_im * s_t
            v_im = u_im * c_t + u_re * s_t
            for idx, (zi, k1l) in enumerate(blocks_out):
                v_cols_re[(k1l, zi, p)] = v_re[idx * devices : (idx + 1) * devices]
                v_cols_im[(k1l, zi, p)] = v_im[idx * devices : (idx + 1) * devices]
        order = [(k1l, zi, p) for k1l in range(pair) for zi in range(n_out) for p in range(n_grp)]
        v_all = jnp.concatenate(
            [
                jnp.concatenate([v_cols_re[key] for key in order], axis=1),
                jnp.concatenate([v_cols_im[key] for key in order], axis=1),
            ],
            axis=0,
        )
        w_all = fft_dot(inv_mat, v_all).reshape(2, devices, pair, n_out, width)
        x_re = w_all[0] * ex_cos - w_all[1] * ex_sin
        x_im = w_all[0] * ex_sin + w_all[1] * ex_cos
        back = jnp.stack([x_re, x_im], axis=1)
        back = lax.all_to_all(
            back.astype(jnp.bfloat16), "seq", split_axis=0, concat_axis=0, tiled=True
        ).astype(jnp.float32)
        back = back.reshape(devices, 2, pair, n_out * width)
        back = jnp.transpose(back, (1, 0, 2, 3)).reshape(2 * rows_all, n_out * width)
        return (fft_dot(out_mat, back) * inv_scale).reshape(devices, n_out, width)

    res_taps = inverse_part([2])
    res_rows = inverse_part([0, 1])

    d_taps = res_taps[:, 0].reshape(devices * block_w, channels)
    d_raw = d_taps * envelope
    d_preact = mat_dot(d_raw, w_out.T) * jnp.cos(preact)
    out_part = mat_dot(hidden.T, d_raw)
    embed_part = mat_dot(features.T, d_preact)
    bias_part = jnp.sum(d_preact, axis=0)
    rank_chan = lax.axis_index("chan")
    n_chan = lax.axis_size("chan")
    flat = jnp.concatenate([out_part.reshape(-1), embed_part.reshape(-1), bias_part])
    piece = -(-flat.shape[0] // (devices * 128)) * 128
    flat = jnp.pad(flat, (0, devices * piece - flat.shape[0])).reshape(devices, piece)

    flat_hi = flat.astype(jnp.bfloat16)
    flat_lo = (flat - flat_hi.astype(jnp.float32)).astype(jnp.bfloat16)
    outgoing = jnp.concatenate(
        [res_rows.reshape(devices, 2 * width).astype(jnp.bfloat16), flat_hi, flat_lo], axis=1
    )
    incoming = lax.all_to_all(outgoing, "seq", split_axis=0, concat_axis=0, tiled=True)
    rows_out = incoming[:, : 2 * width].reshape(devices, 2, width)
    conv_out = rows_out[:, 0].reshape(1, seg_len // 2, 2 * channels)
    d_signal = rows_out[:, 1].reshape(1, seg_len // 2, 2 * channels)
    got_hi = incoming[:, 2 * width : 2 * width + piece].astype(jnp.float32)
    got_lo = incoming[:, 2 * width + piece :].astype(jnp.float32)
    mine = jnp.sum(got_hi + got_lo, axis=0)

    n_all = devices * n_chan
    total = lax.all_to_all(
        jnp.broadcast_to(mine, (n_all, piece)), ("seq", "chan"), 0, 0, tiled=True
    )
    total = total.reshape(devices, n_chan, piece)
    own = lax.dynamic_index_in_dim(total, rank_chan, axis=1, keepdims=False).reshape(-1)
    both = jnp.sum(total, axis=1).reshape(-1)
    n_out = out_part.size
    n_emb = embed_part.size
    out_sum = own[:n_out].reshape(out_part.shape)
    embed_all = both[n_out : n_out + n_emb].reshape(embed_part.shape)
    bias_all = both[n_out + n_emb : n_out + n_emb + bias_part.size]
    norm_scale = 1.0 / math.sqrt(seq_total)
    return (conv_out, d_signal, embed_all * norm_scale, bias_all * norm_scale, out_sum * norm_scale)


def solution(mesh):
    return jax.shard_map(
        local,
        mesh=mesh,
        in_specs=(
            P("chan", "seq", None),
            P("chan", "seq", None),
            P(),
            P(),
            P(),
            P(None, "chan"),
            P("chan"),
        ),
        out_specs=(P("chan", "seq", None), P("chan", "seq", None), P(), P(), P(None, "chan")),
        check_vma=False,
    )
```

```python
import math

import jax
import jax.numpy as jnp
from jax import lax
from jax.sharding import PartitionSpec as P

exact_mode = lax.Precision.HIGH


def mat_dot(lhs_mat, rhs_mat):
    return jnp.dot(lhs_mat, rhs_mat, preferred_element_type=jnp.float32, precision=exact_mode)


def fft_dot(lhs_mat, rhs_mat):
    return jnp.dot(
        lhs_mat, rhs_mat, preferred_element_type=jnp.float32, precision=lax.Precision.HIGH
    )


def band_phase(band_freq, places, seq_total):
    upper_part = places // 1024
    lower_part = places % 1024
    partial_turn = upper_part[:, None] * band_freq[None, :] % seq_total
    wrapped = (partial_turn * 1024 + lower_part[:, None] * band_freq[None, :]) % seq_total
    return wrapped.astype(jnp.float32) * (2.0 * math.pi / seq_total)


def filter_parts(places, band_freq, w_embed, b_embed, w_out, decay, seq_total):
    phases = band_phase(band_freq, places, seq_total)
    features = jnp.concatenate([jnp.cos(phases), jnp.sin(phases)], axis=1)
    preact = mat_dot(features, w_embed) + b_embed[None, :]
    hidden = jnp.sin(preact)
    fraction = places.astype(jnp.float32) / seq_total
    envelope = (
        jnp.exp(-decay[None, :] * fraction[:, None]) * jnp.sqrt((1.0 + decay) / seq_total)[None, :]
    )
    taps = mat_dot(hidden, w_out) * envelope
    return (features, preact, hidden, taps, envelope)


def angle_table(rows_idx, cols_idx, modulus):
    wrapped = rows_idx[:, None] * cols_idx[None, :] % modulus
    angles = wrapped.astype(jnp.float32) * (2.0 * math.pi / modulus)
    return (jnp.cos(angles), jnp.sin(angles))


def local(signal, cotangent, band_freq, w_embed, b_embed, w_out, decay):
    devices = lax.axis_size("seq")
    rank_seq = lax.axis_index("seq")
    seg_len = signal.shape[1] * 2
    channels = signal.shape[2] // 2
    block_w = seg_len // devices
    width = block_w * channels
    rows_all = 2 * devices
    pair = rows_all // devices
    seq_total = seg_len * devices
    fft_size = 2 * seq_total
    inv_scale = 1.0 / fft_size
    n_arr = 3

    dev_ids = jnp.arange(devices, dtype=jnp.int32)
    row_ids = jnp.arange(rows_all, dtype=jnp.int32)
    blk_ids = jnp.arange(block_w, dtype=jnp.int32)
    lane_blk = jnp.arange(width, dtype=jnp.int32) // channels
    b_lane = rank_seq * block_w + lane_blk

    src = jnp.stack(
        [signal.reshape(devices, width), cotangent.reshape(devices, width)], axis=1
    )
    cols = lax.all_to_all(src, "seq", split_axis=0, concat_axis=0, tiled=True)

    places = (
        dev_ids[:, None] * seg_len + rank_seq * block_w + blk_ids[None, :]
    ).reshape(-1)
    features, preact, hidden, taps, envelope = filter_parts(
        places, band_freq, w_embed, b_embed, w_out, decay, seq_total
    )
    stacked = jnp.concatenate(
        [cols.astype(jnp.float32), taps.reshape(devices, 1, width)], axis=1
    ).reshape(devices, n_arr * width)

    col_cos, col_sin = angle_table(row_ids, dev_ids, rows_all)
    y_re = fft_dot(col_cos, stacked).reshape(rows_all, n_arr, width)
    y_im = -fft_dot(col_sin, stacked).reshape(rows_all, n_arr, width)
    tw_cos, tw_sin = angle_table(row_ids, b_lane, fft_size)
    tw_cos = tw_cos[:, None, :]
    tw_sin = tw_sin[:, None, :]
    t_re = y_re * tw_cos + y_im * tw_sin
    t_im = y_im * tw_cos - y_re * tw_sin
    spec = jnp.stack([t_re, t_im], axis=1)
    spec = lax.all_to_all(
        spec.astype(jnp.bfloat16), "seq", split_axis=0, concat_axis=0, tiled=True
    ).astype(jnp.float32)

    q_cos, q_sin = angle_table(dev_ids, dev_ids, devices)
    stage_a = fft_dot(jnp.concatenate([q_cos, q_sin], axis=0), spec.reshape(devices, -1))
    lanes = 2 * channels
    n_grp = width // lanes
    blocks = [(z, k1l) for z in range(n_arr) for k1l in range(pair)]
    n_blk = len(blocks)
    lane_h = jnp.arange(lanes, dtype=jnp.int32) // channels
    flip = jnp.where(lane_h == 0, 1.0, -1.0).astype(jnp.float32)

    def col(k1l, ri, z, p):
        return ((k1l * 2 + ri) * n_arr + z) * width + p * lanes

    def rows_of(part, ri, p):
        return jnp.concatenate(
            [part[:, col(k1l, ri, z, p) : col(k1l, ri, z, p) + lanes] for z, k1l in blocks], axis=0
        )

    def mid_tab(p, count):
        c_t, s_t = angle_table(dev_ids, 2 * p + lane_h, seg_len)
        c_t = jnp.broadcast_to(c_t[None], (count, devices, lanes)).reshape(count * devices, lanes)
        s_t = jnp.broadcast_to(s_t[None], (count, devices, lanes)).reshape(count * devices, lanes)
        return c_t, s_t

    def lin(coefs, vals):
        acc = None
        for w, v in zip(coefs, vals):
            if abs(w) < 1e-12:
                continue
            term = v if w == 1.0 else (-v if w == -1.0 else v * w)
            acc = term if acc is None else acc + term
        return acc

    def w8(p, m):
        k = (p * m) % n_grp
        return (round(math.cos(2 * math.pi * k / n_grp), 15), round(math.sin(2 * math.pi * k / n_grp), 15))

    def half_tw(m):
        ang = 2 * math.pi * m / (2 * n_grp)
        c_t = jnp.where(lane_h == 1, math.cos(ang), 1.0).astype(jnp.float32)
        s_t = jnp.where(lane_h == 1, math.sin(ang), 0.0).astype(jnp.float32)
        return c_t, s_t

    def halves(x):
        return flip * x + jnp.roll(x, channels, axis=1)

    top = stage_a[:devices]
    bot = stage_a[devices:]
    x_re, x_im = [], []
    for p in range(n_grp):
        a_re = rows_of(top, 0, p) + rows_of(bot, 1, p)
        a_im = rows_of(top, 1, p) - rows_of(bot, 0, p)
        c_t, s_t = mid_tab(p, n_blk)
        x_re.append(a_re * c_t + a_im * s_t)
        x_im.append(a_im * c_t - a_re * s_t)
    spec_re, spec_im = [], []
    for m in range(n_grp):
        cs = [w8(p, m) for p in range(n_grp)]
        g_re = lin([c for c, _ in cs] + [s for _, s in cs], x_re + x_im)
        g_im = lin([c for c, _ in cs] + [-s for _, s in cs], x_im + x_re)
        c_t, s_t = half_tw(m)
        h_re = g_re * c_t + g_im * s_t
        h_im = g_im * c_t - g_re * s_t
        spec_re.append(halves(h_re))
        spec_im.append(halves(h_im))

    span = pair * devices
    prod_re, prod_im = [], []
    for m in range(n_grp):
        sig_r, cot_r, tap_r = [spec_re[m][z * span : (z + 1) * span] for z in range(n_arr)]
        sig_i, cot_i, tap_i = [spec_im[m][z * span : (z + 1) * span] for z in range(n_arr)]
        prod_re.append(jnp.concatenate(
            [sig_r * tap_r - sig_i * tap_i, cot_r * tap_r + cot_i * tap_i, cot_r * sig_r + cot_i * sig_i]
        ))
        prod_im.append(jnp.concatenate(
            [sig_r * tap_i + sig_i * tap_r, cot_i * tap_r - cot_r * tap_i, cot_i * sig_r - cot_r * sig_i]
        ))

    inv_mat = jnp.concatenate(
        [
            jnp.concatenate([q_cos, -q_sin], axis=1),
            jnp.concatenate([q_sin, q_cos], axis=1),
        ],
        axis=0,
    )
    b_rows = dev_ids[:, None] * block_w + lane_blk[None, :]
    k1_own = rank_seq * pair + jnp.arange(pair, dtype=jnp.int32)
    ex_ang = (b_rows[:, None, :] * k1_own[None, :, None]) % fft_size
    ex_ang = ex_ang.astype(jnp.float32) * (2.0 * math.pi / fft_size)
    ex_cos = jnp.cos(ex_ang)[:, :, None, :]
    ex_sin = jnp.sin(ex_ang)[:, :, None, :]
    out_mat = jnp.concatenate([col_cos.T, -col_sin.T], axis=1)

    def inverse_part(z_list):
        n_out = len(z_list)
        blocks_out = [(zi, k1l) for zi in range(n_out) for k1l in range(pair)]
        hh_re, hh_im = [], []
        for m in range(n_grp):
            pr = jnp.concatenate([prod_re[m][z * span : (z + 1) * span] for z in z_list])
            pi = jnp.concatenate([prod_im[m][z * span : (z + 1) * span] for z in z_list])
            g_re = halves(pr)
            g_im = halves(pi)
            c_t, s_t = half_tw(m)
            hh_re.append(g_re * c_t - g_im * s_t)
            hh_im.append(g_im * c_t + g_re * s_t)
        v_cols_re, v_cols_im = {}, {}
        for p in range(n_grp):
            cs = [w8(p, m) for m in range(n_grp)]
            u_re = lin([c for c, _ in cs] + [-s for _, s in cs], hh_re + hh_im)
            u_im = lin([c for c, _ in cs] + [s for _, s in cs], hh_im + hh_re)
            c_t, s_t = mid_tab(p, len(blocks_out))
            v_re = u_re * c_t - u_im * s_t
            v_im = u_im * c_t + u_re * s_t
            for idx, (zi, k1l) in enumerate(blocks_out):
                v_cols_re[(k1l, zi, p)] = v_re[idx * devices : (idx + 1) * devices]
                v_cols_im[(k1l, zi, p)] = v_im[idx * devices : (idx + 1) * devices]
        order = [(k1l, zi, p) for k1l in range(pair) for zi in range(n_out) for p in range(n_grp)]
        v_all = jnp.concatenate(
            [
                jnp.concatenate([v_cols_re[key] for key in order], axis=1),
                jnp.concatenate([v_cols_im[key] for key in order], axis=1),
            ],
            axis=0,
        )
        w_all = fft_dot(inv_mat, v_all).reshape(2, devices, pair, n_out, width)
        x_re = w_all[0] * ex_cos - w_all[1] * ex_sin
        x_im = w_all[0] * ex_sin + w_all[1] * ex_cos
        back = jnp.stack([x_re, x_im], axis=1)
        back = lax.all_to_all(
            back.astype(jnp.bfloat16), "seq", split_axis=0, concat_axis=0, tiled=True
        ).astype(jnp.float32)
        back = back.reshape(devices, 2, pair, n_out * width)
        back = jnp.transpose(back, (1, 0, 2, 3)).reshape(2 * rows_all, n_out * width)
        return (fft_dot(out_mat, back) * inv_scale).reshape(devices, n_out, width)

    res_taps = inverse_part([2])
    res_rows = inverse_part([0, 1])

    d_taps = res_taps[:, 0].reshape(devices * block_w, channels)
    d_raw = d_taps * envelope
    d_preact = mat_dot(d_raw, w_out.T) * jnp.cos(preact)
    out_part = mat_dot(hidden.T, d_raw)
    embed_part = mat_dot(features.T, d_preact)
    bias_part = jnp.sum(d_preact, axis=0)
    rank_chan = lax.axis_index("chan")
    n_chan = lax.axis_size("chan")
    flat = jnp.concatenate([out_part.reshape(-1), embed_part.reshape(-1), bias_part])
    piece = -(-flat.shape[0] // (devices * 128)) * 128
    flat = jnp.pad(flat, (0, devices * piece - flat.shape[0])).reshape(devices, piece)

    flat_hi = flat.astype(jnp.bfloat16)
    flat_lo = (flat - flat_hi.astype(jnp.float32)).astype(jnp.bfloat16)
    outgoing = jnp.concatenate(
        [res_rows.reshape(devices, 2 * width).astype(jnp.bfloat16), flat_hi, flat_lo], axis=1
    )
    incoming = lax.all_to_all(outgoing, "seq", split_axis=0, concat_axis=0, tiled=True)
    rows_out = incoming[:, : 2 * width].reshape(devices, 2, width)
    conv_out = rows_out[:, 0].reshape(1, seg_len // 2, 2 * channels)
    d_signal = rows_out[:, 1].reshape(1, seg_len // 2, 2 * channels)
    got_hi = incoming[:, 2 * width : 2 * width + piece].astype(jnp.float32)
    got_lo = incoming[:, 2 * width + piece :].astype(jnp.float32)
    mine = jnp.sum(got_hi + got_lo, axis=0)

    n_all = devices * n_chan
    total = lax.all_to_all(
        jnp.broadcast_to(mine, (n_all, piece)), ("seq", "chan"), 0, 0, tiled=True
    )
    total = total.reshape(devices, n_chan, piece)
    own = lax.dynamic_index_in_dim(total, rank_chan, axis=1, keepdims=False).reshape(-1)
    both = jnp.sum(total, axis=1).reshape(-1)
    n_out = out_part.size
    n_emb = embed_part.size
    out_sum = own[:n_out].reshape(out_part.shape)
    embed_all = both[n_out : n_out + n_emb].reshape(embed_part.shape)
    bias_all = both[n_out + n_emb : n_out + n_emb + bias_part.size]
    norm_scale = 1.0 / math.sqrt(seq_total)
    return (conv_out, d_signal, embed_all * norm_scale, bias_all * norm_scale, out_sum * norm_scale)


def solution(mesh):
    return jax.shard_map(
        local,
        mesh=mesh,
        in_specs=(
            P("chan", "seq", None),
            P("chan", "seq", None),
            P(),
            P(),
            P(),
            P(None, "chan"),
            P("chan"),
        ),
        out_specs=(P("chan", "seq", None), P("chan", "seq", None), P(), P(), P(None, "chan")),
        check_vma=False,
    )
```

```python
import math

import jax
import jax.numpy as jnp
from jax import lax
from jax.sharding import PartitionSpec as P

exact_mode = lax.Precision.HIGH


def mat_dot(lhs_mat, rhs_mat):
    return jnp.dot(lhs_mat, rhs_mat, preferred_element_type=jnp.float32, precision=exact_mode)


def fft_dot(lhs_mat, rhs_mat):
    return jnp.dot(
        lhs_mat, rhs_mat, preferred_element_type=jnp.float32, precision=lax.Precision.HIGH
    )


def band_phase(band_freq, places, seq_total):
    upper_part = places // 1024
    lower_part = places % 1024
    partial_turn = upper_part[:, None] * band_freq[None, :] % seq_total
    wrapped = (partial_turn * 1024 + lower_part[:, None] * band_freq[None, :]) % seq_total
    return wrapped.astype(jnp.float32) * (2.0 * math.pi / seq_total)


def filter_parts(places, band_freq, w_embed, b_embed, w_out, decay, seq_total):
    phases = band_phase(band_freq, places, seq_total)
    features = jnp.concatenate([jnp.cos(phases), jnp.sin(phases)], axis=1)
    preact = mat_dot(features, w_embed) + b_embed[None, :]
    hidden = jnp.sin(preact)
    fraction = places.astype(jnp.float32) / seq_total
    envelope = (
        jnp.exp(-decay[None, :] * fraction[:, None]) * jnp.sqrt((1.0 + decay) / seq_total)[None, :]
    )
    taps = mat_dot(hidden, w_out) * envelope
    return (features, preact, hidden, taps, envelope)


def angle_table(rows_idx, cols_idx, modulus):
    wrapped = rows_idx[:, None] * cols_idx[None, :] % modulus
    angles = wrapped.astype(jnp.float32) * (2.0 * math.pi / modulus)
    return (jnp.cos(angles), jnp.sin(angles))


def local(signal, cotangent, band_freq, w_embed, b_embed, w_out, decay):
    devices = lax.axis_size("seq")
    rank_seq = lax.axis_index("seq")
    seg_len = signal.shape[1] * 2
    channels = signal.shape[2] // 2
    block_w = seg_len // devices
    width = block_w * channels
    rows_all = 2 * devices
    pair = rows_all // devices
    seq_total = seg_len * devices
    fft_size = 2 * seq_total
    inv_scale = 1.0 / fft_size
    n_arr = 3

    dev_ids = jnp.arange(devices, dtype=jnp.int32)
    row_ids = jnp.arange(rows_all, dtype=jnp.int32)
    blk_ids = jnp.arange(block_w, dtype=jnp.int32)
    lane_blk = jnp.arange(width, dtype=jnp.int32) // channels
    b_lane = rank_seq * block_w + lane_blk

    src = jnp.concatenate(
        [signal.reshape(devices, width), cotangent.reshape(devices, width)], axis=1
    )
    cols = lax.all_to_all(src, "seq", split_axis=0, concat_axis=0, tiled=True)
    cols = cols.reshape(devices, 2, width)

    places = (
        dev_ids[:, None] * seg_len + rank_seq * block_w + blk_ids[None, :]
    ).reshape(-1)
    features, preact, hidden, taps, envelope = filter_parts(
        places, band_freq, w_embed, b_embed, w_out, decay, seq_total
    )
    stacked = jnp.concatenate(
        [cols.astype(jnp.float32), taps.reshape(devices, 1, width)], axis=1
    ).reshape(devices, n_arr * width)

    col_cos, col_sin = angle_table(row_ids, dev_ids, rows_all)
    y_re = fft_dot(col_cos, stacked).reshape(rows_all, n_arr, width)
    y_im = -fft_dot(col_sin, stacked).reshape(rows_all, n_arr, width)
    tw_cos, tw_sin = angle_table(row_ids, b_lane, fft_size)
    tw_cos = tw_cos[:, None, :]
    tw_sin = tw_sin[:, None, :]
    t_re = y_re * tw_cos + y_im * tw_sin
    t_im = y_im * tw_cos - y_re * tw_sin
    spec = jnp.stack([t_re, t_im], axis=1)
    spec = lax.all_to_all(
        spec.astype(jnp.bfloat16), "seq", split_axis=0, concat_axis=0, tiled=True
    ).astype(jnp.float32)

    q_cos, q_sin = angle_table(dev_ids, dev_ids, devices)
    stage_a = fft_dot(jnp.concatenate([q_cos, q_sin], axis=0), spec.reshape(devices, -1))
    lanes = 2 * channels
    n_grp = width // lanes
    blocks = [(z, k1l) for z in range(n_arr) for k1l in range(pair)]
    n_blk = len(blocks)
    lane_h = jnp.arange(lanes, dtype=jnp.int32) // channels
    flip = jnp.where(lane_h == 0, 1.0, -1.0).astype(jnp.float32)

    def col(k1l, ri, z, p):
        return ((k1l * 2 + ri) * n_arr + z) * width + p * lanes

    def rows_of(part, ri, p):
        return jnp.concatenate(
            [part[:, col(k1l, ri, z, p) : col(k1l, ri, z, p) + lanes] for z, k1l in blocks], axis=0
        )

    def mid_tab(p, count):
        c_t, s_t = angle_table(dev_ids, 2 * p + lane_h, seg_len)
        c_t = jnp.broadcast_to(c_t[None], (count, devices, lanes)).reshape(count * devices, lanes)
        s_t = jnp.broadcast_to(s_t[None], (count, devices, lanes)).reshape(count * devices, lanes)
        return c_t, s_t

    def lin(coefs, vals):
        acc = None
        for w, v in zip(coefs, vals):
            if abs(w) < 1e-12:
                continue
            term = v if w == 1.0 else (-v if w == -1.0 else v * w)
            acc = term if acc is None else acc + term
        return acc

    def w8(p, m):
        k = (p * m) % n_grp
        return (round(math.cos(2 * math.pi * k / n_grp), 15), round(math.sin(2 * math.pi * k / n_grp), 15))

    def half_tw(m):
        ang = 2 * math.pi * m / (2 * n_grp)
        c_t = jnp.where(lane_h == 1, math.cos(ang), 1.0).astype(jnp.float32)
        s_t = jnp.where(lane_h == 1, math.sin(ang), 0.0).astype(jnp.float32)
        return c_t, s_t

    def halves(x):
        return flip * x + jnp.roll(x, channels, axis=1)

    top = stage_a[:devices]
    bot = stage_a[devices:]
    x_re, x_im = [], []
    for p in range(n_grp):
        a_re = rows_of(top, 0, p) + rows_of(bot, 1, p)
        a_im = rows_of(top, 1, p) - rows_of(bot, 0, p)
        c_t, s_t = mid_tab(p, n_blk)
        x_re.append(a_re * c_t + a_im * s_t)
        x_im.append(a_im * c_t - a_re * s_t)
    spec_re, spec_im = [], []
    for m in range(n_grp):
        cs = [w8(p, m) for p in range(n_grp)]
        g_re = lin([c for c, _ in cs] + [s for _, s in cs], x_re + x_im)
        g_im = lin([c for c, _ in cs] + [-s for _, s in cs], x_im + x_re)
        c_t, s_t = half_tw(m)
        h_re = g_re * c_t + g_im * s_t
        h_im = g_im * c_t - g_re * s_t
        spec_re.append(halves(h_re))
        spec_im.append(halves(h_im))

    span = pair * devices
    prod_re, prod_im = [], []
    for m in range(n_grp):
        sig_r, cot_r, tap_r = [spec_re[m][z * span : (z + 1) * span] for z in range(n_arr)]
        sig_i, cot_i, tap_i = [spec_im[m][z * span : (z + 1) * span] for z in range(n_arr)]
        prod_re.append(jnp.concatenate(
            [sig_r * tap_r - sig_i * tap_i, cot_r * tap_r + cot_i * tap_i, cot_r * sig_r + cot_i * sig_i]
        ))
        prod_im.append(jnp.concatenate(
            [sig_r * tap_i + sig_i * tap_r, cot_i * tap_r - cot_r * tap_i, cot_i * sig_r - cot_r * sig_i]
        ))

    inv_mat = jnp.concatenate(
        [
            jnp.concatenate([q_cos, -q_sin], axis=1),
            jnp.concatenate([q_sin, q_cos], axis=1),
        ],
        axis=0,
    )
    b_rows = dev_ids[:, None] * block_w + lane_blk[None, :]
    k1_own = rank_seq * pair + jnp.arange(pair, dtype=jnp.int32)
    ex_ang = (b_rows[:, None, :] * k1_own[None, :, None]) % fft_size
    ex_ang = ex_ang.astype(jnp.float32) * (2.0 * math.pi / fft_size)
    ex_cos = jnp.cos(ex_ang)[:, :, None, :]
    ex_sin = jnp.sin(ex_ang)[:, :, None, :]
    out_mat = jnp.concatenate([col_cos.T, -col_sin.T], axis=1)

    def inverse_part(z_list):
        n_out = len(z_list)
        blocks_out = [(zi, k1l) for zi in range(n_out) for k1l in range(pair)]
        hh_re, hh_im = [], []
        for m in range(n_grp):
            pr = jnp.concatenate([prod_re[m][z * span : (z + 1) * span] for z in z_list])
            pi = jnp.concatenate([prod_im[m][z * span : (z + 1) * span] for z in z_list])
            g_re = halves(pr)
            g_im = halves(pi)
            c_t, s_t = half_tw(m)
            hh_re.append(g_re * c_t - g_im * s_t)
            hh_im.append(g_im * c_t + g_re * s_t)
        v_cols_re, v_cols_im = {}, {}
        for p in range(n_grp):
            cs = [w8(p, m) for m in range(n_grp)]
            u_re = lin([c for c, _ in cs] + [-s for _, s in cs], hh_re + hh_im)
            u_im = lin([c for c, _ in cs] + [s for _, s in cs], hh_im + hh_re)
            c_t, s_t = mid_tab(p, len(blocks_out))
            v_re = u_re * c_t - u_im * s_t
            v_im = u_im * c_t + u_re * s_t
            for idx, (zi, k1l) in enumerate(blocks_out):
                v_cols_re[(k1l, zi, p)] = v_re[idx * devices : (idx + 1) * devices]
                v_cols_im[(k1l, zi, p)] = v_im[idx * devices : (idx + 1) * devices]
        order = [(k1l, zi, p) for k1l in range(pair) for zi in range(n_out) for p in range(n_grp)]
        v_all = jnp.concatenate(
            [
                jnp.concatenate([v_cols_re[key] for key in order], axis=1),
                jnp.concatenate([v_cols_im[key] for key in order], axis=1),
            ],
            axis=0,
        )
        w_all = fft_dot(inv_mat, v_all).reshape(2, devices, pair, n_out, width)
        x_re = w_all[0] * ex_cos - w_all[1] * ex_sin
        x_im = w_all[0] * ex_sin + w_all[1] * ex_cos
        back = jnp.stack([x_re, x_im], axis=1)
        back = lax.all_to_all(
            back.astype(jnp.bfloat16), "seq", split_axis=0, concat_axis=0, tiled=True
        ).astype(jnp.float32)
        back = back.reshape(devices, 2, pair, n_out * width)
        back = jnp.transpose(back, (1, 0, 2, 3)).reshape(2 * rows_all, n_out * width)
        return (fft_dot(out_mat, back) * inv_scale).reshape(devices, n_out, width)

    res_taps = inverse_part([2])
    res_rows = inverse_part([0, 1])

    d_taps = res_taps[:, 0].reshape(devices * block_w, channels)
    d_raw = d_taps * envelope
    d_preact = mat_dot(d_raw, w_out.T) * jnp.cos(preact)
    out_part = mat_dot(hidden.T, d_raw)
    embed_part = mat_dot(features.T, d_preact)
    bias_part = jnp.sum(d_preact, axis=0)
    rank_chan = lax.axis_index("chan")
    n_chan = lax.axis_size("chan")
    flat = jnp.concatenate([out_part.reshape(-1), embed_part.reshape(-1), bias_part])
    piece = -(-flat.shape[0] // (devices * 128)) * 128
    flat = jnp.pad(flat, (0, devices * piece - flat.shape[0])).reshape(devices, piece)

    flat_hi = flat.astype(jnp.bfloat16)
    flat_lo = (flat - flat_hi.astype(jnp.float32)).astype(jnp.bfloat16)
    outgoing = jnp.concatenate(
        [res_rows.reshape(devices, 2 * width).astype(jnp.bfloat16), flat_hi, flat_lo], axis=1
    )
    incoming = lax.all_to_all(outgoing, "seq", split_axis=0, concat_axis=0, tiled=True)
    rows_out = incoming[:, : 2 * width].reshape(devices, 2, width)
    conv_out = rows_out[:, 0].reshape(1, seg_len // 2, 2 * channels)
    d_signal = rows_out[:, 1].reshape(1, seg_len // 2, 2 * channels)
    got_hi = incoming[:, 2 * width : 2 * width + piece].astype(jnp.float32)
    got_lo = incoming[:, 2 * width + piece :].astype(jnp.float32)
    mine = jnp.sum(got_hi + got_lo, axis=0)

    n_all = devices * n_chan
    total = lax.all_to_all(
        jnp.broadcast_to(mine, (n_all, piece)), ("seq", "chan"), 0, 0, tiled=True
    )
    total = total.reshape(devices, n_chan, piece)
    own = lax.dynamic_index_in_dim(total, rank_chan, axis=1, keepdims=False).reshape(-1)
    both = jnp.sum(total, axis=1).reshape(-1)
    n_out = out_part.size
    n_emb = embed_part.size
    out_sum = own[:n_out].reshape(out_part.shape)
    embed_all = both[n_out : n_out + n_emb].reshape(embed_part.shape)
    bias_all = both[n_out + n_emb : n_out + n_emb + bias_part.size]
    norm_scale = 1.0 / math.sqrt(seq_total)
    return (conv_out, d_signal, embed_all * norm_scale, bias_all * norm_scale, out_sum * norm_scale)


def solution(mesh):
    return jax.shard_map(
        local,
        mesh=mesh,
        in_specs=(
            P("chan", "seq", None),
            P("chan", "seq", None),
            P(),
            P(),
            P(),
            P(None, "chan"),
            P("chan"),
        ),
        out_specs=(P("chan", "seq", None), P("chan", "seq", None), P(), P(), P(None, "chan")),
        check_vma=False,
    )
```
